32 devices in a mesh: row: 8 (over z, x), col: 4 (over y, core).
Axes of the slice: x: 2, y: 2, z: 4, core: 2. Of those that a mesh axis runs over, the one named last changes fastest.
Arguments:
- displacement: bfloat16 [3, 8, 512, 1024], P(None, 'row', 'col'), may hold values from -8 to 8
- magnetic: bfloat16 [3, 8, 512, 1024], P(None, 'row', 'col'), may hold values from -6 to 6
- region: int32 [8, 512, 1024], P('row', 'col'), may hold values from 0 to 7
- permittivity: float32 [8], replicated, may hold values from 1 to 12
Outputs:
- magnetic_new: bfloat16 [3, 8, 512, 1024], P(None, 'row', 'col')
The draws below stay inside these ranges and needn't reach their ends.
All inputs are finite; a program needn't handle non-finite values.
Results may differ from the reference program's by a relative error of at most 0.0065.
Values may be sent and summed in bfloat16 or wider, within the bound.
No kernel may reach another device: no remote copies, remote signals or barrier semaphores. Data moves between devices by JAX's collectives and lax.ppermute only.
A program may use at most 64 MiB of HBM per device.

```python
import math
import jax
import jax.numpy as jnp
from jax import lax

NY = 512
NZ = 1024
REGIONS = 8
NX = 8


def touch_ends(values, rng, smallest, high):
    extent = values.shape
    place = [jax.random.randint(jax.random.fold_in(rng, axis), (), 0, extent[axis]) for axis in range(len(extent))]
    values = values.at[tuple(place)].set(smallest)
    longest = extent.index(max(extent))
    place[longest] = (place[longest] + 1) % extent[longest]
    return values.at[tuple(place)].set(high)


def shard_levels(own_key, dims, cuts, smallest, high):
    factor_of, own = 1.0, jax.random.fold_in(own_key, 6)
    for axis_at, shards_of in cuts:
        draws = jnp.exp(jax.random.uniform(jax.random.fold_in(own, axis_at), (shards_of,), jnp.float32, smallest / len(cuts), high / len(cuts)))
        factor_of = factor_of * jnp.repeat(draws, dims[axis_at] // shards_of).reshape([-1 if axis == axis_at else 1 for axis in range(len(dims))])
    return factor_of


def scatter_about(rng, shape, deviation, limit, split=(), kind=jnp.bfloat16):
    level = shard_levels(rng, shape, split, -0.22, 0.18) if split else 1.0
    array = jax.random.normal(rng, shape, jnp.float32) * deviation * level
    return jnp.minimum(jnp.maximum(array, -limit), limit).astype(kind)


def setup_inputs(seed: int = 0) -> dict:
    key_of = jax.random.split(jax.random.key(seed), 5)
    displacement = scatter_about(key_of[0], (3, NX, NY, NZ), 2.0, 8.0, ((1, 8), (2, 4)))
    magnetic = scatter_about(key_of[1], (3, NX, NY, NZ), 1.0, 6.0, ((1, 8), (2, 4)))
    region = touch_ends(jax.random.randint(key_of[2], (NX, NY, NZ), 0, REGIONS), jax.random.fold_in(key_of[2], 1), 0, REGIONS - 1).astype(jnp.int32)
    permittivity = jnp.clip(jnp.exp(jax.random.uniform(key_of[3], (REGIONS,), jnp.float32, math.log(1.0), math.log(12.0))), 1.0, 12.0)
    return {"displacement": displacement, "magnetic": magnetic, "region": region, "permittivity": permittivity}


TIME_STEP = 0.5


def wavenumber(wave_index, length):
    signed = jnp.where(2 * wave_index < length, wave_index, wave_index - length)
    return jnp.where(2 * wave_index == length, 0.0, signed.astype(jnp.float32) * (2.0 * math.pi / length))


def storage_wave(position, length):
    column_count = length // 8
    return position // column_count + 8 * (position % column_count)


def to_storage(values, axis_number):
    moved = jnp.moveaxis(values, axis_number, -1)
    length = moved.shape[-1]
    leading = moved.shape[:-1]
    moved = jnp.swapaxes(moved.reshape(leading + (length // 8, 8)), -1, -2).reshape(leading + (length,))
    return jnp.moveaxis(moved, -1, axis_number)


def from_storage(values, axis_number):
    moved = jnp.moveaxis(values, axis_number, -1)
    length = moved.shape[-1]
    leading = moved.shape[:-1]
    moved = jnp.swapaxes(moved.reshape(leading + (8, length // 8)), -1, -2).reshape(leading + (length,))
    return jnp.moveaxis(moved, -1, axis_number)


def passed_part(values):
    return lax.optimization_barrier(values.astype(jnp.bfloat16)).astype(jnp.float32)


def passed_complex(values):
    return lax.complex(passed_part(jnp.real(values)), passed_part(jnp.imag(values)))


def reference(displacement, magnetic, region, permittivity):
    reciprocal = 1.0 / permittivity
    cell_scale = jnp.zeros(region.shape, jnp.float32)
    for region_id in range(REGIONS):
        cell_scale = jnp.where(region == region_id, reciprocal[region_id], cell_scale)
    wave_x = wavenumber(jnp.arange(NX, dtype=jnp.int32), NX)[:, None, None]
    wave_y = wavenumber(storage_wave(jnp.arange(NY, dtype=jnp.int32), NY), NY)[None, :, None]
    wave_z = wavenumber(storage_wave(jnp.arange(NZ, dtype=jnp.int32), NZ), NZ)[None, None, :]
    spectra = []
    for component in range(3):
        electric = displacement[component].astype(jnp.float32) * cell_scale
        z_spectrum = passed_complex(to_storage(jnp.fft.fft(electric, axis=2), 2))
        y_spectrum = passed_complex(to_storage(jnp.fft.fft(z_spectrum, axis=1), 1))
        spectra.append(jnp.fft.fft(y_spectrum, axis=0))
    field_x, field_y, field_z = spectra
    curls = [wave_y * field_z - wave_z * field_y,
             wave_z * field_x - wave_x * field_z,
             wave_x * field_y - wave_y * field_x]
    outputs = []
    for component in range(3):
        curl_part = curls[component]
        update = lax.complex(TIME_STEP * jnp.imag(curl_part), -TIME_STEP * jnp.real(curl_part))
        back_x = passed_complex(jnp.fft.ifft(update, axis=0))
        back_y = passed_complex(jnp.fft.ifft(from_storage(back_x, 1), axis=1))
        curl_field = jnp.real(jnp.fft.ifft(from_storage(back_y, 2), axis=2))
        outputs.append((magnetic[component].astype(jnp.float32) + curl_field).astype(jnp.bfloat16))
    return jnp.stack(outputs)
```

```python
import math

import numpy as np
import jax
import jax.numpy as jnp
from jax import lax
from jax.sharding import PartitionSpec as P

TIME_STEP = 0.5
F32 = jnp.float32
BF16 = jnp.bfloat16


def wavenumber(wave_index, length):
    signed = jnp.where(2 * wave_index < length, wave_index, wave_index - length)
    return jnp.where(
        2 * wave_index == length, 0.0, signed.astype(F32) * (2.0 * math.pi / length)
    )


def rounded(values):
    return lax.reduce_precision(values, exponent_bits=8, mantissa_bits=7)


def split_parts(values):
    high = rounded(values)
    low = values - high
    return high.astype(BF16), low.astype(BF16)


def phase_table(rows, cols, length):
    product = lax.iota(jnp.int32, rows)[:, None] * lax.iota(jnp.int32, cols)[None, :]
    angle = (product % length).astype(F32) * (2.0 * math.pi / length)
    return jnp.cos(angle), jnp.sin(angle)


def x_kernel(span_x):
    index = np.arange(span_x)
    signed = np.where(2 * index < span_x, index, index - span_x)
    qx = np.where(2 * index == span_x, 0.0, signed * (2.0 * math.pi / span_x))
    shift = np.arange(span_x)
    phases = np.exp(2j * math.pi * np.outer(shift, index) / span_x)
    taps = (phases * (-0.5j * qx)[None, :]).sum(axis=1) / span_x
    taps = taps.real
    matrix = taps[(shift[:, None] - shift[None, :]) % span_x]
    return matrix.astype(np.float32)


def mat(table_parts, operand, spec):
    total = None
    for part in table_parts:
        term = jnp.einsum(spec, part, operand, preferred_element_type=F32)
        total = term if total is None else total + term
    return total


def curl_update(y_real, y_imag, wave_y, wave_z, kernel):
    half = TIME_STEP

    def along_x(values):
        return jnp.einsum("ab,bkj->akj", kernel, values, precision=lax.Precision.HIGHEST)

    xr, yr, zr = y_real[0], y_real[1], y_real[2]
    xi, yi, zi = y_imag[0], y_imag[1], y_imag[2]
    qy = half * wave_y
    qz = half * wave_z
    gyr, gyi = along_x(yr), along_x(yi)
    gzr, gzi = along_x(zr), along_x(zi)
    b_real = jnp.stack([qy * zi - qz * yi, qz * xi - gzr, gyr - qy * xi])
    b_imag = jnp.stack([qz * yr - qy * zr, -qz * xr - gzi, gyi + qy * xr])
    return b_real, b_imag


def on_device(displacement, magnetic, region, permittivity):
    row_count = lax.axis_size("row")
    col_count = lax.axis_size("col")
    devices = row_count * col_count
    members, local_x, local_y, depth = displacement.shape
    width_y = local_y * col_count
    span_x = local_x * row_count
    hermitian = (depth // 2) % devices == 0
    columns = depth // 2 if hermitian else depth
    per_device = columns // devices
    me = lax.axis_index("row") * col_count + lax.axis_index("col")

    reciprocal = 1.0 / permittivity
    cell_scale = jnp.zeros(region.shape, F32)
    for region_id in range(permittivity.shape[0]):
        cell_scale = jnp.where(region == region_id, reciprocal[region_id], cell_scale)
    electric = displacement.astype(F32) * cell_scale[None]

    cos_z, sin_z = phase_table(depth, columns, depth)
    if hermitian:
        parity = (1 - 2 * (lax.iota(jnp.int32, depth) % 2)).astype(F32)
        sin_part = jnp.concatenate([parity[:, None], -sin_z[:, 1:]], axis=1)
    else:
        sin_part = -sin_z
    table_z = jnp.concatenate([cos_z, sin_part], axis=1)
    z_high, z_low = split_parts(table_z)

    e_high, e_low = split_parts(electric)
    spectrum = (
        jnp.einsum("clyz,zk->clyk", e_high, z_high, preferred_element_type=F32)
        + jnp.einsum("clyz,zk->clyk", e_low, z_high, preferred_element_type=F32)
        + jnp.einsum("clyz,zk->clyk", e_high, z_low, preferred_element_type=F32)
    )
    spectrum = spectrum.astype(BF16).reshape(
        members, local_x, local_y, 2, devices, per_device
    )
    gathered = lax.all_to_all(
        spectrum, ("row", "col"), split_axis=4, concat_axis=2, tiled=True
    )
    gathered = gathered.reshape(members, local_x, row_count, width_y, 2, per_device)
    gathered = jnp.swapaxes(gathered, 1, 2).reshape(
        members, span_x, width_y, 2, per_device
    )

    cos_y, sin_y = phase_table(width_y, width_y, width_y)
    cos_y_parts = split_parts(cos_y)
    sin_y_parts = split_parts(sin_y)
    spec_fwd = "ky,cxypj->cxkpj"
    by_cos = mat(cos_y_parts, gathered, spec_fwd)
    by_sin = mat(sin_y_parts, gathered, spec_fwd)
    y_real = by_cos[:, :, :, 0] + by_sin[:, :, :, 1]
    y_imag = by_cos[:, :, :, 1] - by_sin[:, :, :, 0]

    kernel = jnp.asarray(x_kernel(span_x))
    wave_y = wavenumber(lax.iota(jnp.int32, width_y), width_y)[:, None]
    wave_z = wavenumber(me * per_device + lax.iota(jnp.int32, per_device), depth)

    def inverse_y(b_real, b_imag):
        stacked = jnp.stack([b_real, b_imag], axis=3).astype(BF16)
        spec_inv = "yk,cxkpj->cxypj"
        by_cos = mat(cos_y_parts, stacked, spec_inv)
        by_sin = mat(sin_y_parts, stacked, spec_inv)
        scale = 1.0 / width_y
        out_real = (by_cos[:, :, :, 0] - by_sin[:, :, :, 1]) * scale
        out_imag = (by_cos[:, :, :, 1] + by_sin[:, :, :, 0]) * scale
        return rounded(out_real), rounded(out_imag)

    b_real, b_imag = curl_update(rounded(y_real), rounded(y_imag), wave_y, wave_z, kernel)
    back_real, back_imag = inverse_y(rounded(b_real), rounded(b_imag))

    if hermitian:
        first_real = y_real[..., 0]
        first_imag = y_imag[..., 0]

        def mirrored(values):
            return jnp.roll(jnp.flip(values, axis=2), 1, axis=2)

        mirror_real = mirrored(first_real)
        mirror_imag = mirrored(first_imag)
        plane_real = jnp.stack(
            [0.5 * (first_real + mirror_real), 0.5 * (first_imag + mirror_imag)], axis=-1
        )
        plane_imag = jnp.stack(
            [0.5 * (first_imag - mirror_imag), -0.5 * (first_real - mirror_real)], axis=-1
        )
        pb_real, pb_imag = curl_update(
            rounded(plane_real), rounded(plane_imag), wave_y, jnp.zeros((2,), F32), kernel
        )
        pback_real, _ = inverse_y(rounded(pb_real), rounded(pb_imag))
        is_first = me == 0
        fixed_real = jnp.where(is_first, pback_real[..., 0], back_real[..., 0])
        fixed_imag = jnp.where(is_first, pback_real[..., 1], back_imag[..., 0])
        back_real = jnp.concatenate([fixed_real[..., None], back_real[..., 1:]], axis=-1)
        back_imag = jnp.concatenate([fixed_imag[..., None], back_imag[..., 1:]], axis=-1)

    outgoing = jnp.stack([back_real, back_imag], axis=3).astype(BF16)
    outgoing = outgoing.reshape(members, row_count, local_x, width_y, 2, per_device)
    outgoing = jnp.swapaxes(outgoing, 1, 2).reshape(
        members, local_x, devices, local_y, 2, per_device
    )
    returned = lax.all_to_all(
        outgoing, ("row", "col"), split_axis=2, concat_axis=5, tiled=True
    )
    returned = returned.reshape(members, local_x, local_y, 2 * columns)

    weight = np.full((2 * columns,), 1.0 / depth, np.float32)
    if hermitian:
        weight[:] = 2.0 / depth
        weight[0] = 1.0 / depth
        weight[columns] = 1.0 / depth
    weighted = (returned.astype(F32) * jnp.asarray(weight)).astype(BF16)
    field = jnp.einsum(
        "clyk,zk->clyz", weighted, z_high, preferred_element_type=F32
    ) + jnp.einsum("clyk,zk->clyz", weighted, z_low, preferred_element_type=F32)
    return (magnetic.astype(F32) + field).astype(BF16)


def solution(mesh):
    in_specs = (
        P(None, "row", "col", None),
        P(None, "row", "col", None),
        P("row", "col", None),
        P(),
    )
    out_specs = P(None, "row", "col", None)
    return jax.shard_map(
        on_device, mesh=mesh, in_specs=in_specs, out_specs=out_specs, check_vma=False
    )
```

```python
import math

import numpy as np
import jax
import jax.numpy as jnp
from jax import lax
from jax.sharding import PartitionSpec as P

TIME_STEP = 0.5
F32 = jnp.float32
BF16 = jnp.bfloat16


def wavenumber(wave_index, length):
    signed = jnp.where(2 * wave_index < length, wave_index, wave_index - length)
    return jnp.where(
        2 * wave_index == length, 0.0, signed.astype(F32) * (2.0 * math.pi / length)
    )


def rounded(values):
    return lax.reduce_precision(values, exponent_bits=8, mantissa_bits=7)


def split_parts(values):
    high = rounded(values)
    low = values - high
    return high.astype(BF16), low.astype(BF16)


def direct_phase(rows, cols, length, step):
    product = (lax.iota(jnp.int32, rows)[:, None] * step) * lax.iota(jnp.int32, cols)[None, :]
    angle = (product % length).astype(F32) * (2.0 * math.pi / length)
    return jnp.cos(angle), jnp.sin(angle)


def phase_table(rows, cols, length):
    block = 32
    if rows % block or rows <= block:
        return direct_phase(rows, cols, length, 1)
    outer_cos, outer_sin = direct_phase(rows // block, cols, length, block)
    inner_cos, inner_sin = direct_phase(block, cols, length, 1)
    outer_cos, outer_sin = outer_cos[:, None], outer_sin[:, None]
    inner_cos, inner_sin = inner_cos[None], inner_sin[None]
    cosine = outer_cos * inner_cos - outer_sin * inner_sin
    sine = outer_sin * inner_cos + outer_cos * inner_sin
    return cosine.reshape(rows, cols), sine.reshape(rows, cols)


def x_kernel(span_x):
    index = np.arange(span_x)
    signed = np.where(2 * index < span_x, index, index - span_x)
    qx = np.where(2 * index == span_x, 0.0, signed * (2.0 * math.pi / span_x))
    shift = np.arange(span_x)
    phases = np.exp(2j * math.pi * np.outer(shift, index) / span_x)
    taps = (phases * (-0.5j * qx)[None, :]).sum(axis=1) / span_x
    taps = taps.real
    matrix = taps[(shift[:, None] - shift[None, :]) % span_x]
    return matrix.astype(np.float32)


def mat(table_parts, operand, spec):
    total = None
    for part in table_parts:
        term = jnp.einsum(spec, part, operand, preferred_element_type=F32)
        total = term if total is None else total + term
    return total


def curl_update(y_real, y_imag, wave_y, wave_z, kernel):
    half = TIME_STEP

    def along_x(values):
        return jnp.einsum("ab,jbk->jak", kernel, values, precision=lax.Precision.HIGHEST)

    xr, yr, zr = y_real[0], y_real[1], y_real[2]
    xi, yi, zi = y_imag[0], y_imag[1], y_imag[2]
    qy = half * wave_y
    qz = half * wave_z[:, None, None]
    gyr, gyi = along_x(yr), along_x(yi)
    gzr, gzi = along_x(zr), along_x(zi)
    b_real = jnp.stack([qy * zi - qz * yi, qz * xi - gzr, gyr - qy * xi])
    b_imag = jnp.stack([qz * yr - qy * zr, -qz * xr - gzi, gyi + qy * xr])
    return b_real, b_imag


def on_device(displacement, magnetic, region, permittivity):
    row_count = lax.axis_size("row")
    col_count = lax.axis_size("col")
    devices = row_count * col_count
    members, local_x, local_y, depth = displacement.shape
    width_y = local_y * col_count
    span_x = local_x * row_count
    hermitian = (depth // 2) % devices == 0
    columns = depth // 2 if hermitian else depth
    per_device = columns // devices
    me = lax.axis_index("row") * col_count + lax.axis_index("col")

    reciprocal = 1.0 / permittivity
    cell_scale = jnp.zeros(region.shape, F32)
    for region_id in range(permittivity.shape[0]):
        cell_scale = jnp.where(region == region_id, reciprocal[region_id], cell_scale)
    electric = displacement.astype(F32) * cell_scale[None]

    cos_z, sin_z = phase_table(depth, columns, depth)
    if hermitian:
        parity = (1 - 2 * (lax.iota(jnp.int32, depth) % 2)).astype(F32)
        sin_part = jnp.concatenate([parity[:, None], -sin_z[:, 1:]], axis=1)
    else:
        sin_part = -sin_z
    table_z = jnp.concatenate([cos_z, sin_part], axis=1)
    z_high, z_low = split_parts(table_z)

    e_high, e_low = split_parts(electric)
    spec_z = "zk,clyz->clky"
    spectrum = (
        jnp.einsum(spec_z, z_high, e_high, preferred_element_type=F32)
        + jnp.einsum(spec_z, z_high, e_low, preferred_element_type=F32)
        + jnp.einsum(spec_z, z_low, e_high, preferred_element_type=F32)
    )
    spectrum = spectrum.astype(BF16).reshape(
        members, local_x, 2, devices, per_device, local_y
    )
    gathered = lax.all_to_all(
        spectrum, ("row", "col"), split_axis=3, concat_axis=5, tiled=True
    )
    gathered = gathered.reshape(members, local_x, 2, per_device, row_count, width_y)
    gathered = jnp.moveaxis(gathered, 1, 4).reshape(
        members, 2, per_device, span_x, width_y
    )

    cos_y, sin_y = phase_table(width_y, width_y, width_y)
    cos_y_parts = split_parts(cos_y)
    sin_y_parts = split_parts(sin_y)
    spec_y = "yk,cpjxy->cpjxk"
    by_cos = mat(cos_y_parts, gathered, spec_y)
    by_sin = mat(sin_y_parts, gathered, spec_y)
    y_real = by_cos[:, 0] + by_sin[:, 1]
    y_imag = by_cos[:, 1] - by_sin[:, 0]

    kernel = jnp.asarray(x_kernel(span_x))
    wave_y = wavenumber(lax.iota(jnp.int32, width_y), width_y)
    wave_z = wavenumber(me * per_device + lax.iota(jnp.int32, per_device), depth)

    def inverse_y(b_real, b_imag):
        stacked = jnp.stack([b_real, b_imag], axis=1).astype(BF16)
        by_cos = mat(cos_y_parts, stacked, spec_y)
        by_sin = mat(sin_y_parts, stacked, spec_y)
        scale = 1.0 / width_y
        out_real = (by_cos[:, 0] - by_sin[:, 1]) * scale
        out_imag = (by_cos[:, 1] + by_sin[:, 0]) * scale
        return rounded(out_real), rounded(out_imag)

    b_real, b_imag = curl_update(rounded(y_real), rounded(y_imag), wave_y, wave_z, kernel)
    back_real, back_imag = inverse_y(rounded(b_real), rounded(b_imag))

    if hermitian:
        first_real = y_real[:, 0]
        first_imag = y_imag[:, 0]

        def mirrored(values):
            return jnp.roll(jnp.flip(values, axis=-1), 1, axis=-1)

        mirror_real = mirrored(first_real)
        mirror_imag = mirrored(first_imag)
        plane_real = jnp.stack(
            [0.5 * (first_real + mirror_real), 0.5 * (first_imag + mirror_imag)], axis=1
        )
        plane_imag = jnp.stack(
            [0.5 * (first_imag - mirror_imag), -0.5 * (first_real - mirror_real)], axis=1
        )
        pb_real, pb_imag = curl_update(
            rounded(plane_real), rounded(plane_imag), wave_y, jnp.zeros((2,), F32), kernel
        )
        pback_real, _ = inverse_y(rounded(pb_real), rounded(pb_imag))
        is_first = me == 0
        fixed_real = jnp.where(is_first, pback_real[:, 0], back_real[:, 0])
        fixed_imag = jnp.where(is_first, pback_real[:, 1], back_imag[:, 0])
        back_real = jnp.concatenate([fixed_real[:, None], back_real[:, 1:]], axis=1)
        back_imag = jnp.concatenate([fixed_imag[:, None], back_imag[:, 1:]], axis=1)

    outgoing = jnp.stack([back_real, back_imag], axis=1).astype(BF16)
    outgoing = outgoing.reshape(
        members, 2, per_device, row_count, local_x, col_count, local_y
    )
    outgoing = jnp.moveaxis(outgoing, 4, 1).reshape(
        members, local_x, 2, per_device, devices, local_y
    )
    returned = lax.all_to_all(
        outgoing, ("row", "col"), split_axis=4, concat_axis=3, tiled=True
    )
    returned = returned.reshape(members, local_x, 2 * columns, local_y)

    weight = np.full((2 * columns,), 1.0 / depth, np.float32)
    if hermitian:
        weight[:] = 2.0 / depth
        weight[0] = 1.0 / depth
        weight[columns] = 1.0 / depth
    weight = jnp.asarray(weight)[:, None]
    weighted = (returned.astype(F32) * weight).astype(BF16)
    spec_back = "clky,zk->clyz"
    field = jnp.einsum(spec_back, weighted, z_high, preferred_element_type=F32) + jnp.einsum(
        spec_back, weighted, z_low, preferred_element_type=F32
    )
    return (magnetic.astype(F32) + field).astype(BF16)


def solution(mesh):
    in_specs = (
        P(None, "row", "col", None),
        P(None, "row", "col", None),
        P("row", "col", None),
        P(),
    )
    out_specs = P(None, "row", "col", None)
    return jax.shard_map(
        on_device, mesh=mesh, in_specs=in_specs, out_specs=out_specs, check_vma=False
    )
```

```python
import math

import numpy as np
import jax
import jax.numpy as jnp
from jax import lax
from jax.sharding import PartitionSpec as P

TIME_STEP = 0.5
F32 = jnp.float32
BF16 = jnp.bfloat16


def wavenumber(wave_index, length):
    signed = jnp.where(2 * wave_index < length, wave_index, wave_index - length)
    return jnp.where(
        2 * wave_index == length, 0.0, signed.astype(F32) * (2.0 * math.pi / length)
    )


def rounded(values):
    return lax.reduce_precision(values, exponent_bits=8, mantissa_bits=7)


def split_parts(values):
    high = rounded(values)
    low = values - high
    return high.astype(BF16), low.astype(BF16)


def direct_phase(rows, cols, length, step):
    product = (lax.iota(jnp.int32, rows)[:, None] * step) * lax.iota(jnp.int32, cols)[None, :]
    angle = (product % length).astype(F32) * (2.0 * math.pi / length)
    return jnp.cos(angle), jnp.sin(angle)


def phase_table(rows, cols, length):
    block = 32
    if rows % block or rows <= block:
        return direct_phase(rows, cols, length, 1)
    outer_cos, outer_sin = direct_phase(rows // block, cols, length, block)
    inner_cos, inner_sin = direct_phase(block, cols, length, 1)
    outer_cos, outer_sin = outer_cos[:, None], outer_sin[:, None]
    inner_cos, inner_sin = inner_cos[None], inner_sin[None]
    cosine = outer_cos * inner_cos - outer_sin * inner_sin
    sine = outer_sin * inner_cos + outer_cos * inner_sin
    return cosine.reshape(rows, cols), sine.reshape(rows, cols)


def x_kernel(span_x):
    index = np.arange(span_x)
    signed = np.where(2 * index < span_x, index, index - span_x)
    qx = np.where(2 * index == span_x, 0.0, signed * (2.0 * math.pi / span_x))
    shift = np.arange(span_x)
    phases = np.exp(2j * math.pi * np.outer(shift, index) / span_x)
    taps = (phases * (-0.5j * qx)[None, :]).sum(axis=1) / span_x
    taps = taps.real
    matrix = taps[(shift[:, None] - shift[None, :]) % span_x]
    return matrix.astype(np.float32)


def mat(table_parts, operand, spec):
    total = None
    for part in table_parts:
        term = jnp.einsum(spec, part, operand, preferred_element_type=F32)
        total = term if total is None else total + term
    return total


def curl_update(y_real, y_imag, wave_y, wave_z, kernel):
    half = TIME_STEP

    def along_x(values):
        return jnp.einsum("ab,jbk->jak", kernel, values, precision=lax.Precision.HIGHEST)

    xr, yr, zr = y_real[0], y_real[1], y_real[2]
    xi, yi, zi = y_imag[0], y_imag[1], y_imag[2]
    qy = half * wave_y
    qz = half * wave_z[:, None, None]
    gyr, gyi = along_x(yr), along_x(yi)
    gzr, gzi = along_x(zr), along_x(zi)
    b_real = jnp.stack([qy * zi - qz * yi, qz * xi - gzr, gyr - qy * xi])
    b_imag = jnp.stack([qz * yr - qy * zr, -qz * xr - gzi, gyi + qy * xr])
    return b_real, b_imag


def on_device(displacement, magnetic, region, permittivity):
    row_count = lax.axis_size("row")
    col_count = lax.axis_size("col")
    devices = row_count * col_count
    members, local_x, local_y, depth = displacement.shape
    width_y = local_y * col_count
    span_x = local_x * row_count
    hermitian = (depth // 2) % devices == 0
    columns = depth // 2 if hermitian else depth
    per_device = columns // devices
    me = lax.axis_index("row") * col_count + lax.axis_index("col")

    reciprocal = 1.0 / permittivity
    cell_scale = jnp.zeros(region.shape, F32)
    for region_id in range(permittivity.shape[0]):
        cell_scale = jnp.where(region == region_id, reciprocal[region_id], cell_scale)
    electric = displacement.astype(F32) * cell_scale[None]

    cos_z, sin_z = phase_table(depth, columns, depth)
    if hermitian:
        parity = (1 - 2 * (lax.iota(jnp.int32, depth) % 2)).astype(F32)
        sin_part = jnp.concatenate([parity[:, None], -sin_z[:, 1:]], axis=1)
    else:
        sin_part = -sin_z
    table_z = jnp.concatenate([cos_z, sin_part], axis=1)
    weight = np.full((2 * columns,), 2.0 / depth if hermitian else 1.0 / depth, np.float32)
    if hermitian:
        weight[0] = 1.0 / depth
        weight[columns] = 1.0 / depth
    chunks = 2 if per_device % 2 == 0 else 1
    chunk = per_device // chunks

    def chunk_columns(values, index):
        values = values.reshape(values.shape[:-1] + (2, devices, per_device))
        values = values[..., index * chunk : (index + 1) * chunk]
        return values.reshape(values.shape[:-3] + (2 * devices * chunk,))

    e_high, e_low = split_parts(electric)
    cos_y, sin_y = phase_table(width_y, width_y, width_y)
    cos_y_parts = split_parts(cos_y)
    sin_y_parts = split_parts(sin_y)
    spec_y = "yk,cpjxy->cpjxk"
    kernel = jnp.asarray(x_kernel(span_x))
    wave_y = wavenumber(lax.iota(jnp.int32, width_y), width_y)
    is_first = me == 0

    def inverse_y(b_real, b_imag):
        stacked = jnp.stack([b_real, b_imag], axis=1).astype(BF16)
        by_cos = mat(cos_y_parts, stacked, spec_y)
        by_sin = mat(sin_y_parts, stacked, spec_y)
        scale = 1.0 / width_y
        out_real = (by_cos[:, 0] - by_sin[:, 1]) * scale
        out_imag = (by_cos[:, 1] + by_sin[:, 0]) * scale
        return rounded(out_real), rounded(out_imag)

    def forward_z(index):
        z_high, z_low = split_parts(chunk_columns(table_z, index))
        spec_z = "zk,clyz->clky"
        spectrum = (
            jnp.einsum(spec_z, z_high, e_high, preferred_element_type=F32)
            + jnp.einsum(spec_z, z_high, e_low, preferred_element_type=F32)
            + jnp.einsum(spec_z, z_low, e_high, preferred_element_type=F32)
        )
        spectrum = spectrum.astype(BF16).reshape(
            members, local_x, 2, devices, chunk, local_y
        )
        return lax.all_to_all(
            spectrum, ("row", "col"), split_axis=3, concat_axis=5, tiled=True
        )

    def middle(gathered, index):
        gathered = gathered.reshape(members, local_x, 2, chunk, row_count, width_y)
        gathered = jnp.moveaxis(gathered, 1, 4).reshape(members, 2, chunk, span_x, width_y)
        by_cos = mat(cos_y_parts, gathered, spec_y)
        by_sin = mat(sin_y_parts, gathered, spec_y)
        y_real = by_cos[:, 0] + by_sin[:, 1]
        y_imag = by_cos[:, 1] - by_sin[:, 0]
        first_m = me * per_device + index * chunk
        wave_z = wavenumber(first_m + lax.iota(jnp.int32, chunk), depth)
        b_real, b_imag = curl_update(rounded(y_real), rounded(y_imag), wave_y, wave_z, kernel)
        back_real, back_imag = inverse_y(rounded(b_real), rounded(b_imag))

        if hermitian and index == 0:
            first_real = y_real[:, 0]
            first_imag = y_imag[:, 0]

            def mirrored(values):
                return jnp.roll(jnp.flip(values, axis=-1), 1, axis=-1)

            mirror_real = mirrored(first_real)
            mirror_imag = mirrored(first_imag)
            plane_real = jnp.stack(
                [0.5 * (first_real + mirror_real), 0.5 * (first_imag + mirror_imag)], axis=1
            )
            plane_imag = jnp.stack(
                [0.5 * (first_imag - mirror_imag), -0.5 * (first_real - mirror_real)], axis=1
            )
            pb_real, pb_imag = curl_update(
                rounded(plane_real), rounded(plane_imag), wave_y, jnp.zeros((2,), F32), kernel
            )
            pback_real, _ = inverse_y(rounded(pb_real), rounded(pb_imag))
            fixed_real = jnp.where(is_first, pback_real[:, 0], back_real[:, 0])
            fixed_imag = jnp.where(is_first, pback_real[:, 1], back_imag[:, 0])
            back_real = jnp.concatenate([fixed_real[:, None], back_real[:, 1:]], axis=1)
            back_imag = jnp.concatenate([fixed_imag[:, None], back_imag[:, 1:]], axis=1)

        outgoing = jnp.stack([back_real, back_imag], axis=1).astype(BF16)
        outgoing = outgoing.reshape(members, 2, chunk, row_count, local_x, col_count, local_y)
        outgoing = jnp.moveaxis(outgoing, 4, 1).reshape(
            members, local_x, 2, chunk, devices, local_y
        )
        return lax.all_to_all(
            outgoing, ("row", "col"), split_axis=4, concat_axis=3, tiled=True
        )

    def inverse_z(returned, index):
        returned = returned.reshape(members, local_x, 2 * devices * chunk, local_y)
        scale = chunk_columns(jnp.asarray(weight), index)[:, None]
        weighted = (returned.astype(F32) * scale).astype(BF16)
        z_high, z_low = split_parts(chunk_columns(table_z, index))
        spec_back = "clky,zk->clyz"
        return jnp.einsum(spec_back, weighted, z_high, preferred_element_type=F32) + jnp.einsum(
            spec_back, weighted, z_low, preferred_element_type=F32
        )

    field = None
    for index in range(chunks):
        part = inverse_z(middle(forward_z(index), index), index)
        field = part if field is None else field + part
    return (magnetic.astype(F32) + field).astype(BF16)


def solution(mesh):
    in_specs = (
        P(None, "row", "col", None),
        P(None, "row", "col", None),
        P("row", "col", None),
        P(),
    )
    out_specs = P(None, "row", "col", None)
    return jax.shard_map(
        on_device, mesh=mesh, in_specs=in_specs, out_specs=out_specs, check_vma=False
    )
```

```python
import math

import numpy as np
import jax
import jax.numpy as jnp
from jax import lax
from jax.sharding import PartitionSpec as P

TIME_STEP = 0.5
F32 = jnp.float32
BF16 = jnp.bfloat16


def wavenumber(wave_index, length):
    signed = jnp.where(2 * wave_index < length, wave_index, wave_index - length)
    return jnp.where(
        2 * wave_index == length, 0.0, signed.astype(F32) * (2.0 * math.pi / length)
    )


def rounded(values):
    return lax.reduce_precision(values, exponent_bits=8, mantissa_bits=7)


def split_parts(values):
    high = rounded(values)
    low = values - high
    return high.astype(BF16), low.astype(BF16)


def direct_phase(rows, cols, length, step):
    product = (lax.iota(jnp.int32, rows)[:, None] * step) * lax.iota(jnp.int32, cols)[None, :]
    angle = (product % length).astype(F32) * (2.0 * math.pi / length)
    return jnp.cos(angle), jnp.sin(angle)


def phase_table(rows, cols, length):
    block = 32
    if rows % block or rows <= block:
        return direct_phase(rows, cols, length, 1)
    outer_cos, outer_sin = direct_phase(rows // block, cols, length, block)
    inner_cos, inner_sin = direct_phase(block, cols, length, 1)
    outer_cos, outer_sin = outer_cos[:, None], outer_sin[:, None]
    inner_cos, inner_sin = inner_cos[None], inner_sin[None]
    cosine = outer_cos * inner_cos - outer_sin * inner_sin
    sine = outer_sin * inner_cos + outer_cos * inner_sin
    return cosine.reshape(rows, cols), sine.reshape(rows, cols)


def x_kernel(span_x):
    index = np.arange(span_x)
    signed = np.where(2 * index < span_x, index, index - span_x)
    qx = np.where(2 * index == span_x, 0.0, signed * (2.0 * math.pi / span_x))
    shift = np.arange(span_x)
    phases = np.exp(2j * math.pi * np.outer(shift, index) / span_x)
    taps = (phases * (-0.5j * qx)[None, :]).sum(axis=1) / span_x
    taps = taps.real
    matrix = taps[(shift[:, None] - shift[None, :]) % span_x]
    return matrix.astype(np.float32)


def mat(table_parts, operand, spec):
    total = None
    for part in table_parts:
        term = jnp.einsum(spec, part, operand, preferred_element_type=F32)
        total = term if total is None else total + term
    return total


def curl_update(y_real, y_imag, wave_y, wave_z, kernel):
    half = TIME_STEP

    def along_x(values):
        return jnp.einsum("ab,jbk->jak", kernel, values, precision=lax.Precision.HIGHEST)

    xr, yr, zr = y_real[0], y_real[1], y_real[2]
    xi, yi, zi = y_imag[0], y_imag[1], y_imag[2]
    qy = half * wave_y
    qz = half * wave_z[:, None, None]
    gyr, gyi = along_x(yr), along_x(yi)
    gzr, gzi = along_x(zr), along_x(zi)
    b_real = jnp.stack([qy * zi - qz * yi, qz * xi - gzr, gyr - qy * xi])
    b_imag = jnp.stack([qz * yr - qy * zr, -qz * xr - gzi, gyi + qy * xr])
    return b_real, b_imag


def on_device(displacement, magnetic, region, permittivity):
    row_count = lax.axis_size("row")
    col_count = lax.axis_size("col")
    devices = row_count * col_count
    members, local_x, local_y, depth = displacement.shape
    width_y = local_y * col_count
    span_x = local_x * row_count
    hermitian = (depth // 2) % devices == 0
    columns = depth // 2 if hermitian else depth
    per_device = columns // devices
    me = lax.axis_index("row") * col_count + lax.axis_index("col")

    reciprocal = 1.0 / permittivity
    regions = permittivity.shape[0]
    if regions == 8:
        level = [reciprocal[region_id] for region_id in range(regions)]
        for bit in (1, 2, 4):
            chosen = (region & bit) != 0
            level = [
                jnp.where(chosen, level[pair + 1], level[pair])
                for pair in range(0, len(level), 2)
            ]
        cell_scale = level[0]
    else:
        cell_scale = jnp.zeros(region.shape, F32)
        for region_id in range(regions):
            cell_scale = jnp.where(region == region_id, reciprocal[region_id], cell_scale)
    electric = displacement.astype(F32) * cell_scale[None]

    cos_z, sin_z = phase_table(depth, columns, depth)
    if hermitian:
        parity = (1 - 2 * (lax.iota(jnp.int32, depth) % 2)).astype(F32)
        sin_part = jnp.concatenate([parity[:, None], -sin_z[:, 1:]], axis=1)
    else:
        sin_part = -sin_z
    table_z = jnp.concatenate([cos_z, sin_part], axis=1)
    z_high, z_low = split_parts(table_z)

    e_high, e_low = split_parts(electric)
    spec_z = "zk,clyz->clky"
    spectrum = (
        jnp.einsum(spec_z, z_high, e_high, preferred_element_type=F32)
        + jnp.einsum(spec_z, z_high, e_low, preferred_element_type=F32)
        + jnp.einsum(spec_z, z_low, e_high, preferred_element_type=F32)
    )
    spectrum = spectrum.astype(BF16).reshape(
        members, local_x, 2, devices, per_device, local_y
    )
    gathered = lax.all_to_all(
        spectrum, ("row", "col"), split_axis=3, concat_axis=5, tiled=True
    )
    gathered = gathered.reshape(members, local_x, 2, per_device, row_count, width_y)
    gathered = jnp.moveaxis(gathered, 1, 4).reshape(
        members, 2, per_device, span_x, width_y
    )

    cos_y, sin_y = phase_table(width_y, width_y, width_y)
    cos_y_parts = split_parts(cos_y)
    sin_y_parts = split_parts(sin_y)
    spec_y = "yk,cpjxy->cpjxk"
    by_cos = mat(cos_y_parts, gathered, spec_y)
    by_sin = mat(sin_y_parts, gathered, spec_y)
    y_real = by_cos[:, 0] + by_sin[:, 1]
    y_imag = by_cos[:, 1] - by_sin[:, 0]

    kernel = jnp.asarray(x_kernel(span_x))
    wave_y = wavenumber(lax.iota(jnp.int32, width_y), width_y)
    wave_z = wavenumber(me * per_device + lax.iota(jnp.int32, per_device), depth)

    def inverse_y(b_real, b_imag):
        stacked = jnp.stack([b_real, b_imag], axis=1).astype(BF16)
        by_cos = mat(cos_y_parts, stacked, spec_y)
        by_sin = mat(sin_y_parts, stacked, spec_y)
        scale = 1.0 / width_y
        out_real = (by_cos[:, 0] - by_sin[:, 1]) * scale
        out_imag = (by_cos[:, 1] + by_sin[:, 0]) * scale
        return rounded(out_real), rounded(out_imag)

    b_real, b_imag = curl_update(rounded(y_real), rounded(y_imag), wave_y, wave_z, kernel)
    back_real, back_imag = inverse_y(rounded(b_real), rounded(b_imag))

    if hermitian:
        plane_real = by_cos[:, :, 0]
        plane_imag = -by_sin[:, :, 0]
        pb_real, pb_imag = curl_update(
            rounded(plane_real), rounded(plane_imag), wave_y, jnp.zeros((2,), F32), kernel
        )
        pback_real, _ = inverse_y(rounded(pb_real), rounded(pb_imag))
        is_first = me == 0
        fixed_real = jnp.where(is_first, pback_real[:, 0], back_real[:, 0])
        fixed_imag = jnp.where(is_first, pback_real[:, 1], back_imag[:, 0])
        back_real = jnp.concatenate([fixed_real[:, None], back_real[:, 1:]], axis=1)
        back_imag = jnp.concatenate([fixed_imag[:, None], back_imag[:, 1:]], axis=1)

    outgoing = jnp.stack([back_real, back_imag], axis=1).astype(BF16)
    outgoing = outgoing.reshape(
        members, 2, per_device, row_count, local_x, col_count, local_y
    )
    outgoing = jnp.moveaxis(outgoing, 4, 1).reshape(
        members, local_x, 2, per_device, devices, local_y
    )
    returned = lax.all_to_all(
        outgoing, ("row", "col"), split_axis=4, concat_axis=3, tiled=True
    )
    returned = returned.reshape(members, local_x, 2 * columns, local_y)

    weight = np.full((2 * columns,), 1.0 / depth, np.float32)
    if hermitian:
        weight[:] = 2.0 / depth
        weight[0] = 1.0 / depth
        weight[columns] = 1.0 / depth
    weight = jnp.asarray(weight)[:, None]
    weighted = (returned.astype(F32) * weight).astype(BF16)
    spec_back = "clky,zk->clyz"
    field = jnp.einsum(spec_back, weighted, z_high, preferred_element_type=F32) + jnp.einsum(
        spec_back, weighted, z_low, preferred_element_type=F32
    )
    return (magnetic.astype(F32) + field).astype(BF16)


def solution(mesh):
    in_specs = (
        P(None, "row", "col", None),
        P(None, "row", "col", None),
        P("row", "col", None),
        P(),
    )
    out_specs = P(None, "row", "col", None)
    return jax.shard_map(
        on_device, mesh=mesh, in_specs=in_specs, out_specs=out_specs, check_vma=False
    )
```

```python
import math

import numpy as np
import jax
import jax.numpy as jnp
from jax import lax
from jax.sharding import PartitionSpec as P

TIME_STEP = 0.5
F32 = jnp.float32
BF16 = jnp.bfloat16


def wavenumber(wave_index, length):
    signed = jnp.where(2 * wave_index < length, wave_index, wave_index - length)
    return jnp.where(
        2 * wave_index == length, 0.0, signed.astype(F32) * (2.0 * math.pi / length)
    )


def rounded(values):
    return lax.reduce_precision(values, exponent_bits=8, mantissa_bits=7)


def split_parts(values):
    high = rounded(values)
    low = values - high
    return high.astype(BF16), low.astype(BF16)


def direct_phase(rows, cols, length, step):
    product = (lax.iota(jnp.int32, rows)[:, None] * step) * lax.iota(jnp.int32, cols)[None, :]
    angle = (product % length).astype(F32) * (2.0 * math.pi / length)
    return jnp.cos(angle), jnp.sin(angle)


def phase_table(rows, cols, length):
    block = 32
    if rows % block or rows <= block:
        return direct_phase(rows, cols, length, 1)
    outer_cos, outer_sin = direct_phase(rows // block, cols, length, block)
    inner_cos, inner_sin = direct_phase(block, cols, length, 1)
    outer_cos, outer_sin = outer_cos[:, None], outer_sin[:, None]
    inner_cos, inner_sin = inner_cos[None], inner_sin[None]
    cosine = outer_cos * inner_cos - outer_sin * inner_sin
    sine = outer_sin * inner_cos + outer_cos * inner_sin
    return cosine.reshape(rows, cols), sine.reshape(rows, cols)


def x_kernel(span_x):
    index = np.arange(span_x)
    signed = np.where(2 * index < span_x, index, index - span_x)
    qx = np.where(2 * index == span_x, 0.0, signed * (2.0 * math.pi / span_x))
    shift = np.arange(span_x)
    phases = np.exp(2j * math.pi * np.outer(shift, index) / span_x)
    taps = (phases * (-0.5j * qx)[None, :]).sum(axis=1) / span_x
    taps = taps.real
    matrix = taps[(shift[:, None] - shift[None, :]) % span_x]
    return matrix.astype(np.float32)


def mat(table_parts, operand, spec):
    total = None
    for part in table_parts:
        term = jnp.einsum(spec, part, operand, preferred_element_type=F32)
        total = term if total is None else total + term
    return total


def curl_update(y_real, y_imag, wave_y, wave_z, kernel):
    half = TIME_STEP

    def along_x(values):
        return jnp.einsum("ab,jbk->jak", kernel, values, precision=lax.Precision.HIGHEST)

    xr, yr, zr = y_real[0], y_real[1], y_real[2]
    xi, yi, zi = y_imag[0], y_imag[1], y_imag[2]
    qy = half * wave_y
    qz = half * wave_z[:, None, None]
    gyr, gyi = along_x(yr), along_x(yi)
    gzr, gzi = along_x(zr), along_x(zi)
    b_real = jnp.stack([qy * zi - qz * yi, qz * xi - gzr, gyr - qy * xi])
    b_imag = jnp.stack([qz * yr - qy * zr, -qz * xr - gzi, gyi + qy * xr])
    return b_real, b_imag


def on_device(displacement, magnetic, region, permittivity):
    row_count = lax.axis_size("row")
    col_count = lax.axis_size("col")
    devices = row_count * col_count
    members, local_x, local_y, depth = displacement.shape
    width_y = local_y * col_count
    span_x = local_x * row_count
    hermitian = (depth // 2) % devices == 0
    columns = depth // 2 if hermitian else depth
    per_device = columns // devices
    me = lax.axis_index("row") * col_count + lax.axis_index("col")

    reciprocal = 1.0 / permittivity
    regions = permittivity.shape[0]
    one_hot = (region[..., None] == lax.iota(jnp.int32, regions)).astype(BF16)
    first = rounded(reciprocal)
    rest = reciprocal - first
    second = rounded(rest)
    parts = (first, second, rest - second)
    cell_scale = None
    for part in parts:
        term = jnp.einsum(
            "...k,k->...", one_hot, part.astype(BF16), preferred_element_type=F32
        )
        cell_scale = term if cell_scale is None else cell_scale + term
    electric = displacement.astype(F32) * cell_scale[None]

    cos_z, sin_z = phase_table(depth, columns, depth)
    if hermitian:
        parity = (1 - 2 * (lax.iota(jnp.int32, depth) % 2)).astype(F32)
        sin_part = jnp.concatenate([parity[:, None], -sin_z[:, 1:]], axis=1)
    else:
        sin_part = -sin_z
    table_z = jnp.concatenate([cos_z, sin_part], axis=1)
    z_high, z_low = split_parts(table_z)

    e_high, e_low = split_parts(electric)
    spec_z = "zk,clyz->clky"
    spectrum = (
        jnp.einsum(spec_z, z_high, e_high, preferred_element_type=F32)
        + jnp.einsum(spec_z, z_high, e_low, preferred_element_type=F32)
        + jnp.einsum(spec_z, z_low, e_high, preferred_element_type=F32)
    )
    spectrum = spectrum.astype(BF16).reshape(
        members, local_x, 2, devices, per_device, local_y
    )
    gathered = lax.all_to_all(
        spectrum, ("row", "col"), split_axis=3, concat_axis=5, tiled=True
    )
    gathered = gathered.reshape(members, local_x, 2, per_device, row_count, width_y)
    gathered = jnp.moveaxis(gathered, 1, 4).reshape(
        members, 2, per_device, span_x, width_y
    )

    cos_y, sin_y = phase_table(width_y, width_y, width_y)
    cos_y_parts = split_parts(cos_y)
    sin_y_parts = split_parts(sin_y)
    spec_y = "yk,cpjxy->cpjxk"
    by_cos = mat(cos_y_parts, gathered, spec_y)
    by_sin = mat(sin_y_parts, gathered, spec_y)
    y_real = by_cos[:, 0] + by_sin[:, 1]
    y_imag = by_cos[:, 1] - by_sin[:, 0]

    kernel = jnp.asarray(x_kernel(span_x))
    wave_y = wavenumber(lax.iota(jnp.int32, width_y), width_y)
    wave_z = wavenumber(me * per_device + lax.iota(jnp.int32, per_device), depth)

    def inverse_y(b_real, b_imag):
        stacked = jnp.stack([b_real, b_imag], axis=1).astype(BF16)
        by_cos = mat(cos_y_parts, stacked, spec_y)
        by_sin = mat(sin_y_parts, stacked, spec_y)
        scale = 1.0 / width_y
        out_real = (by_cos[:, 0] - by_sin[:, 1]) * scale
        out_imag = (by_cos[:, 1] + by_sin[:, 0]) * scale
        return rounded(out_real), rounded(out_imag)

    b_real, b_imag = curl_update(rounded(y_real), rounded(y_imag), wave_y, wave_z, kernel)
    back_real, back_imag = inverse_y(rounded(b_real), rounded(b_imag))

    if hermitian:
        plane_real = by_cos[:, :, 0]
        plane_imag = -by_sin[:, :, 0]
        pb_real, pb_imag = curl_update(
            rounded(plane_real), rounded(plane_imag), wave_y, jnp.zeros((2,), F32), kernel
        )
        pback_real, _ = inverse_y(rounded(pb_real), rounded(pb_imag))
        is_first = me == 0
        fixed_real = jnp.where(is_first, pback_real[:, 0], back_real[:, 0])
        fixed_imag = jnp.where(is_first, pback_real[:, 1], back_imag[:, 0])
        back_real = jnp.concatenate([fixed_real[:, None], back_real[:, 1:]], axis=1)
        back_imag = jnp.concatenate([fixed_imag[:, None], back_imag[:, 1:]], axis=1)

    outgoing = jnp.stack([back_real, back_imag], axis=1).astype(BF16)
    outgoing = outgoing.reshape(
        members, 2, per_device, row_count, local_x, col_count, local_y
    )
    outgoing = jnp.moveaxis(outgoing, 4, 1).reshape(
        members, local_x, 2, per_device, devices, local_y
    )
    returned = lax.all_to_all(
        outgoing, ("row", "col"), split_axis=4, concat_axis=3, tiled=True
    )
    returned = returned.reshape(members, local_x, 2 * columns, local_y)

    weight = np.full((2 * columns,), 1.0 / depth, np.float32)
    if hermitian:
        weight[:] = 2.0 / depth
        weight[0] = 1.0 / depth
        weight[columns] = 1.0 / depth
    weight = jnp.asarray(weight)[:, None]
    weighted = (returned.astype(F32) * weight).astype(BF16)
    spec_back = "clky,zk->clyz"
    field = jnp.einsum(spec_back, weighted, z_high, preferred_element_type=F32) + jnp.einsum(
        spec_back, weighted, z_low, preferred_element_type=F32
    )
    return (magnetic.astype(F32) + field).astype(BF16)


def solution(mesh):
    in_specs = (
        P(None, "row", "col", None),
        P(None, "row", "col", None),
        P("row", "col", None),
        P(),
    )
    out_specs = P(None, "row", "col", None)
    return jax.shard_map(
        on_device, mesh=mesh, in_specs=in_specs, out_specs=out_specs, check_vma=False
    )
```

```python
import math

import numpy as np
import jax
import jax.numpy as jnp
from jax import lax
from jax.sharding import PartitionSpec as P

TIME_STEP = 0.5
F32 = jnp.float32
BF16 = jnp.bfloat16


def wavenumber(wave_index, length):
    signed = jnp.where(2 * wave_index < length, wave_index, wave_index - length)
    return jnp.where(
        2 * wave_index == length, 0.0, signed.astype(F32) * (2.0 * math.pi / length)
    )


def rounded(values):
    return lax.reduce_precision(values, exponent_bits=8, mantissa_bits=7)


def split_parts(values):
    high = rounded(values)
    low = values - high
    return high.astype(BF16), low.astype(BF16)


def direct_phase(rows, cols, length, step):
    product = (lax.iota(jnp.int32, rows)[:, None] * step) * lax.iota(jnp.int32, cols)[None, :]
    angle = (product % length).astype(F32) * (2.0 * math.pi / length)
    return jnp.cos(angle), jnp.sin(angle)


def phase_table(rows, cols, length):
    block = 32
    if rows % block or rows <= block:
        return direct_phase(rows, cols, length, 1)
    outer_cos, outer_sin = direct_phase(rows // block, cols, length, block)
    inner_cos, inner_sin = direct_phase(block, cols, length, 1)
    outer_cos, outer_sin = outer_cos[:, None], outer_sin[:, None]
    inner_cos, inner_sin = inner_cos[None], inner_sin[None]
    cosine = outer_cos * inner_cos - outer_sin * inner_sin
    sine = outer_sin * inner_cos + outer_cos * inner_sin
    return cosine.reshape(rows, cols), sine.reshape(rows, cols)


def x_kernel(span_x):
    index = np.arange(span_x)
    signed = np.where(2 * index < span_x, index, index - span_x)
    qx = np.where(2 * index == span_x, 0.0, signed * (2.0 * math.pi / span_x))
    shift = np.arange(span_x)
    phases = np.exp(2j * math.pi * np.outer(shift, index) / span_x)
    taps = (phases * (-0.5j * qx)[None, :]).sum(axis=1) / span_x
    taps = taps.real
    matrix = taps[(shift[:, None] - shift[None, :]) % span_x]
    return matrix.astype(np.float32)


def mat(table_parts, operand, spec):
    total = None
    for part in table_parts:
        term = jnp.einsum(spec, part, operand, preferred_element_type=F32)
        total = term if total is None else total + term
    return total


def curl_update(y_real, y_imag, wave_y, wave_z, kernel):
    half = TIME_STEP

    def along_x(values):
        return jnp.einsum("ab,jbk->jak", kernel, values, precision=lax.Precision.HIGHEST)

    xr, yr, zr = y_real[0], y_real[1], y_real[2]
    xi, yi, zi = y_imag[0], y_imag[1], y_imag[2]
    qy = half * wave_y
    qz = half * wave_z[:, None, None]
    gyr, gyi = along_x(yr), along_x(yi)
    gzr, gzi = along_x(zr), along_x(zi)
    b_real = jnp.stack([qy * zi - qz * yi, qz * xi - gzr, gyr - qy * xi])
    b_imag = jnp.stack([qz * yr - qy * zr, -qz * xr - gzi, gyi + qy * xr])
    return b_real, b_imag


def on_device(displacement, magnetic, region, permittivity):
    row_count = lax.axis_size("row")
    col_count = lax.axis_size("col")
    devices = row_count * col_count
    members, local_x, local_y, depth = displacement.shape
    width_y = local_y * col_count
    span_x = local_x * row_count
    hermitian = (depth // 2) % devices == 0
    columns = depth // 2 if hermitian else depth
    per_device = columns // devices
    me = lax.axis_index("row") * col_count + lax.axis_index("col")

    reciprocal = 1.0 / permittivity
    regions = permittivity.shape[0]
    one_hot = (region[..., None] == lax.iota(jnp.int32, regions)).astype(BF16)
    first = rounded(reciprocal)
    rest = reciprocal - first
    second = rounded(rest)
    parts = (first, second, rest - second)
    cell_scale = None
    for part in parts:
        term = jnp.einsum(
            "...k,k->...", one_hot, part.astype(BF16), preferred_element_type=F32
        )
        cell_scale = term if cell_scale is None else cell_scale + term
    electric = displacement.astype(F32) * cell_scale[None]

    cos_z, sin_z = phase_table(depth, columns, depth)
    if hermitian:
        parity = (1 - 2 * (lax.iota(jnp.int32, depth) % 2)).astype(F32)
        sin_part = jnp.concatenate([parity[:, None], -sin_z[:, 1:]], axis=1)
    else:
        sin_part = -sin_z
    table_z = jnp.stack(
        [cos_z.reshape(depth, devices, per_device), sin_part.reshape(depth, devices, per_device)],
        axis=2,
    ).reshape(depth, 2 * columns)
    z_high, z_low = split_parts(table_z)
    rows = members * local_x * local_y

    e_high, e_low = split_parts(electric.reshape(rows, depth))
    spec_z = "zk,rz->kr"
    spectrum = (
        jnp.einsum(spec_z, z_high, e_high, preferred_element_type=F32)
        + jnp.einsum(spec_z, z_high, e_low, preferred_element_type=F32)
        + jnp.einsum(spec_z, z_low, e_high, preferred_element_type=F32)
    )
    spectrum = spectrum.astype(BF16).reshape(
        devices, 2, per_device, members, local_x, local_y
    )
    gathered = lax.all_to_all(
        spectrum, ("row", "col"), split_axis=0, concat_axis=0, tiled=True
    )
    gathered = gathered.reshape(
        row_count, col_count, 2, per_device, members, local_x, local_y
    )
    gathered = jnp.transpose(gathered, (4, 2, 3, 0, 5, 1, 6)).reshape(
        members, 2, per_device, span_x, width_y
    )

    cos_y, sin_y = phase_table(width_y, width_y, width_y)
    cos_y_parts = split_parts(cos_y)
    sin_y_parts = split_parts(sin_y)
    spec_y = "yk,cpjxy->cpjxk"
    by_cos = mat(cos_y_parts, gathered, spec_y)
    by_sin = mat(sin_y_parts, gathered, spec_y)
    y_real = by_cos[:, 0] + by_sin[:, 1]
    y_imag = by_cos[:, 1] - by_sin[:, 0]

    kernel = jnp.asarray(x_kernel(span_x))
    wave_y = wavenumber(lax.iota(jnp.int32, width_y), width_y)
    wave_z = wavenumber(me * per_device + lax.iota(jnp.int32, per_device), depth)

    def inverse_y(b_real, b_imag):
        stacked = jnp.stack([b_real, b_imag], axis=1).astype(BF16)
        by_cos = mat(cos_y_parts, stacked, spec_y)
        by_sin = mat(sin_y_parts, stacked, spec_y)
        scale = 1.0 / width_y
        out_real = (by_cos[:, 0] - by_sin[:, 1]) * scale
        out_imag = (by_cos[:, 1] + by_sin[:, 0]) * scale
        return rounded(out_real), rounded(out_imag)

    b_real, b_imag = curl_update(rounded(y_real), rounded(y_imag), wave_y, wave_z, kernel)
    back_real, back_imag = inverse_y(rounded(b_real), rounded(b_imag))

    if hermitian:
        plane_real = by_cos[:, :, 0]
        plane_imag = -by_sin[:, :, 0]
        pb_real, pb_imag = curl_update(
            rounded(plane_real), rounded(plane_imag), wave_y, jnp.zeros((2,), F32), kernel
        )
        pback_real, _ = inverse_y(rounded(pb_real), rounded(pb_imag))
        is_first = me == 0
        fixed_real = jnp.where(is_first, pback_real[:, 0], back_real[:, 0])
        fixed_imag = jnp.where(is_first, pback_real[:, 1], back_imag[:, 0])
        back_real = jnp.concatenate([fixed_real[:, None], back_real[:, 1:]], axis=1)
        back_imag = jnp.concatenate([fixed_imag[:, None], back_imag[:, 1:]], axis=1)

    outgoing = jnp.stack([back_real, back_imag], axis=1).astype(BF16)
    outgoing = outgoing.reshape(
        members, 2, per_device, row_count, local_x, col_count, local_y
    )
    outgoing = jnp.transpose(outgoing, (3, 5, 1, 2, 0, 4, 6)).reshape(
        devices, 2, per_device, members, local_x, local_y
    )
    returned = lax.all_to_all(
        outgoing, ("row", "col"), split_axis=0, concat_axis=0, tiled=True
    )
    returned = returned.reshape(2 * columns, rows)

    weight = np.full((devices, 2, per_device), 1.0 / depth, np.float32)
    if hermitian:
        weight[:] = 2.0 / depth
        weight[0, :, 0] = 1.0 / depth
    weight = jnp.asarray(weight.reshape(2 * columns, 1))
    weighted = (returned.astype(F32) * weight).astype(BF16)
    spec_back = "kr,zk->rz"
    field = jnp.einsum(spec_back, weighted, z_high, preferred_element_type=F32) + jnp.einsum(
        spec_back, weighted, z_low, preferred_element_type=F32
    )
    field = field.reshape(members, local_x, local_y, depth)
    return (magnetic.astype(F32) + field).astype(BF16)


def solution(mesh):
    in_specs = (
        P(None, "row", "col", None),
        P(None, "row", "col", None),
        P("row", "col", None),
        P(),
    )
    out_specs = P(None, "row", "col", None)
    return jax.shard_map(
        on_device, mesh=mesh, in_specs=in_specs, out_specs=out_specs, check_vma=False
    )
```

```python
import math

import numpy as np
import jax
import jax.numpy as jnp
from jax import lax
from jax.sharding import PartitionSpec as P

TIME_STEP = 0.5
F32 = jnp.float32
BF16 = jnp.bfloat16


def wavenumber(wave_index, length):
    signed = jnp.where(2 * wave_index < length, wave_index, wave_index - length)
    return jnp.where(
        2 * wave_index == length, 0.0, signed.astype(F32) * (2.0 * math.pi / length)
    )


def rounded(values):
    return lax.reduce_precision(values, exponent_bits=8, mantissa_bits=7)


def split_parts(values):
    high = rounded(values)
    low = values - high
    return high.astype(BF16), low.astype(BF16)


def direct_phase(rows, cols, length, step):
    product = (lax.iota(jnp.int32, rows)[:, None] * step) * lax.iota(jnp.int32, cols)[None, :]
    angle = (product % length).astype(F32) * (2.0 * math.pi / length)
    return jnp.cos(angle), jnp.sin(angle)


def phase_table(rows, cols, length):
    block = 32
    if rows % block or rows <= block:
        return direct_phase(rows, cols, length, 1)
    outer_cos, outer_sin = direct_phase(rows // block, cols, length, block)
    inner_cos, inner_sin = direct_phase(block, cols, length, 1)
    outer_cos, outer_sin = outer_cos[:, None], outer_sin[:, None]
    inner_cos, inner_sin = inner_cos[None], inner_sin[None]
    cosine = outer_cos * inner_cos - outer_sin * inner_sin
    sine = outer_sin * inner_cos + outer_cos * inner_sin
    return cosine.reshape(rows, cols), sine.reshape(rows, cols)


def x_kernel(span_x):
    index = np.arange(span_x)
    signed = np.where(2 * index < span_x, index, index - span_x)
    qx = np.where(2 * index == span_x, 0.0, signed * (2.0 * math.pi / span_x))
    shift = np.arange(span_x)
    phases = np.exp(2j * math.pi * np.outer(shift, index) / span_x)
    taps = (phases * (-0.5j * qx)[None, :]).sum(axis=1) / span_x
    taps = taps.real
    matrix = taps[(shift[:, None] - shift[None, :]) % span_x]
    return matrix.astype(np.float32)


def mat(table_parts, operand, spec):
    total = None
    for part in table_parts:
        term = jnp.einsum(spec, part, operand, preferred_element_type=F32)
        total = term if total is None else total + term
    return total


def curl_update(y_real, y_imag, wave_y, wave_z, kernel):
    half = TIME_STEP

    def along_x(values):
        return jnp.einsum("ab,jbk->jak", kernel, values, precision=lax.Precision.HIGHEST)

    xr, yr, zr = y_real[0], y_real[1], y_real[2]
    xi, yi, zi = y_imag[0], y_imag[1], y_imag[2]
    qy = half * wave_y
    qz = half * wave_z[:, None, None]
    gyr, gyi = along_x(yr), along_x(yi)
    gzr, gzi = along_x(zr), along_x(zi)
    b_real = jnp.stack([qy * zi - qz * yi, qz * xi - gzr, gyr - qy * xi])
    b_imag = jnp.stack([qz * yr - qy * zr, -qz * xr - gzi, gyi + qy * xr])
    return b_real, b_imag


def on_device(displacement, magnetic, region, permittivity):
    row_count = lax.axis_size("row")
    col_count = lax.axis_size("col")
    devices = row_count * col_count
    members, local_x, local_y, depth = displacement.shape
    width_y = local_y * col_count
    span_x = local_x * row_count
    hermitian = (depth // 2) % devices == 0
    columns = depth // 2 if hermitian else depth
    per_device = columns // devices
    me = lax.axis_index("row") * col_count + lax.axis_index("col")

    reciprocal = 1.0 / permittivity
    regions = permittivity.shape[0]
    one_hot = (region[..., None] == lax.iota(jnp.int32, regions)).astype(BF16)
    first = rounded(reciprocal)
    rest = reciprocal - first
    second = rounded(rest)
    parts = (first, second, rest - second)
    cell_scale = None
    for part in parts:
        term = jnp.einsum(
            "...k,k->...", one_hot, part.astype(BF16), preferred_element_type=F32
        )
        cell_scale = term if cell_scale is None else cell_scale + term
    electric = displacement.astype(F32) * cell_scale[None]

    cos_z, sin_z = phase_table(columns, depth, depth)
    if hermitian:
        parity = (1 - 2 * (lax.iota(jnp.int32, depth) % 2)).astype(F32)
        sin_part = jnp.concatenate([parity[None, :], -sin_z[1:]], axis=0)
    else:
        sin_part = -sin_z
    table_z = jnp.stack(
        [cos_z.reshape(devices, per_device, depth), sin_part.reshape(devices, per_device, depth)],
        axis=1,
    ).reshape(2 * columns, depth)
    z_high, z_low = split_parts(table_z)
    rows = members * local_x * local_y

    e_high, e_low = split_parts(electric.reshape(rows, depth))
    spec_z = "kz,rz->kr"
    spectrum = (
        jnp.einsum(spec_z, z_high, e_high, preferred_element_type=F32)
        + jnp.einsum(spec_z, z_high, e_low, preferred_element_type=F32)
        + jnp.einsum(spec_z, z_low, e_high, preferred_element_type=F32)
    )
    spectrum = spectrum.astype(BF16).reshape(
        devices, 2, per_device, members, local_x, local_y
    )
    gathered = lax.all_to_all(
        spectrum, ("row", "col"), split_axis=0, concat_axis=0, tiled=True
    )
    gathered = gathered.reshape(
        row_count, col_count, 2, per_device, members, local_x, local_y
    )
    gathered = jnp.transpose(gathered, (4, 2, 3, 0, 5, 1, 6)).reshape(
        members, 2, per_device, span_x, width_y
    )

    cos_y, sin_y = phase_table(width_y, width_y, width_y)
    cos_y_parts = split_parts(cos_y)
    sin_y_parts = split_parts(sin_y)
    spec_y = "yk,cpjxy->cpjxk"
    by_cos = mat(cos_y_parts, gathered, spec_y)
    by_sin = mat(sin_y_parts, gathered, spec_y)
    y_real = by_cos[:, 0] + by_sin[:, 1]
    y_imag = by_cos[:, 1] - by_sin[:, 0]

    kernel = jnp.asarray(x_kernel(span_x))
    wave_y = wavenumber(lax.iota(jnp.int32, width_y), width_y)
    wave_z = wavenumber(me * per_device + lax.iota(jnp.int32, per_device), depth)

    def inverse_y(b_real, b_imag):
        stacked = jnp.stack([b_real, b_imag], axis=1).astype(BF16)
        by_cos = mat(cos_y_parts, stacked, spec_y)
        by_sin = mat(sin_y_parts, stacked, spec_y)
        scale = 1.0 / width_y
        out_real = (by_cos[:, 0] - by_sin[:, 1]) * scale
        out_imag = (by_cos[:, 1] + by_sin[:, 0]) * scale
        return rounded(out_real), rounded(out_imag)

    b_real, b_imag = curl_update(rounded(y_real), rounded(y_imag), wave_y, wave_z, kernel)
    back_real, back_imag = inverse_y(rounded(b_real), rounded(b_imag))

    if hermitian:
        plane_real = by_cos[:, :, 0]
        plane_imag = -by_sin[:, :, 0]
        pb_real, pb_imag = curl_update(
            rounded(plane_real), rounded(plane_imag), wave_y, jnp.zeros((2,), F32), kernel
        )
        pback_real, _ = inverse_y(rounded(pb_real), rounded(pb_imag))
        is_first = me == 0
        fixed_real = jnp.where(is_first, pback_real[:, 0], back_real[:, 0])
        fixed_imag = jnp.where(is_first, pback_real[:, 1], back_imag[:, 0])
        back_real = jnp.concatenate([fixed_real[:, None], back_real[:, 1:]], axis=1)
        back_imag = jnp.concatenate([fixed_imag[:, None], back_imag[:, 1:]], axis=1)

    outgoing = jnp.stack([back_real, back_imag], axis=1).astype(BF16)
    outgoing = outgoing.reshape(
        members, 2, per_device, row_count, local_x, col_count, local_y
    )
    outgoing = jnp.transpose(outgoing, (3, 5, 1, 2, 0, 4, 6)).reshape(
        devices, 2, per_device, members, local_x, local_y
    )
    returned = lax.all_to_all(
        outgoing, ("row", "col"), split_axis=0, concat_axis=0, tiled=True
    )
    returned = returned.reshape(2 * columns, rows)

    weight = np.full((devices, 2, per_device), 1.0 / depth, np.float32)
    if hermitian:
        weight[:] = 2.0 / depth
        weight[0, :, 0] = 1.0 / depth
    weight = jnp.asarray(weight.reshape(2 * columns, 1))
    weighted = (returned.astype(F32) * weight).astype(BF16)
    spec_back = "kr,kz->rz"
    field = jnp.einsum(spec_back, weighted, z_high, preferred_element_type=F32) + jnp.einsum(
        spec_back, weighted, z_low, preferred_element_type=F32
    )
    field = field.reshape(members, local_x, local_y, depth)
    return (magnetic.astype(F32) + field).astype(BF16)


def solution(mesh):
    in_specs = (
        P(None, "row", "col", None),
        P(None, "row", "col", None),
        P("row", "col", None),
        P(),
    )
    out_specs = P(None, "row", "col", None)
    return jax.shard_map(
        on_device, mesh=mesh, in_specs=in_specs, out_specs=out_specs, check_vma=False
    )
```

```python
import math

import numpy as np
import jax
import jax.numpy as jnp
from jax import lax
from jax.sharding import PartitionSpec as P

TIME_STEP = 0.5
F32 = jnp.float32
BF16 = jnp.bfloat16


def wavenumber(wave_index, length):
    signed = jnp.where(2 * wave_index < length, wave_index, wave_index - length)
    return jnp.where(
        2 * wave_index == length, 0.0, signed.astype(F32) * (2.0 * math.pi / length)
    )


def rounded(values):
    return lax.reduce_precision(values, exponent_bits=8, mantissa_bits=7)


def split_parts(values):
    high = rounded(values)
    low = values - high
    return high.astype(BF16), low.astype(BF16)


def direct_phase(rows, cols, length, step):
    product = (lax.iota(jnp.int32, rows)[:, None] * step) * lax.iota(jnp.int32, cols)[None, :]
    angle = (product % length).astype(F32) * (2.0 * math.pi / length)
    return jnp.cos(angle), jnp.sin(angle)


def phase_table(rows, cols, length):
    block = 32
    if rows % block or rows <= block:
        return direct_phase(rows, cols, length, 1)
    outer_cos, outer_sin = direct_phase(rows // block, cols, length, block)
    inner_cos, inner_sin = direct_phase(block, cols, length, 1)
    outer_cos, outer_sin = outer_cos[:, None], outer_sin[:, None]
    inner_cos, inner_sin = inner_cos[None], inner_sin[None]
    cosine = outer_cos * inner_cos - outer_sin * inner_sin
    sine = outer_sin * inner_cos + outer_cos * inner_sin
    return cosine.reshape(rows, cols), sine.reshape(rows, cols)


def x_kernel(span_x):
    index = np.arange(span_x)
    signed = np.where(2 * index < span_x, index, index - span_x)
    qx = np.where(2 * index == span_x, 0.0, signed * (2.0 * math.pi / span_x))
    shift = np.arange(span_x)
    phases = np.exp(2j * math.pi * np.outer(shift, index) / span_x)
    taps = (phases * (-0.5j * qx)[None, :]).sum(axis=1) / span_x
    taps = taps.real
    matrix = taps[(shift[:, None] - shift[None, :]) % span_x]
    return matrix.astype(np.float32)


def mat(table_parts, operand, spec):
    total = None
    for part in table_parts:
        term = jnp.einsum(spec, part, operand, preferred_element_type=F32)
        total = term if total is None else total + term
    return total


def curl_update(y_real, y_imag, wave_y, wave_z, kernel):
    half = TIME_STEP

    def along_x(values):
        return jnp.einsum("ab,jbk->jak", kernel, values, precision=lax.Precision.HIGHEST)

    xr, yr, zr = y_real[0], y_real[1], y_real[2]
    xi, yi, zi = y_imag[0], y_imag[1], y_imag[2]
    qy = half * wave_y
    qz = half * wave_z[:, None, None]
    gyr, gyi = along_x(yr), along_x(yi)
    gzr, gzi = along_x(zr), along_x(zi)
    b_real = jnp.stack([qy * zi - qz * yi, qz * xi - gzr, gyr - qy * xi])
    b_imag = jnp.stack([qz * yr - qy * zr, -qz * xr - gzi, gyi + qy * xr])
    return b_real, b_imag


def on_device(displacement, magnetic, region, permittivity):
    row_count = lax.axis_size("row")
    col_count = lax.axis_size("col")
    devices = row_count * col_count
    members, local_x, local_y, depth = displacement.shape
    width_y = local_y * col_count
    span_x = local_x * row_count
    hermitian = (depth // 2) % devices == 0
    columns = depth // 2 if hermitian else depth
    per_device = columns // devices
    me = lax.axis_index("row") * col_count + lax.axis_index("col")

    reciprocal = 1.0 / permittivity
    regions = permittivity.shape[0]
    one_hot = (region[..., None] == lax.iota(jnp.int32, regions)).astype(BF16)
    first = rounded(reciprocal)
    rest = reciprocal - first
    second = rounded(rest)
    parts = (first, second, rest - second)
    cell_scale = None
    for part in parts:
        term = jnp.einsum(
            "...k,k->...", one_hot, part.astype(BF16), preferred_element_type=F32
        )
        cell_scale = term if cell_scale is None else cell_scale + term
    electric = displacement.astype(F32) * cell_scale[None]

    cos_z, sin_z = phase_table(columns, depth, depth)
    if hermitian:
        parity = (1 - 2 * (lax.iota(jnp.int32, depth) % 2)).astype(F32)
        sin_part = jnp.concatenate([parity[None, :], -sin_z[1:]], axis=0)
    else:
        sin_part = -sin_z
    table_z = jnp.stack(
        [cos_z.reshape(devices, per_device, depth), sin_part.reshape(devices, per_device, depth)],
        axis=1,
    ).reshape(2 * columns, depth)
    z_high, z_low = split_parts(table_z)
    rows = members * local_x * local_y

    e_high, e_low = split_parts(electric.reshape(rows, depth))
    spec_z = "kz,rz->kr"
    spectrum = (
        jnp.einsum(spec_z, z_high, e_high, preferred_element_type=F32)
        + jnp.einsum(spec_z, z_high, e_low, preferred_element_type=F32)
        + jnp.einsum(spec_z, z_low, e_high, preferred_element_type=F32)
    )
    spectrum = spectrum.astype(BF16).reshape(devices, 2 * per_device, rows)
    gathered = lax.all_to_all(
        spectrum, ("row", "col"), split_axis=0, concat_axis=0, tiled=True
    )
    gathered = gathered.reshape(
        row_count, col_count, 2, per_device, members, local_x, local_y
    )
    gathered = jnp.transpose(gathered, (4, 2, 3, 0, 5, 1, 6)).reshape(
        members, 2, per_device, span_x, width_y
    )

    cos_y, sin_y = phase_table(width_y, width_y, width_y)
    cos_y_parts = split_parts(cos_y)
    sin_y_parts = split_parts(sin_y)
    spec_y = "yk,cpjxy->cpjxk"
    by_cos = mat(cos_y_parts, gathered, spec_y)
    by_sin = mat(sin_y_parts, gathered, spec_y)
    y_real = by_cos[:, 0] + by_sin[:, 1]
    y_imag = by_cos[:, 1] - by_sin[:, 0]

    kernel = jnp.asarray(x_kernel(span_x))
    wave_y = wavenumber(lax.iota(jnp.int32, width_y), width_y)
    wave_z = wavenumber(me * per_device + lax.iota(jnp.int32, per_device), depth)

    def inverse_y(b_real, b_imag):
        stacked = jnp.stack([b_real, b_imag], axis=1).astype(BF16)
        by_cos = mat(cos_y_parts, stacked, spec_y)
        by_sin = mat(sin_y_parts, stacked, spec_y)
        scale = 1.0 / width_y
        out_real = (by_cos[:, 0] - by_sin[:, 1]) * scale
        out_imag = (by_cos[:, 1] + by_sin[:, 0]) * scale
        return rounded(out_real), rounded(out_imag)

    b_real, b_imag = curl_update(rounded(y_real), rounded(y_imag), wave_y, wave_z, kernel)
    back_real, back_imag = inverse_y(rounded(b_real), rounded(b_imag))

    if hermitian:
        plane_real = by_cos[:, :, 0]
        plane_imag = -by_sin[:, :, 0]
        pb_real, pb_imag = curl_update(
            rounded(plane_real), rounded(plane_imag), wave_y, jnp.zeros((2,), F32), kernel
        )
        pback_real, _ = inverse_y(rounded(pb_real), rounded(pb_imag))
        is_first = me == 0
        fixed_real = jnp.where(is_first, pback_real[:, 0], back_real[:, 0])
        fixed_imag = jnp.where(is_first, pback_real[:, 1], back_imag[:, 0])
        back_real = jnp.concatenate([fixed_real[:, None], back_real[:, 1:]], axis=1)
        back_imag = jnp.concatenate([fixed_imag[:, None], back_imag[:, 1:]], axis=1)

    outgoing = jnp.stack([back_real, back_imag], axis=1).astype(BF16)
    outgoing = outgoing.reshape(
        members, 2, per_device, row_count, local_x, col_count, local_y
    )
    outgoing = jnp.transpose(outgoing, (3, 5, 1, 2, 0, 4, 6)).reshape(
        devices, 2 * per_device, rows
    )
    returned = lax.all_to_all(
        outgoing, ("row", "col"), split_axis=0, concat_axis=0, tiled=True
    )
    returned = returned.reshape(2 * columns, rows)

    weight = np.full((devices, 2, per_device), 1.0 / depth, np.float32)
    if hermitian:
        weight[:] = 2.0 / depth
        weight[0, :, 0] = 1.0 / depth
    weight = jnp.asarray(weight.reshape(2 * columns, 1))
    weighted = (returned.astype(F32) * weight).astype(BF16)
    spec_back = "kr,kz->rz"
    field = jnp.einsum(spec_back, weighted, z_high, preferred_element_type=F32) + jnp.einsum(
        spec_back, weighted, z_low, preferred_element_type=F32
    )
    field = field.reshape(members, local_x, local_y, depth)
    return (magnetic.astype(F32) + field).astype(BF16)


def solution(mesh):
    in_specs = (
        P(None, "row", "col", None),
        P(None, "row", "col", None),
        P("row", "col", None),
        P(),
    )
    out_specs = P(None, "row", "col", None)
    return jax.shard_map(
        on_device, mesh=mesh, in_specs=in_specs, out_specs=out_specs, check_vma=False
    )
```

```python
import math

import numpy as np
import jax
import jax.numpy as jnp
from jax import lax
from jax.experimental import pallas as pl
from jax.experimental.pallas import tpu as pltpu
from jax.sharding import PartitionSpec as P

TIME_STEP = 0.5
F32 = jnp.float32
BF16 = jnp.bfloat16


def wavenumber(wave_index, length):
    signed = jnp.where(2 * wave_index < length, wave_index, wave_index - length)
    return jnp.where(
        2 * wave_index == length, 0.0, signed.astype(F32) * (2.0 * math.pi / length)
    )


def rounded(values):
    return lax.reduce_precision(values, exponent_bits=8, mantissa_bits=7)


def split_parts(values):
    high = rounded(values)
    low = values - high
    return high.astype(BF16), low.astype(BF16)


def direct_phase(rows, cols, length, step):
    product = (lax.iota(jnp.int32, rows)[:, None] * step) * lax.iota(jnp.int32, cols)[None, :]
    angle = (product % length).astype(F32) * (2.0 * math.pi / length)
    return jnp.cos(angle), jnp.sin(angle)


def phase_table(rows, cols, length):
    block = 32
    if rows % block or rows <= block:
        return direct_phase(rows, cols, length, 1)
    outer_cos, outer_sin = direct_phase(rows // block, cols, length, block)
    inner_cos, inner_sin = direct_phase(block, cols, length, 1)
    outer_cos, outer_sin = outer_cos[:, None], outer_sin[:, None]
    inner_cos, inner_sin = inner_cos[None], inner_sin[None]
    cosine = outer_cos * inner_cos - outer_sin * inner_sin
    sine = outer_sin * inner_cos + outer_cos * inner_sin
    return cosine.reshape(rows, cols), sine.reshape(rows, cols)


def electric_kernel(reciprocal_ref, region_ref, displacement_ref, high_ref, low_ref):
    region = region_ref[...]
    scale = jnp.zeros(region.shape, F32)
    for region_id in range(reciprocal_ref.shape[0]):
        scale = jnp.where(region == region_id, reciprocal_ref[region_id], scale)
    for member in range(displacement_ref.shape[0]):
        field = displacement_ref[member].astype(F32) * scale
        high = field.astype(BF16)
        high_ref[member] = high
        low_ref[member] = (field - high.astype(F32)).astype(BF16)


def electric_parts(displacement, region, reciprocal):
    members, local_x, local_y, depth = displacement.shape
    lines = local_x * local_y
    block = 32 if lines % 32 == 0 else lines
    field_spec = pl.BlockSpec((members, block, depth), lambda index: (0, index, 0))
    shape = jax.ShapeDtypeStruct((members, lines, depth), BF16)
    elements = members * lines * depth
    return pl.pallas_call(
        electric_kernel,
        grid=(lines // block,),
        in_specs=[
            pl.BlockSpec(memory_space=pltpu.SMEM),
            pl.BlockSpec((block, depth), lambda index: (index, 0)),
            field_spec,
        ],
        out_specs=[field_spec, field_spec],
        out_shape=[shape, shape],
        cost_estimate=pl.CostEstimate(
            flops=20 * elements, transcendentals=0, bytes_accessed=6 * elements + 4 * lines * depth
        ),
    )(reciprocal, region.reshape(lines, depth), displacement.reshape(members, lines, depth))


def x_kernel(span_x):
    index = np.arange(span_x)
    signed = np.where(2 * index < span_x, index, index - span_x)
    qx = np.where(2 * index == span_x, 0.0, signed * (2.0 * math.pi / span_x))
    shift = np.arange(span_x)
    phases = np.exp(2j * math.pi * np.outer(shift, index) / span_x)
    taps = (phases * (-0.5j * qx)[None, :]).sum(axis=1) / span_x
    taps = taps.real
    matrix = taps[(shift[:, None] - shift[None, :]) % span_x]
    return matrix.astype(np.float32)


def mat(table_parts, operand, spec):
    total = None
    for part in table_parts:
        term = jnp.einsum(spec, part, operand, preferred_element_type=F32)
        total = term if total is None else total + term
    return total


def curl_update(y_real, y_imag, wave_y, wave_z, kernel):
    half = TIME_STEP

    def along_x(values):
        return jnp.einsum("ab,jbk->jak", kernel, values, precision=lax.Precision.HIGHEST)

    xr, yr, zr = y_real[0], y_real[1], y_real[2]
    xi, yi, zi = y_imag[0], y_imag[1], y_imag[2]
    qy = half * wave_y
    qz = half * wave_z[:, None, None]
    gyr, gyi = along_x(yr), along_x(yi)
    gzr, gzi = along_x(zr), along_x(zi)
    b_real = jnp.stack([qy * zi - qz * yi, qz * xi - gzr, gyr - qy * xi])
    b_imag = jnp.stack([qz * yr - qy * zr, -qz * xr - gzi, gyi + qy * xr])
    return b_real, b_imag


def on_device(displacement, magnetic, region, permittivity):
    row_count = lax.axis_size("row")
    col_count = lax.axis_size("col")
    devices = row_count * col_count
    members, local_x, local_y, depth = displacement.shape
    width_y = local_y * col_count
    span_x = local_x * row_count
    hermitian = (depth // 2) % devices == 0
    columns = depth // 2 if hermitian else depth
    per_device = columns // devices
    me = lax.axis_index("row") * col_count + lax.axis_index("col")

    reciprocal = 1.0 / permittivity

    cos_z, sin_z = phase_table(columns, depth, depth)
    if hermitian:
        parity = (1 - 2 * (lax.iota(jnp.int32, depth) % 2)).astype(F32)
        sin_part = jnp.concatenate([parity[None, :], -sin_z[1:]], axis=0)
    else:
        sin_part = -sin_z
    table_z = jnp.stack(
        [cos_z.reshape(devices, per_device, depth), sin_part.reshape(devices, per_device, depth)],
        axis=1,
    ).reshape(2 * columns, depth)
    z_high, z_low = split_parts(table_z)
    rows = members * local_x * local_y

    e_high, e_low = electric_parts(displacement, region, reciprocal)
    e_high = e_high.reshape(rows, depth)
    e_low = e_low.reshape(rows, depth)
    spec_z = "kz,rz->kr"
    spectrum = (
        jnp.einsum(spec_z, z_high, e_high, preferred_element_type=F32)
        + jnp.einsum(spec_z, z_high, e_low, preferred_element_type=F32)
        + jnp.einsum(spec_z, z_low, e_high, preferred_element_type=F32)
    )
    spectrum = spectrum.astype(BF16).reshape(
        devices, 2, per_device, members, local_x, local_y
    )
    gathered = lax.all_to_all(
        spectrum, ("row", "col"), split_axis=0, concat_axis=0, tiled=True
    )
    gathered = gathered.reshape(
        row_count, col_count, 2, per_device, members, local_x, local_y
    )
    gathered = jnp.transpose(gathered, (4, 2, 3, 0, 5, 1, 6)).reshape(
        members, 2, per_device, span_x, width_y
    )

    cos_y, sin_y = phase_table(width_y, width_y, width_y)
    cos_y_parts = split_parts(cos_y)
    sin_y_parts = split_parts(sin_y)
    spec_y = "yk,cpjxy->cpjxk"
    by_cos = mat(cos_y_parts, gathered, spec_y)
    by_sin = mat(sin_y_parts, gathered, spec_y)
    y_real = by_cos[:, 0] + by_sin[:, 1]
    y_imag = by_cos[:, 1] - by_sin[:, 0]

    kernel = jnp.asarray(x_kernel(span_x))
    wave_y = wavenumber(lax.iota(jnp.int32, width_y), width_y)
    wave_z = wavenumber(me * per_device + lax.iota(jnp.int32, per_device), depth)

    def inverse_y(b_real, b_imag):
        stacked = jnp.stack([b_real, b_imag], axis=1).astype(BF16)
        by_cos = mat(cos_y_parts, stacked, spec_y)
        by_sin = mat(sin_y_parts, stacked, spec_y)
        scale = 1.0 / width_y
        out_real = (by_cos[:, 0] - by_sin[:, 1]) * scale
        out_imag = (by_cos[:, 1] + by_sin[:, 0]) * scale
        return rounded(out_real), rounded(out_imag)

    b_real, b_imag = curl_update(rounded(y_real), rounded(y_imag), wave_y, wave_z, kernel)
    back_real, back_imag = inverse_y(rounded(b_real), rounded(b_imag))

    if hermitian:
        plane_real = by_cos[:, :, 0]
        plane_imag = -by_sin[:, :, 0]
        pb_real, pb_imag = curl_update(
            rounded(plane_real), rounded(plane_imag), wave_y, jnp.zeros((2,), F32), kernel
        )
        pback_real, _ = inverse_y(rounded(pb_real), rounded(pb_imag))
        is_first = me == 0
        fixed_real = jnp.where(is_first, pback_real[:, 0], back_real[:, 0])
        fixed_imag = jnp.where(is_first, pback_real[:, 1], back_imag[:, 0])
        back_real = jnp.concatenate([fixed_real[:, None], back_real[:, 1:]], axis=1)
        back_imag = jnp.concatenate([fixed_imag[:, None], back_imag[:, 1:]], axis=1)

    outgoing = jnp.stack([back_real, back_imag], axis=1).astype(BF16)
    outgoing = outgoing.reshape(
        members, 2, per_device, row_count, local_x, col_count, local_y
    )
    outgoing = jnp.transpose(outgoing, (3, 5, 1, 2, 0, 4, 6)).reshape(
        devices, 2, per_device, members, local_x, local_y
    )
    returned = lax.all_to_all(
        outgoing, ("row", "col"), split_axis=0, concat_axis=0, tiled=True
    )
    returned = returned.reshape(2 * columns, rows)

    weight = np.full((devices, 2, per_device), 1.0 / depth, np.float32)
    if hermitian:
        weight[:] = 2.0 / depth
        weight[0, :, 0] = 1.0 / depth
    weight = jnp.asarray(weight.reshape(2 * columns, 1))
    weighted = (returned.astype(F32) * weight).astype(BF16)
    spec_back = "kr,kz->rz"
    field = jnp.einsum(spec_back, weighted, z_high, preferred_element_type=F32) + jnp.einsum(
        spec_back, weighted, z_low, preferred_element_type=F32
    )
    field = field.reshape(members, local_x, local_y, depth)
    return (magnetic.astype(F32) + field).astype(BF16)


def solution(mesh):
    in_specs = (
        P(None, "row", "col", None),
        P(None, "row", "col", None),
        P("row", "col", None),
        P(),
    )
    out_specs = P(None, "row", "col", None)
    return jax.shard_map(
        on_device, mesh=mesh, in_specs=in_specs, out_specs=out_specs, check_vma=False
    )
```

```python
import math

import numpy as np
import jax
import jax.numpy as jnp
from jax import lax
from jax.sharding import PartitionSpec as P

TIME_STEP = 0.5
F32 = jnp.float32
BF16 = jnp.bfloat16


def wavenumber(wave_index, length):
    signed = jnp.where(2 * wave_index < length, wave_index, wave_index - length)
    return jnp.where(
        2 * wave_index == length, 0.0, signed.astype(F32) * (2.0 * math.pi / length)
    )


def rounded(values):
    return lax.reduce_precision(values, exponent_bits=8, mantissa_bits=7)


def split_parts(values):
    high = rounded(values)
    low = values - high
    return high.astype(BF16), low.astype(BF16)


def direct_phase(rows, cols, length, step):
    product = (lax.iota(jnp.int32, rows)[:, None] * step) * lax.iota(jnp.int32, cols)[None, :]
    angle = (product % length).astype(F32) * (2.0 * math.pi / length)
    return jnp.cos(angle), jnp.sin(angle)


def phase_table(rows, cols, length):
    block = 32
    if rows % block or rows <= block:
        return direct_phase(rows, cols, length, 1)
    outer_cos, outer_sin = direct_phase(rows // block, cols, length, block)
    inner_cos, inner_sin = direct_phase(block, cols, length, 1)
    outer_cos, outer_sin = outer_cos[:, None], outer_sin[:, None]
    inner_cos, inner_sin = inner_cos[None], inner_sin[None]
    cosine = outer_cos * inner_cos - outer_sin * inner_sin
    sine = outer_sin * inner_cos + outer_cos * inner_sin
    return cosine.reshape(rows, cols), sine.reshape(rows, cols)


def x_kernel(span_x):
    index = np.arange(span_x)
    signed = np.where(2 * index < span_x, index, index - span_x)
    qx = np.where(2 * index == span_x, 0.0, signed * (2.0 * math.pi / span_x))
    shift = np.arange(span_x)
    phases = np.exp(2j * math.pi * np.outer(shift, index) / span_x)
    taps = (phases * (-0.5j * qx)[None, :]).sum(axis=1) / span_x
    taps = taps.real
    matrix = taps[(shift[:, None] - shift[None, :]) % span_x]
    return matrix.astype(np.float32)


def mat(table_parts, operand, spec):
    total = None
    for part in table_parts:
        term = jnp.einsum(spec, part, operand, preferred_element_type=F32)
        total = term if total is None else total + term
    return total


def curl_update(y_real, y_imag, wave_y, wave_z, kernel):
    half = TIME_STEP

    def along_x(values):
        return jnp.einsum("ab,jbk->jak", kernel, values, precision=lax.Precision.HIGHEST)

    xr, yr, zr = y_real[0], y_real[1], y_real[2]
    xi, yi, zi = y_imag[0], y_imag[1], y_imag[2]
    qy = half * wave_y
    qz = half * wave_z[:, None, None]
    gyr, gyi = along_x(yr), along_x(yi)
    gzr, gzi = along_x(zr), along_x(zi)
    b_real = jnp.stack([qy * zi - qz * yi, qz * xi - gzr, gyr - qy * xi])
    b_imag = jnp.stack([qz * yr - qy * zr, -qz * xr - gzi, gyi + qy * xr])
    return b_real, b_imag


def on_device(displacement, magnetic, region, permittivity):
    row_count = lax.axis_size("row")
    col_count = lax.axis_size("col")
    devices = row_count * col_count
    members, local_x, local_y, depth = displacement.shape
    width_y = local_y * col_count
    span_x = local_x * row_count
    hermitian = (depth // 2) % devices == 0
    columns = depth // 2 if hermitian else depth
    per_device = columns // devices
    me = lax.axis_index("row") * col_count + lax.axis_index("col")

    reciprocal = 1.0 / permittivity
    regions = permittivity.shape[0]
    one_hot = (region[..., None] == lax.iota(jnp.int32, regions)).astype(BF16)
    first = rounded(reciprocal)
    rest = reciprocal - first
    second = rounded(rest)
    parts = (first, second, rest - second)
    cell_scale = None
    for part in parts:
        term = jnp.einsum(
            "...k,k->...", one_hot, part.astype(BF16), preferred_element_type=F32
        )
        cell_scale = term if cell_scale is None else cell_scale + term
    electric = displacement.astype(F32) * cell_scale[None]

    cos_z, sin_z = phase_table(columns, depth, depth)
    if hermitian:
        parity = (1 - 2 * (lax.iota(jnp.int32, depth) % 2)).astype(F32)
        sin_part = jnp.concatenate([parity[None, :], -sin_z[1:]], axis=0)
    else:
        sin_part = -sin_z
    table_z = jnp.stack(
        [cos_z.reshape(devices, per_device, depth), sin_part.reshape(devices, per_device, depth)],
        axis=1,
    ).reshape(2 * columns, depth)
    z_high, z_low = split_parts(table_z)
    rows = members * local_x * local_y

    spectrum = jnp.einsum(
        "kz,rz->kr", table_z, electric.reshape(rows, depth), precision=lax.Precision.HIGH
    )
    spectrum = spectrum.astype(BF16).reshape(
        devices, 2, per_device, members, local_x, local_y
    )
    gathered = lax.all_to_all(
        spectrum, ("row", "col"), split_axis=0, concat_axis=0, tiled=True
    )
    gathered = gathered.reshape(
        row_count, col_count, 2, per_device, members, local_x, local_y
    )
    gathered = jnp.transpose(gathered, (4, 2, 3, 0, 5, 1, 6)).reshape(
        members, 2, per_device, span_x, width_y
    )

    cos_y, sin_y = phase_table(width_y, width_y, width_y)
    cos_y_parts = split_parts(cos_y)
    sin_y_parts = split_parts(sin_y)
    spec_y = "yk,cpjxy->cpjxk"
    by_cos = mat(cos_y_parts, gathered, spec_y)
    by_sin = mat(sin_y_parts, gathered, spec_y)
    y_real = by_cos[:, 0] + by_sin[:, 1]
    y_imag = by_cos[:, 1] - by_sin[:, 0]

    kernel = jnp.asarray(x_kernel(span_x))
    wave_y = wavenumber(lax.iota(jnp.int32, width_y), width_y)
    wave_z = wavenumber(me * per_device + lax.iota(jnp.int32, per_device), depth)

    def inverse_y(b_real, b_imag):
        stacked = jnp.stack([b_real, b_imag], axis=1).astype(BF16)
        by_cos = mat(cos_y_parts, stacked, spec_y)
        by_sin = mat(sin_y_parts, stacked, spec_y)
        scale = 1.0 / width_y
        out_real = (by_cos[:, 0] - by_sin[:, 1]) * scale
        out_imag = (by_cos[:, 1] + by_sin[:, 0]) * scale
        return rounded(out_real), rounded(out_imag)

    b_real, b_imag = curl_update(rounded(y_real), rounded(y_imag), wave_y, wave_z, kernel)
    back_real, back_imag = inverse_y(rounded(b_real), rounded(b_imag))

    if hermitian:
        plane_real = by_cos[:, :, 0]
        plane_imag = -by_sin[:, :, 0]
        pb_real, pb_imag = curl_update(
            rounded(plane_real), rounded(plane_imag), wave_y, jnp.zeros((2,), F32), kernel
        )
        pback_real, _ = inverse_y(rounded(pb_real), rounded(pb_imag))
        is_first = me == 0
        fixed_real = jnp.where(is_first, pback_real[:, 0], back_real[:, 0])
        fixed_imag = jnp.where(is_first, pback_real[:, 1], back_imag[:, 0])
        back_real = jnp.concatenate([fixed_real[:, None], back_real[:, 1:]], axis=1)
        back_imag = jnp.concatenate([fixed_imag[:, None], back_imag[:, 1:]], axis=1)

    outgoing = jnp.stack([back_real, back_imag], axis=1).astype(BF16)
    outgoing = outgoing.reshape(
        members, 2, per_device, row_count, local_x, col_count, local_y
    )
    outgoing = jnp.transpose(outgoing, (3, 5, 1, 2, 0, 4, 6)).reshape(
        devices, 2, per_device, members, local_x, local_y
    )
    returned = lax.all_to_all(
        outgoing, ("row", "col"), split_axis=0, concat_axis=0, tiled=True
    )
    returned = returned.reshape(2 * columns, rows)

    weight = np.full((devices, 2, per_device), 1.0 / depth, np.float32)
    if hermitian:
        weight[:] = 2.0 / depth
        weight[0, :, 0] = 1.0 / depth
    weight = jnp.asarray(weight.reshape(2 * columns, 1))
    weighted = (returned.astype(F32) * weight).astype(BF16)
    spec_back = "kr,kz->rz"
    field = jnp.einsum(spec_back, weighted, z_high, preferred_element_type=F32) + jnp.einsum(
        spec_back, weighted, z_low, preferred_element_type=F32
    )
    field = field.reshape(members, local_x, local_y, depth)
    return (magnetic.astype(F32) + field).astype(BF16)


def solution(mesh):
    in_specs = (
        P(None, "row", "col", None),
        P(None, "row", "col", None),
        P("row", "col", None),
        P(),
    )
    out_specs = P(None, "row", "col", None)
    return jax.shard_map(
        on_device, mesh=mesh, in_specs=in_specs, out_specs=out_specs, check_vma=False
    )
```

```python
import math

import numpy as np
import jax
import jax.numpy as jnp
from jax import lax
from jax.sharding import PartitionSpec as P

TIME_STEP = 0.5
F32 = jnp.float32
BF16 = jnp.bfloat16


def wavenumber(wave_index, length):
    signed = jnp.where(2 * wave_index < length, wave_index, wave_index - length)
    return jnp.where(
        2 * wave_index == length, 0.0, signed.astype(F32) * (2.0 * math.pi / length)
    )


def rounded(values):
    return lax.reduce_precision(values, exponent_bits=8, mantissa_bits=7)


def split_parts(values):
    high = rounded(values)
    low = values - high
    return high.astype(BF16), low.astype(BF16)


def direct_phase(rows, cols, length, step):
    product = (lax.iota(jnp.int32, rows)[:, None] * step) * lax.iota(jnp.int32, cols)[None, :]
    angle = (product % length).astype(F32) * (2.0 * math.pi / length)
    return jnp.cos(angle), jnp.sin(angle)


def phase_table(rows, cols, length):
    block = 32
    if rows % block or rows <= block:
        return direct_phase(rows, cols, length, 1)
    outer_cos, outer_sin = direct_phase(rows // block, cols, length, block)
    inner_cos, inner_sin = direct_phase(block, cols, length, 1)
    outer_cos, outer_sin = outer_cos[:, None], outer_sin[:, None]
    inner_cos, inner_sin = inner_cos[None], inner_sin[None]
    cosine = outer_cos * inner_cos - outer_sin * inner_sin
    sine = outer_sin * inner_cos + outer_cos * inner_sin
    return cosine.reshape(rows, cols), sine.reshape(rows, cols)


def x_kernel(span_x):
    index = np.arange(span_x)
    signed = np.where(2 * index < span_x, index, index - span_x)
    qx = np.where(2 * index == span_x, 0.0, signed * (2.0 * math.pi / span_x))
    shift = np.arange(span_x)
    phases = np.exp(2j * math.pi * np.outer(shift, index) / span_x)
    taps = (phases * (-0.5j * qx)[None, :]).sum(axis=1) / span_x
    taps = taps.real
    matrix = taps[(shift[:, None] - shift[None, :]) % span_x]
    return matrix.astype(np.float32)


def mat(table_parts, operand, spec):
    total = None
    for part in table_parts:
        term = jnp.einsum(spec, part, operand, preferred_element_type=F32)
        total = term if total is None else total + term
    return total


def curl_update(y_real, y_imag, wave_y, wave_z, kernel):
    half = TIME_STEP

    def along_x(values):
        return jnp.einsum("ab,jbk->jak", kernel, values, precision=lax.Precision.HIGHEST)

    xr, yr, zr = y_real[0], y_real[1], y_real[2]
    xi, yi, zi = y_imag[0], y_imag[1], y_imag[2]
    qy = half * wave_y
    qz = half * wave_z[:, None, None]
    gyr, gyi = along_x(yr), along_x(yi)
    gzr, gzi = along_x(zr), along_x(zi)
    b_real = jnp.stack([qy * zi - qz * yi, qz * xi - gzr, gyr - qy * xi])
    b_imag = jnp.stack([qz * yr - qy * zr, -qz * xr - gzi, gyi + qy * xr])
    return b_real, b_imag


def on_device(displacement, magnetic, region, permittivity):
    row_count = lax.axis_size("row")
    col_count = lax.axis_size("col")
    devices = row_count * col_count
    members, local_x, local_y, depth = displacement.shape
    width_y = local_y * col_count
    span_x = local_x * row_count
    hermitian = (depth // 2) % devices == 0
    columns = depth // 2 if hermitian else depth
    per_device = columns // devices
    me = lax.axis_index("row") * col_count + lax.axis_index("col")

    reciprocal = 1.0 / permittivity
    regions = permittivity.shape[0]
    one_hot = (region[..., None] == lax.iota(jnp.int32, regions)).astype(BF16)
    first = rounded(reciprocal)
    rest = reciprocal - first
    second = rounded(rest)
    parts = (first, second, rest - second)
    cell_scale = None
    for part in parts:
        term = jnp.einsum(
            "...k,k->...", one_hot, part.astype(BF16), preferred_element_type=F32
        )
        cell_scale = term if cell_scale is None else cell_scale + term
    electric = displacement.astype(F32) * cell_scale[None]

    cos_z, sin_z = phase_table(columns, depth, depth)
    if hermitian:
        parity = (1 - 2 * (lax.iota(jnp.int32, depth) % 2)).astype(F32)
        sin_part = jnp.concatenate([parity[None, :], -sin_z[1:]], axis=0)
    else:
        sin_part = -sin_z
    table_z = jnp.stack(
        [cos_z.reshape(devices, per_device, depth), sin_part.reshape(devices, per_device, depth)],
        axis=1,
    ).reshape(2 * columns, depth)
    z_high, z_low = split_parts(table_z)
    rows = members * local_x * local_y

    e_high, e_low = split_parts(electric.reshape(rows, depth))
    spec_z = "dpjz,cyz->dpcjy"
    blocks = (devices, 2, per_device, depth)
    lines = (members * local_x, local_y, depth)
    z_high4, z_low4 = z_high.reshape(blocks), z_low.reshape(blocks)
    e_high, e_low = e_high.reshape(lines), e_low.reshape(lines)
    spectrum = (
        jnp.einsum(spec_z, z_high4, e_high, preferred_element_type=F32)
        + jnp.einsum(spec_z, z_high4, e_low, preferred_element_type=F32)
        + jnp.einsum(spec_z, z_low4, e_high, preferred_element_type=F32)
    )
    spectrum = spectrum.astype(BF16)
    gathered = lax.all_to_all(
        spectrum, ("row", "col"), split_axis=0, concat_axis=0, tiled=True
    )
    gathered = gathered.reshape(
        row_count, col_count, 2, members, local_x, per_device, local_y
    )
    gathered = jnp.transpose(gathered, (3, 2, 5, 0, 4, 1, 6)).reshape(
        members, 2, per_device, span_x, width_y
    )

    cos_y, sin_y = phase_table(width_y, width_y, width_y)
    cos_y_parts = split_parts(cos_y)
    sin_y_parts = split_parts(sin_y)
    spec_y = "yk,cpjxy->cpjxk"
    by_cos = mat(cos_y_parts, gathered, spec_y)
    by_sin = mat(sin_y_parts, gathered, spec_y)
    y_real = by_cos[:, 0] + by_sin[:, 1]
    y_imag = by_cos[:, 1] - by_sin[:, 0]

    kernel = jnp.asarray(x_kernel(span_x))
    wave_y = wavenumber(lax.iota(jnp.int32, width_y), width_y)
    wave_z = wavenumber(me * per_device + lax.iota(jnp.int32, per_device), depth)

    def inverse_y(b_real, b_imag):
        stacked = jnp.stack([b_real, b_imag], axis=1).astype(BF16)
        by_cos = mat(cos_y_parts, stacked, spec_y)
        by_sin = mat(sin_y_parts, stacked, spec_y)
        scale = 1.0 / width_y
        out_real = (by_cos[:, 0] - by_sin[:, 1]) * scale
        out_imag = (by_cos[:, 1] + by_sin[:, 0]) * scale
        return rounded(out_real), rounded(out_imag)

    b_real, b_imag = curl_update(rounded(y_real), rounded(y_imag), wave_y, wave_z, kernel)
    back_real, back_imag = inverse_y(rounded(b_real), rounded(b_imag))

    if hermitian:
        plane_real = by_cos[:, :, 0]
        plane_imag = -by_sin[:, :, 0]
        pb_real, pb_imag = curl_update(
            rounded(plane_real), rounded(plane_imag), wave_y, jnp.zeros((2,), F32), kernel
        )
        pback_real, _ = inverse_y(rounded(pb_real), rounded(pb_imag))
        is_first = me == 0
        fixed_real = jnp.where(is_first, pback_real[:, 0], back_real[:, 0])
        fixed_imag = jnp.where(is_first, pback_real[:, 1], back_imag[:, 0])
        back_real = jnp.concatenate([fixed_real[:, None], back_real[:, 1:]], axis=1)
        back_imag = jnp.concatenate([fixed_imag[:, None], back_imag[:, 1:]], axis=1)

    outgoing = jnp.stack([back_real, back_imag], axis=1).astype(BF16)
    outgoing = outgoing.reshape(
        members, 2, per_device, row_count, local_x, col_count, local_y
    )
    outgoing = jnp.transpose(outgoing, (3, 5, 1, 2, 0, 4, 6)).reshape(
        devices, 2, per_device, members, local_x, local_y
    )
    returned = lax.all_to_all(
        outgoing, ("row", "col"), split_axis=0, concat_axis=0, tiled=True
    )
    returned = returned.reshape(2 * columns, rows)

    weight = np.full((devices, 2, per_device), 1.0 / depth, np.float32)
    if hermitian:
        weight[:] = 2.0 / depth
        weight[0, :, 0] = 1.0 / depth
    weight = jnp.asarray(weight.reshape(2 * columns, 1))
    weighted = (returned.astype(F32) * weight).astype(BF16)
    spec_back = "kr,kz->rz"
    field = jnp.einsum(spec_back, weighted, z_high, preferred_element_type=F32) + jnp.einsum(
        spec_back, weighted, z_low, preferred_element_type=F32
    )
    field = field.reshape(members, local_x, local_y, depth)
    return (magnetic.astype(F32) + field).astype(BF16)


def solution(mesh):
    in_specs = (
        P(None, "row", "col", None),
        P(None, "row", "col", None),
        P("row", "col", None),
        P(),
    )
    out_specs = P(None, "row", "col", None)
    return jax.shard_map(
        on_device, mesh=mesh, in_specs=in_specs, out_specs=out_specs, check_vma=False
    )
```

```python
import math

import numpy as np
import jax
import jax.numpy as jnp
from jax import lax
from jax.sharding import PartitionSpec as P

TIME_STEP = 0.5
F32 = jnp.float32
BF16 = jnp.bfloat16


def wavenumber(wave_index, length):
    signed = jnp.where(2 * wave_index < length, wave_index, wave_index - length)
    return jnp.where(
        2 * wave_index == length, 0.0, signed.astype(F32) * (2.0 * math.pi / length)
    )


def rounded(values):
    return lax.reduce_precision(values, exponent_bits=8, mantissa_bits=7)


def split_parts(values):
    high = rounded(values)
    low = values - high
    return high.astype(BF16), low.astype(BF16)


def direct_phase(rows, cols, length, step):
    product = (lax.iota(jnp.int32, rows)[:, None] * step) * lax.iota(jnp.int32, cols)[None, :]
    angle = (product % length).astype(F32) * (2.0 * math.pi / length)
    return jnp.cos(angle), jnp.sin(angle)


def phase_table(rows, cols, length):
    block = 32
    if rows % block or rows <= block:
        return direct_phase(rows, cols, length, 1)
    outer_cos, outer_sin = direct_phase(rows // block, cols, length, block)
    inner_cos, inner_sin = direct_phase(block, cols, length, 1)
    outer_cos, outer_sin = outer_cos[:, None], outer_sin[:, None]
    inner_cos, inner_sin = inner_cos[None], inner_sin[None]
    cosine = outer_cos * inner_cos - outer_sin * inner_sin
    sine = outer_sin * inner_cos + outer_cos * inner_sin
    return cosine.reshape(rows, cols), sine.reshape(rows, cols)


def x_kernel(span_x):
    index = np.arange(span_x)
    signed = np.where(2 * index < span_x, index, index - span_x)
    qx = np.where(2 * index == span_x, 0.0, signed * (2.0 * math.pi / span_x))
    shift = np.arange(span_x)
    phases = np.exp(2j * math.pi * np.outer(shift, index) / span_x)
    taps = (phases * (-0.5j * qx)[None, :]).sum(axis=1) / span_x
    taps = taps.real
    matrix = taps[(shift[:, None] - shift[None, :]) % span_x]
    return matrix.astype(np.float32)


def mat(table_parts, operand, spec):
    total = None
    for part in table_parts:
        term = jnp.einsum(spec, part, operand, preferred_element_type=F32)
        total = term if total is None else total + term
    return total


def curl_update(y_real, y_imag, wave_y, wave_z, kernel):
    half = TIME_STEP

    def along_x(values):
        return jnp.einsum("ab,jbk->jak", kernel, values, precision=lax.Precision.HIGHEST)

    xr, yr, zr = y_real[0], y_real[1], y_real[2]
    xi, yi, zi = y_imag[0], y_imag[1], y_imag[2]
    qy = half * wave_y
    qz = half * wave_z[:, None, None]
    gyr, gyi = along_x(yr), along_x(yi)
    gzr, gzi = along_x(zr), along_x(zi)
    b_real = jnp.stack([qy * zi - qz * yi, qz * xi - gzr, gyr - qy * xi])
    b_imag = jnp.stack([qz * yr - qy * zr, -qz * xr - gzi, gyi + qy * xr])
    return b_real, b_imag


def on_device(displacement, magnetic, region, permittivity):
    row_count = lax.axis_size("row")
    col_count = lax.axis_size("col")
    devices = row_count * col_count
    members, local_x, local_y, depth = displacement.shape
    width_y = local_y * col_count
    span_x = local_x * row_count
    hermitian = (depth // 2) % devices == 0
    columns = depth // 2 if hermitian else depth
    per_device = columns // devices
    me = lax.axis_index("row") * col_count + lax.axis_index("col")

    reciprocal = 1.0 / permittivity
    regions = permittivity.shape[0]
    first = rounded(reciprocal)
    rest = reciprocal - first
    second = rounded(rest)
    parts = jnp.concatenate([first, second, rest - second]).astype(BF16)
    slots = lax.iota(jnp.int32, 3 * regions) % regions
    one_hot = (region[..., None] == slots).astype(BF16)
    cell_scale = jnp.einsum("...k,k->...", one_hot, parts, preferred_element_type=F32)
    electric = displacement.astype(F32) * cell_scale[None]

    cos_z, sin_z = phase_table(columns, depth, depth)
    if hermitian:
        parity = (1 - 2 * (lax.iota(jnp.int32, depth) % 2)).astype(F32)
        sin_part = jnp.concatenate([parity[None, :], -sin_z[1:]], axis=0)
    else:
        sin_part = -sin_z
    table_z = jnp.stack(
        [cos_z.reshape(devices, per_device, depth), sin_part.reshape(devices, per_device, depth)],
        axis=1,
    ).reshape(2 * columns, depth)
    z_high, z_low = split_parts(table_z)
    rows = members * local_x * local_y

    e_high, e_low = split_parts(electric.reshape(rows, depth))
    spec_z = "dpjz,cyz->dcpjy"
    blocks = (devices, 2, per_device, depth)
    lines = (members * local_x, local_y, depth)
    z_high4, z_low4 = z_high.reshape(blocks), z_low.reshape(blocks)
    e_high, e_low = e_high.reshape(lines), e_low.reshape(lines)
    spectrum = (
        jnp.einsum(spec_z, z_high4, e_high, preferred_element_type=F32)
        + jnp.einsum(spec_z, z_high4, e_low, preferred_element_type=F32)
        + jnp.einsum(spec_z, z_low4, e_high, preferred_element_type=F32)
    )
    spectrum = spectrum.astype(BF16)
    gathered = lax.all_to_all(
        spectrum, ("row", "col"), split_axis=0, concat_axis=0, tiled=True
    )
    gathered = gathered.reshape(
        row_count, col_count, members, local_x, 2, per_device, local_y
    )
    gathered = jnp.transpose(gathered, (2, 4, 5, 0, 3, 1, 6)).reshape(
        members, 2, per_device, span_x, width_y
    )

    cos_y, sin_y = phase_table(width_y, width_y, width_y)
    cos_y_parts = split_parts(cos_y)
    sin_y_parts = split_parts(sin_y)
    spec_y = "yk,cpjxy->cpjxk"
    by_cos = mat(cos_y_parts, gathered, spec_y)
    by_sin = mat(sin_y_parts, gathered, spec_y)
    y_real = by_cos[:, 0] + by_sin[:, 1]
    y_imag = by_cos[:, 1] - by_sin[:, 0]

    kernel = jnp.asarray(x_kernel(span_x))
    wave_y = wavenumber(lax.iota(jnp.int32, width_y), width_y)
    wave_z = wavenumber(me * per_device + lax.iota(jnp.int32, per_device), depth)

    def inverse_y(b_real, b_imag):
        stacked = jnp.stack([b_real, b_imag], axis=1).astype(BF16)
        by_cos = mat(cos_y_parts, stacked, spec_y)
        by_sin = mat(sin_y_parts, stacked, spec_y)
        scale = 1.0 / width_y
        out_real = (by_cos[:, 0] - by_sin[:, 1]) * scale
        out_imag = (by_cos[:, 1] + by_sin[:, 0]) * scale
        return rounded(out_real), rounded(out_imag)

    b_real, b_imag = curl_update(rounded(y_real), rounded(y_imag), wave_y, wave_z, kernel)
    back_real, back_imag = inverse_y(rounded(b_real), rounded(b_imag))

    if hermitian:
        plane_real = by_cos[:, :, 0]
        plane_imag = -by_sin[:, :, 0]
        pb_real, pb_imag = curl_update(
            rounded(plane_real), rounded(plane_imag), wave_y, jnp.zeros((2,), F32), kernel
        )
        pback_real, _ = inverse_y(rounded(pb_real), rounded(pb_imag))
        is_first = me == 0
        fixed_real = jnp.where(is_first, pback_real[:, 0], back_real[:, 0])
        fixed_imag = jnp.where(is_first, pback_real[:, 1], back_imag[:, 0])
        back_real = jnp.concatenate([fixed_real[:, None], back_real[:, 1:]], axis=1)
        back_imag = jnp.concatenate([fixed_imag[:, None], back_imag[:, 1:]], axis=1)

    outgoing = jnp.stack([back_real, back_imag], axis=1).astype(BF16)
    outgoing = outgoing.reshape(
        members, 2, per_device, row_count, local_x, col_count, local_y
    )
    outgoing = jnp.transpose(outgoing, (3, 5, 1, 2, 0, 4, 6)).reshape(
        devices, 2, per_device, members, local_x, local_y
    )
    returned = lax.all_to_all(
        outgoing, ("row", "col"), split_axis=0, concat_axis=0, tiled=True
    )
    returned = returned.reshape(2 * columns, rows)

    weight = np.full((devices, 2, per_device), 1.0 / depth, np.float32)
    if hermitian:
        weight[:] = 2.0 / depth
        weight[0, :, 0] = 1.0 / depth
    weight = jnp.asarray(weight.reshape(2 * columns, 1))
    weighted = (returned.astype(F32) * weight).astype(BF16)
    spec_back = "kr,kz->rz"
    field = jnp.einsum(spec_back, weighted, z_high, preferred_element_type=F32) + jnp.einsum(
        spec_back, weighted, z_low, preferred_element_type=F32
    )
    field = field.reshape(members, local_x, local_y, depth)
    return (magnetic.astype(F32) + field).astype(BF16)


def solution(mesh):
    in_specs = (
        P(None, "row", "col", None),
        P(None, "row", "col", None),
        P("row", "col", None),
        P(),
    )
    out_specs = P(None, "row", "col", None)
    return jax.shard_map(
        on_device, mesh=mesh, in_specs=in_specs, out_specs=out_specs, check_vma=False
    )
```

```python
import math

import numpy as np
import jax
import jax.numpy as jnp
from jax import lax
from jax.sharding import PartitionSpec as P

TIME_STEP = 0.5
F32 = jnp.float32
BF16 = jnp.bfloat16


def wavenumber(wave_index, length):
    signed = jnp.where(2 * wave_index < length, wave_index, wave_index - length)
    return jnp.where(
        2 * wave_index == length, 0.0, signed.astype(F32) * (2.0 * math.pi / length)
    )


def rounded(values):
    return lax.reduce_precision(values, exponent_bits=8, mantissa_bits=7)


def split_parts(values):
    high = rounded(values)
    low = values - high
    return high.astype(BF16), low.astype(BF16)


def direct_phase(rows, cols, length, step):
    product = (lax.iota(jnp.int32, rows)[:, None] * step) * lax.iota(jnp.int32, cols)[None, :]
    angle = (product % length).astype(F32) * (2.0 * math.pi / length)
    return jnp.cos(angle), jnp.sin(angle)


def phase_table(rows, cols, length):
    block = 32
    if rows % block or rows <= block:
        return direct_phase(rows, cols, length, 1)
    outer_cos, outer_sin = direct_phase(rows // block, cols, length, block)
    inner_cos, inner_sin = direct_phase(block, cols, length, 1)
    outer_cos, outer_sin = outer_cos[:, None], outer_sin[:, None]
    inner_cos, inner_sin = inner_cos[None], inner_sin[None]
    cosine = outer_cos * inner_cos - outer_sin * inner_sin
    sine = outer_sin * inner_cos + outer_cos * inner_sin
    return cosine.reshape(rows, cols), sine.reshape(rows, cols)


def x_kernel(span_x):
    index = np.arange(span_x)
    signed = np.where(2 * index < span_x, index, index - span_x)
    qx = np.where(2 * index == span_x, 0.0, signed * (2.0 * math.pi / span_x))
    shift = np.arange(span_x)
    phases = np.exp(2j * math.pi * np.outer(shift, index) / span_x)
    taps = (phases * (-0.5j * qx)[None, :]).sum(axis=1) / span_x
    taps = taps.real
    matrix = taps[(shift[:, None] - shift[None, :]) % span_x]
    return matrix.astype(np.float32)


def mat(table_parts, operand, spec):
    total = None
    for part in table_parts:
        term = jnp.einsum(spec, part, operand, preferred_element_type=F32)
        total = term if total is None else total + term
    return total


def curl_update(y_real, y_imag, wave_y, wave_z, kernel):
    half = TIME_STEP

    def along_x(values):
        return jnp.einsum("ab,jbk->jak", kernel, values, precision=lax.Precision.HIGHEST)

    xr, yr, zr = y_real[0], y_real[1], y_real[2]
    xi, yi, zi = y_imag[0], y_imag[1], y_imag[2]
    qy = half * wave_y
    qz = half * wave_z[:, None, None]
    gyr, gyi = along_x(yr), along_x(yi)
    gzr, gzi = along_x(zr), along_x(zi)
    b_real = jnp.stack([qy * zi - qz * yi, qz * xi - gzr, gyr - qy * xi])
    b_imag = jnp.stack([qz * yr - qy * zr, -qz * xr - gzi, gyi + qy * xr])
    return b_real, b_imag


def on_device(displacement, magnetic, region, permittivity):
    row_count = lax.axis_size("row")
    col_count = lax.axis_size("col")
    devices = row_count * col_count
    members, local_x, local_y, depth = displacement.shape
    width_y = local_y * col_count
    span_x = local_x * row_count
    hermitian = (depth // 2) % devices == 0
    columns = depth // 2 if hermitian else depth
    per_device = columns // devices
    me = lax.axis_index("row") * col_count + lax.axis_index("col")

    reciprocal = 1.0 / permittivity
    regions = permittivity.shape[0]
    first = rounded(reciprocal)
    rest = reciprocal - first
    second = rounded(rest)
    parts = jnp.concatenate([first, second, rest - second]).astype(BF16)
    slots = lax.iota(jnp.int32, 3 * regions) % regions
    one_hot = (region[..., None] == slots).astype(BF16)
    cell_scale = jnp.einsum("...k,k->...", one_hot, parts, preferred_element_type=F32)
    electric = displacement.astype(F32) * cell_scale[None]

    cos_z, sin_z = phase_table(columns, depth, depth)
    if hermitian:
        parity = (1 - 2 * (lax.iota(jnp.int32, depth) % 2)).astype(F32)
        first_row = (lax.iota(jnp.int32, columns) == 0)[:, None]
        sin_part = jnp.where(first_row, parity[None, :], -sin_z)
    else:
        sin_part = -sin_z
    table_z = jnp.stack(
        [cos_z.reshape(devices, per_device, depth), sin_part.reshape(devices, per_device, depth)],
        axis=1,
    ).reshape(2 * columns, depth)
    z_high, z_low = split_parts(table_z)
    rows = members * local_x * local_y

    e_high, e_low = split_parts(electric.reshape(rows, depth))
    spec_z = "dpjz,cyz->dcpjy"
    blocks = (devices, 2, per_device, depth)
    lines = (members * local_x, local_y, depth)
    z_high4, z_low4 = z_high.reshape(blocks), z_low.reshape(blocks)
    e_high, e_low = e_high.reshape(lines), e_low.reshape(lines)
    spectrum = (
        jnp.einsum(spec_z, z_high4, e_high, preferred_element_type=F32)
        + jnp.einsum(spec_z, z_high4, e_low, preferred_element_type=F32)
        + jnp.einsum(spec_z, z_low4, e_high, preferred_element_type=F32)
    )
    spectrum = spectrum.astype(BF16)
    gathered = lax.all_to_all(
        spectrum, ("row", "col"), split_axis=0, concat_axis=0, tiled=True
    )
    gathered = gathered.reshape(
        row_count, col_count, members, local_x, 2, per_device, local_y
    )
    gathered = jnp.transpose(gathered, (2, 4, 5, 0, 3, 1, 6)).reshape(
        members, 2, per_device, span_x, width_y
    )

    cos_y, sin_y = phase_table(width_y, width_y, width_y)
    cos_y_parts = split_parts(cos_y)
    sin_y_parts = split_parts(sin_y)
    spec_y = "yk,cpjxy->cpjxk"
    by_cos = mat(cos_y_parts, gathered, spec_y)
    by_sin = mat(sin_y_parts, gathered, spec_y)
    y_real = by_cos[:, 0] + by_sin[:, 1]
    y_imag = by_cos[:, 1] - by_sin[:, 0]

    kernel = jnp.asarray(x_kernel(span_x))
    wave_y = wavenumber(lax.iota(jnp.int32, width_y), width_y)
    wave_z = wavenumber(me * per_device + lax.iota(jnp.int32, per_device), depth)

    def inverse_y(b_real, b_imag):
        stacked = jnp.stack([b_real, b_imag], axis=1).astype(BF16)
        by_cos = mat(cos_y_parts, stacked, spec_y)
        by_sin = mat(sin_y_parts, stacked, spec_y)
        scale = 1.0 / width_y
        out_real = (by_cos[:, 0] - by_sin[:, 1]) * scale
        out_imag = (by_cos[:, 1] + by_sin[:, 0]) * scale
        return rounded(out_real), rounded(out_imag)

    b_real, b_imag = curl_update(rounded(y_real), rounded(y_imag), wave_y, wave_z, kernel)
    back_real, back_imag = inverse_y(rounded(b_real), rounded(b_imag))

    if hermitian:
        plane_real = by_cos[:, :, 0]
        plane_imag = -by_sin[:, :, 0]
        pb_real, pb_imag = curl_update(
            rounded(plane_real), rounded(plane_imag), wave_y, jnp.zeros((2,), F32), kernel
        )
        pback_real, _ = inverse_y(rounded(pb_real), rounded(pb_imag))
        is_first = me == 0
        packed = ((lax.iota(jnp.int32, per_device) == 0) & is_first)[None, :, None, None]
        back_real = jnp.where(packed, pback_real[:, 0:1], back_real)
        back_imag = jnp.where(packed, pback_real[:, 1:2], back_imag)

    outgoing = jnp.stack([back_real, back_imag], axis=1).astype(BF16)
    outgoing = outgoing.reshape(
        members, 2, per_device, row_count, local_x, col_count, local_y
    )
    outgoing = jnp.transpose(outgoing, (3, 5, 1, 2, 0, 4, 6)).reshape(
        devices, 2, per_device, members, local_x, local_y
    )
    returned = lax.all_to_all(
        outgoing, ("row", "col"), split_axis=0, concat_axis=0, tiled=True
    )
    returned = returned.reshape(2 * columns, rows)

    weight = np.full((devices, 2, per_device), 1.0 / depth, np.float32)
    if hermitian:
        weight[:] = 2.0 / depth
        weight[0, :, 0] = 1.0 / depth
    weight = jnp.asarray(weight.reshape(2 * columns, 1))
    weighted = (returned.astype(F32) * weight).astype(BF16)
    spec_back = "kr,kz->rz"
    field = jnp.einsum(spec_back, weighted, z_high, preferred_element_type=F32) + jnp.einsum(
        spec_back, weighted, z_low, preferred_element_type=F32
    )
    field = field.reshape(members, local_x, local_y, depth)
    return (magnetic.astype(F32) + field).astype(BF16)


def solution(mesh):
    in_specs = (
        P(None, "row", "col", None),
        P(None, "row", "col", None),
        P("row", "col", None),
        P(),
    )
    out_specs = P(None, "row", "col", None)
    return jax.shard_map(
        on_device, mesh=mesh, in_specs=in_specs, out_specs=out_specs, check_vma=False
    )
```

```python
import math

import numpy as np
import jax
import jax.numpy as jnp
from jax import lax
from jax.sharding import PartitionSpec as P

TIME_STEP = 0.5
F32 = jnp.float32
BF16 = jnp.bfloat16


def wavenumber(wave_index, length):
    signed = jnp.where(2 * wave_index < length, wave_index, wave_index - length)
    return jnp.where(
        2 * wave_index == length, 0.0, signed.astype(F32) * (2.0 * math.pi / length)
    )


def rounded(values):
    return lax.reduce_precision(values, exponent_bits=8, mantissa_bits=7)


def split_parts(values):
    high = rounded(values)
    low = values - high
    return high.astype(BF16), low.astype(BF16)


def direct_phase(rows, cols, length, step):
    product = (lax.iota(jnp.int32, rows)[:, None] * step) * lax.iota(jnp.int32, cols)[None, :]
    angle = (product % length).astype(F32) * (2.0 * math.pi / length)
    return jnp.cos(angle), jnp.sin(angle)


def phase_table(rows, cols, length):
    block = 32
    if rows % block or rows <= block:
        return direct_phase(rows, cols, length, 1)
    outer_cos, outer_sin = direct_phase(rows // block, cols, length, block)
    inner_cos, inner_sin = direct_phase(block, cols, length, 1)
    outer_cos, outer_sin = outer_cos[:, None], outer_sin[:, None]
    inner_cos, inner_sin = inner_cos[None], inner_sin[None]
    cosine = outer_cos * inner_cos - outer_sin * inner_sin
    sine = outer_sin * inner_cos + outer_cos * inner_sin
    return cosine.reshape(rows, cols), sine.reshape(rows, cols)


def x_kernel(span_x):
    index = np.arange(span_x)
    signed = np.where(2 * index < span_x, index, index - span_x)
    qx = np.where(2 * index == span_x, 0.0, signed * (2.0 * math.pi / span_x))
    shift = np.arange(span_x)
    phases = np.exp(2j * math.pi * np.outer(shift, index) / span_x)
    taps = (phases * (-0.5j * qx)[None, :]).sum(axis=1) / span_x
    taps = taps.real
    matrix = taps[(shift[:, None] - shift[None, :]) % span_x]
    return matrix.astype(np.float32)


def mat(table_parts, operand, spec):
    total = None
    for part in table_parts:
        term = jnp.einsum(spec, part, operand, preferred_element_type=F32)
        total = term if total is None else total + term
    return total


def curl_update(y_real, y_imag, wave_y, wave_z, kernel):
    half = TIME_STEP

    def along_x(values):
        return jnp.einsum("ab,jbk->jak", kernel, values, precision=lax.Precision.HIGHEST)

    xr, yr, zr = y_real[0], y_real[1], y_real[2]
    xi, yi, zi = y_imag[0], y_imag[1], y_imag[2]
    qy = half * wave_y
    qz = half * wave_z[:, None, None]
    gyr, gyi = along_x(yr), along_x(yi)
    gzr, gzi = along_x(zr), along_x(zi)
    b_real = jnp.stack([qy * zi - qz * yi, qz * xi - gzr, gyr - qy * xi])
    b_imag = jnp.stack([qz * yr - qy * zr, -qz * xr - gzi, gyi + qy * xr])
    return b_real, b_imag


def on_device(displacement, magnetic, region, permittivity):
    row_count = lax.axis_size("row")
    col_count = lax.axis_size("col")
    devices = row_count * col_count
    members, local_x, local_y, depth = displacement.shape
    width_y = local_y * col_count
    span_x = local_x * row_count
    hermitian = (depth // 2) % devices == 0
    columns = depth // 2 if hermitian else depth
    per_device = columns // devices
    me = lax.axis_index("row") * col_count + lax.axis_index("col")

    reciprocal = 1.0 / permittivity
    regions = permittivity.shape[0]
    first = rounded(reciprocal)
    rest = reciprocal - first
    second = rounded(rest)
    parts = jnp.concatenate([first, second, rest - second]).astype(BF16)
    slots = lax.iota(jnp.int32, 3 * regions) % regions
    one_hot = (region[None] == slots.reshape((-1,) + (1,) * region.ndim)).astype(BF16)
    cell_scale = jnp.einsum("k...,k->...", one_hot, parts, preferred_element_type=F32)
    electric = displacement.astype(F32) * cell_scale[None]

    cos_z, sin_z = phase_table(columns, depth, depth)
    if hermitian:
        parity = (1 - 2 * (lax.iota(jnp.int32, depth) % 2)).astype(F32)
        first_row = (lax.iota(jnp.int32, columns) == 0)[:, None]
        sin_part = jnp.where(first_row, parity[None, :], -sin_z)
    else:
        sin_part = -sin_z
    table_z = jnp.stack(
        [cos_z.reshape(devices, per_device, depth), sin_part.reshape(devices, per_device, depth)],
        axis=1,
    ).reshape(2 * columns, depth)
    z_high, z_low = split_parts(table_z)
    rows = members * local_x * local_y

    e_high, e_low = split_parts(electric.reshape(rows, depth))
    spec_z = "dpjz,cyz->dcpjy"
    blocks = (devices, 2, per_device, depth)
    lines = (members * local_x, local_y, depth)
    z_high4, z_low4 = z_high.reshape(blocks), z_low.reshape(blocks)
    e_high, e_low = e_high.reshape(lines), e_low.reshape(lines)
    spectrum = (
        jnp.einsum(spec_z, z_high4, e_high, preferred_element_type=F32)
        + jnp.einsum(spec_z, z_high4, e_low, preferred_element_type=F32)
        + jnp.einsum(spec_z, z_low4, e_high, preferred_element_type=F32)
    )
    spectrum = spectrum.astype(BF16)
    gathered = lax.all_to_all(
        spectrum, ("row", "col"), split_axis=0, concat_axis=0, tiled=True
    )
    gathered = gathered.reshape(
        row_count, col_count, members, local_x, 2, per_device, local_y
    )
    gathered = jnp.transpose(gathered, (2, 4, 5, 0, 3, 1, 6)).reshape(
        members, 2, per_device, span_x, width_y
    )

    cos_y, sin_y = phase_table(width_y, width_y, width_y)
    cos_y_parts = split_parts(cos_y)
    sin_y_parts = split_parts(sin_y)
    spec_y = "yk,cpjxy->cpjxk"
    by_cos = mat(cos_y_parts, gathered, spec_y)
    by_sin = mat(sin_y_parts, gathered, spec_y)
    y_real = by_cos[:, 0] + by_sin[:, 1]
    y_imag = by_cos[:, 1] - by_sin[:, 0]

    kernel = jnp.asarray(x_kernel(span_x))
    wave_y = wavenumber(lax.iota(jnp.int32, width_y), width_y)
    wave_z = wavenumber(me * per_device + lax.iota(jnp.int32, per_device), depth)

    def inverse_y(b_real, b_imag):
        stacked = jnp.stack([b_real, b_imag], axis=1).astype(BF16)
        by_cos = mat(cos_y_parts, stacked, spec_y)
        by_sin = mat(sin_y_parts, stacked, spec_y)
        scale = 1.0 / width_y
        out_real = (by_cos[:, 0] - by_sin[:, 1]) * scale
        out_imag = (by_cos[:, 1] + by_sin[:, 0]) * scale
        return rounded(out_real), rounded(out_imag)

    b_real, b_imag = curl_update(rounded(y_real), rounded(y_imag), wave_y, wave_z, kernel)
    back_real, back_imag = inverse_y(rounded(b_real), rounded(b_imag))

    if hermitian:
        plane_real = by_cos[:, :, 0]
        plane_imag = -by_sin[:, :, 0]
        pb_real, pb_imag = curl_update(
            rounded(plane_real), rounded(plane_imag), wave_y, jnp.zeros((2,), F32), kernel
        )
        pback_real, _ = inverse_y(rounded(pb_real), rounded(pb_imag))
        is_first = me == 0
        packed = ((lax.iota(jnp.int32, per_device) == 0) & is_first)[None, :, None, None]
        back_real = jnp.where(packed, pback_real[:, 0:1], back_real)
        back_imag = jnp.where(packed, pback_real[:, 1:2], back_imag)

    outgoing = jnp.stack([back_real, back_imag], axis=1).astype(BF16)
    outgoing = outgoing.reshape(
        members, 2, per_device, row_count, local_x, col_count, local_y
    )
    outgoing = jnp.transpose(outgoing, (3, 5, 1, 2, 0, 4, 6)).reshape(
        devices, 2, per_device, members, local_x, local_y
    )
    returned = lax.all_to_all(
        outgoing, ("row", "col"), split_axis=0, concat_axis=0, tiled=True
    )
    returned = returned.reshape(2 * columns, rows)

    weight = np.full((devices, 2, per_device), 1.0 / depth, np.float32)
    if hermitian:
        weight[:] = 2.0 / depth
        weight[0, :, 0] = 1.0 / depth
    weight = jnp.asarray(weight.reshape(2 * columns, 1))
    weighted = (returned.astype(F32) * weight).astype(BF16)
    spec_back = "kr,kz->rz"
    field = jnp.einsum(spec_back, weighted, z_high, preferred_element_type=F32) + jnp.einsum(
        spec_back, weighted, z_low, preferred_element_type=F32
    )
    field = field.reshape(members, local_x, local_y, depth)
    return (magnetic.astype(F32) + field).astype(BF16)


def solution(mesh):
    in_specs = (
        P(None, "row", "col", None),
        P(None, "row", "col", None),
        P("row", "col", None),
        P(),
    )
    out_specs = P(None, "row", "col", None)
    return jax.shard_map(
        on_device, mesh=mesh, in_specs=in_specs, out_specs=out_specs, check_vma=False
    )
```

```python
import math

import numpy as np
import jax
import jax.numpy as jnp
from jax import lax
from jax.sharding import PartitionSpec as P

TIME_STEP = 0.5
F32 = jnp.float32
BF16 = jnp.bfloat16


def wavenumber(wave_index, length):
    signed = jnp.where(2 * wave_index < length, wave_index, wave_index - length)
    return jnp.where(
        2 * wave_index == length, 0.0, signed.astype(F32) * (2.0 * math.pi / length)
    )


def rounded(values):
    return lax.reduce_precision(values, exponent_bits=8, mantissa_bits=7)


def split_parts(values):
    high = rounded(values)
    low = values - high
    return high.astype(BF16), low.astype(BF16)


def direct_phase(rows, cols, length, step):
    product = (lax.iota(jnp.int32, rows)[:, None] * step) * lax.iota(jnp.int32, cols)[None, :]
    angle = (product % length).astype(F32) * (2.0 * math.pi / length)
    return jnp.cos(angle), jnp.sin(angle)


def phase_table(rows, cols, length):
    block = 32
    if rows % block or rows <= block:
        return direct_phase(rows, cols, length, 1)
    outer_cos, outer_sin = direct_phase(rows // block, cols, length, block)
    inner_cos, inner_sin = direct_phase(block, cols, length, 1)
    outer_cos, outer_sin = outer_cos[:, None], outer_sin[:, None]
    inner_cos, inner_sin = inner_cos[None], inner_sin[None]
    cosine = outer_cos * inner_cos - outer_sin * inner_sin
    sine = outer_sin * inner_cos + outer_cos * inner_sin
    return cosine.reshape(rows, cols), sine.reshape(rows, cols)


def x_kernel(span_x):
    index = np.arange(span_x)
    signed = np.where(2 * index < span_x, index, index - span_x)
    qx = np.where(2 * index == span_x, 0.0, signed * (2.0 * math.pi / span_x))
    shift = np.arange(span_x)
    phases = np.exp(2j * math.pi * np.outer(shift, index) / span_x)
    taps = (phases * (-0.5j * qx)[None, :]).sum(axis=1) / span_x
    taps = taps.real
    matrix = taps[(shift[:, None] - shift[None, :]) % span_x]
    return matrix.astype(np.float32)


def mat(table_parts, operand, spec):
    total = None
    for part in table_parts:
        term = jnp.einsum(spec, part, operand, preferred_element_type=F32)
        total = term if total is None else total + term
    return total


def curl_update(y_real, y_imag, wave_y, wave_z, kernel):
    half = TIME_STEP

    def along_x(values):
        return jnp.einsum("ab,jbk->jak", kernel, values, precision=lax.Precision.HIGHEST)

    xr, yr, zr = y_real[0], y_real[1], y_real[2]
    xi, yi, zi = y_imag[0], y_imag[1], y_imag[2]
    qy = half * wave_y
    qz = half * wave_z[:, None, None]
    gyr, gyi = along_x(yr), along_x(yi)
    gzr, gzi = along_x(zr), along_x(zi)
    b_real = jnp.stack([qy * zi - qz * yi, qz * xi - gzr, gyr - qy * xi])
    b_imag = jnp.stack([qz * yr - qy * zr, -qz * xr - gzi, gyi + qy * xr])
    return b_real, b_imag


def on_device(displacement, magnetic, region, permittivity):
    row_count = lax.axis_size("row")
    col_count = lax.axis_size("col")
    devices = row_count * col_count
    members, local_x, local_y, depth = displacement.shape
    width_y = local_y * col_count
    span_x = local_x * row_count
    hermitian = (depth // 2) % devices == 0
    columns = depth // 2 if hermitian else depth
    per_device = columns // devices
    me = lax.axis_index("row") * col_count + lax.axis_index("col")

    reciprocal = 1.0 / permittivity
    regions = permittivity.shape[0]
    first = rounded(reciprocal)
    rest = reciprocal - first
    second = rounded(rest)
    parts = jnp.concatenate([first, second, rest - second]).astype(BF16)
    slots = lax.iota(jnp.int32, 3 * regions) % regions
    one_hot = (region[..., None] == slots).astype(BF16)
    cell_scale = jnp.einsum("...k,k->...", one_hot, parts, preferred_element_type=F32)
    electric = displacement.astype(F32) * cell_scale[None]

    cos_z, sin_z = phase_table(columns, depth, depth)
    if hermitian:
        parity = (1 - 2 * (lax.iota(jnp.int32, depth) % 2)).astype(F32)
        first_row = (lax.iota(jnp.int32, columns) == 0)[:, None]
        sin_part = jnp.where(first_row, parity[None, :], -sin_z)
    else:
        sin_part = -sin_z
    table_z = jnp.stack(
        [cos_z.reshape(devices, per_device, depth), sin_part.reshape(devices, per_device, depth)],
        axis=1,
    ).reshape(2 * columns, depth)
    z_high, z_low = split_parts(table_z)
    rows = members * local_x * local_y

    e_high, e_low = split_parts(electric.reshape(rows, depth))
    spec_z = "dpjz,cyz->dcpjy"
    blocks = (devices, 2, per_device, depth)
    lines = (members * local_x, local_y, depth)
    z_high4, z_low4 = z_high.reshape(blocks), z_low.reshape(blocks)
    e_high, e_low = e_high.reshape(lines), e_low.reshape(lines)
    spectrum = (
        jnp.einsum(spec_z, z_high4, e_high, preferred_element_type=F32)
        + jnp.einsum(spec_z, z_high4, e_low, preferred_element_type=F32)
        + jnp.einsum(spec_z, z_low4, e_high, preferred_element_type=F32)
    )
    spectrum = spectrum.astype(BF16)
    gathered = lax.all_to_all(
        spectrum, ("row", "col"), split_axis=0, concat_axis=0, tiled=True
    )
    gathered = gathered.reshape(
        row_count, col_count, members, local_x, 2, per_device, local_y
    )
    gathered = jnp.transpose(gathered, (2, 4, 5, 0, 3, 1, 6)).reshape(
        members, 2, per_device, span_x, width_y
    )

    cos_y, sin_y = phase_table(width_y, width_y, width_y)
    cos_y_parts = split_parts(cos_y)
    sin_y_parts = split_parts(sin_y)
    spec_y = "yk,cpjxy->cpjxk"
    by_cos = mat(cos_y_parts, gathered, spec_y)
    by_sin = mat(sin_y_parts, gathered, spec_y)
    y_real = by_cos[:, 0] + by_sin[:, 1]
    y_imag = by_cos[:, 1] - by_sin[:, 0]

    kernel = jnp.asarray(x_kernel(span_x))
    wave_y = wavenumber(lax.iota(jnp.int32, width_y), width_y)
    wave_z = wavenumber(me * per_device + lax.iota(jnp.int32, per_device), depth)

    def inverse_y(b_real, b_imag):
        stacked = jnp.stack([b_real, b_imag], axis=1).astype(BF16)
        by_cos = mat(cos_y_parts, stacked, spec_y)
        by_sin = mat(sin_y_parts, stacked, spec_y)
        scale = 1.0 / width_y
        out_real = (by_cos[:, 0] - by_sin[:, 1]) * scale
        out_imag = (by_cos[:, 1] + by_sin[:, 0]) * scale
        return rounded(out_real), rounded(out_imag)

    b_real, b_imag = curl_update(rounded(y_real), rounded(y_imag), wave_y, wave_z, kernel)
    back_real, back_imag = inverse_y(rounded(b_real), rounded(b_imag))

    if hermitian:
        plane_real = by_cos[:, :, 0]
        plane_imag = -by_sin[:, :, 0]
        pb_real, pb_imag = curl_update(
            rounded(plane_real), rounded(plane_imag), wave_y, jnp.zeros((2,), F32), kernel
        )
        pback_real, _ = inverse_y(rounded(pb_real), rounded(pb_imag))
        is_first = me == 0
        packed = ((lax.iota(jnp.int32, per_device) == 0) & is_first)[None, :, None, None]
        back_real = jnp.where(packed, pback_real[:, 0:1], back_real)
        back_imag = jnp.where(packed, pback_real[:, 1:2], back_imag)

    outgoing = jnp.stack([back_real, back_imag], axis=1).astype(BF16)
    outgoing = outgoing.reshape(
        members, 2, per_device, row_count, local_x, col_count, local_y
    )
    outgoing = jnp.transpose(outgoing, (3, 5, 1, 2, 0, 4, 6)).reshape(
        devices, 2, per_device, members, local_x, local_y
    )
    returned = lax.all_to_all(
        outgoing, ("row", "col"), split_axis=0, concat_axis=0, tiled=True
    )
    returned = returned.reshape(2 * columns, rows)

    weight = np.full((devices, 2, per_device), 1.0 / depth, np.float32)
    if hermitian:
        weight[:] = 2.0 / depth
        weight[0, :, 0] = 1.0 / depth
    weight = jnp.asarray(weight.reshape(2 * columns, 1))
    back_high = (z_high.astype(F32) * weight).astype(BF16)
    back_low = (z_low.astype(F32) * weight).astype(BF16)
    spec_back = "kr,kz->rz"
    field = jnp.einsum(spec_back, returned, back_high, preferred_element_type=F32) + jnp.einsum(
        spec_back, returned, back_low, preferred_element_type=F32
    )
    field = field.reshape(members, local_x, local_y, depth)
    return (magnetic.astype(F32) + field).astype(BF16)


def solution(mesh):
    in_specs = (
        P(None, "row", "col", None),
        P(None, "row", "col", None),
        P("row", "col", None),
        P(),
    )
    out_specs = P(None, "row", "col", None)
    return jax.shard_map(
        on_device, mesh=mesh, in_specs=in_specs, out_specs=out_specs, check_vma=False
    )
```

```python
import math

import numpy as np
import jax
import jax.numpy as jnp
from jax import lax
from jax.sharding import PartitionSpec as P

TIME_STEP = 0.5
F32 = jnp.float32
BF16 = jnp.bfloat16


def wavenumber(wave_index, length):
    signed = jnp.where(2 * wave_index < length, wave_index, wave_index - length)
    return jnp.where(
        2 * wave_index == length, 0.0, signed.astype(F32) * (2.0 * math.pi / length)
    )


def rounded(values):
    return lax.reduce_precision(values, exponent_bits=8, mantissa_bits=7)


def split_parts(values):
    high = rounded(values)
    low = values - high
    return high.astype(BF16), low.astype(BF16)


def direct_phase(rows, cols, length, step):
    product = (lax.iota(jnp.int32, rows)[:, None] * step) * lax.iota(jnp.int32, cols)[None, :]
    angle = (product % length).astype(F32) * (2.0 * math.pi / length)
    return jnp.cos(angle), jnp.sin(angle)


def phase_table(rows, cols, length):
    block = 32
    if rows % block or rows <= block:
        return direct_phase(rows, cols, length, 1)
    outer_cos, outer_sin = direct_phase(rows // block, cols, length, block)
    inner_cos, inner_sin = direct_phase(block, cols, length, 1)
    outer_cos, outer_sin = outer_cos[:, None], outer_sin[:, None]
    inner_cos, inner_sin = inner_cos[None], inner_sin[None]
    cosine = outer_cos * inner_cos - outer_sin * inner_sin
    sine = outer_sin * inner_cos + outer_cos * inner_sin
    return cosine.reshape(rows, cols), sine.reshape(rows, cols)


def x_kernel(span_x):
    index = np.arange(span_x)
    signed = np.where(2 * index < span_x, index, index - span_x)
    qx = np.where(2 * index == span_x, 0.0, signed * (2.0 * math.pi / span_x))
    shift = np.arange(span_x)
    phases = np.exp(2j * math.pi * np.outer(shift, index) / span_x)
    taps = (phases * (-0.5j * qx)[None, :]).sum(axis=1) / span_x
    taps = taps.real
    matrix = taps[(shift[:, None] - shift[None, :]) % span_x]
    return matrix.astype(np.float32)


def mat(table_parts, operand, spec):
    total = None
    for part in table_parts:
        term = jnp.einsum(spec, part, operand, preferred_element_type=F32)
        total = term if total is None else total + term
    return total


def curl_update(y_real, y_imag, wave_y, wave_z, kernel):
    half = TIME_STEP

    def along_x(values):
        return jnp.einsum("ab,jbk->jak", kernel, values, precision=lax.Precision.HIGHEST)

    xr, yr, zr = y_real[0], y_real[1], y_real[2]
    xi, yi, zi = y_imag[0], y_imag[1], y_imag[2]
    qy = half * wave_y
    qz = half * wave_z[:, None, None]
    gyr, gyi = along_x(yr), along_x(yi)
    gzr, gzi = along_x(zr), along_x(zi)
    b_real = jnp.stack([qy * zi - qz * yi, qz * xi - gzr, gyr - qy * xi])
    b_imag = jnp.stack([qz * yr - qy * zr, -qz * xr - gzi, gyi + qy * xr])
    return b_real, b_imag


def on_device(displacement, magnetic, region, permittivity):
    row_count = lax.axis_size("row")
    col_count = lax.axis_size("col")
    devices = row_count * col_count
    members, local_x, local_y, depth = displacement.shape
    width_y = local_y * col_count
    span_x = local_x * row_count
    hermitian = (depth // 2) % devices == 0
    columns = depth // 2 if hermitian else depth
    per_device = columns // devices
    me = lax.axis_index("row") * col_count + lax.axis_index("col")

    reciprocal = 1.0 / permittivity
    regions = permittivity.shape[0]
    first = rounded(reciprocal)
    rest = reciprocal - first
    second = rounded(rest)
    parts = jnp.concatenate([first, second, rest - second]).astype(BF16)
    slots = lax.iota(jnp.int32, 3 * regions) % regions
    one_hot = (region[..., None] == slots).astype(BF16)
    cell_scale = jnp.einsum("...k,k->...", one_hot, parts, preferred_element_type=F32)
    electric = displacement.astype(F32) * cell_scale[None]

    cos_z, sin_z = phase_table(columns, depth, depth)
    if hermitian:
        parity = (1 - 2 * (lax.iota(jnp.int32, depth) % 2)).astype(F32)
        first_row = (lax.iota(jnp.int32, columns) == 0)[:, None]
        sin_part = jnp.where(first_row, parity[None, :], -sin_z)
    else:
        sin_part = -sin_z
    table_z = jnp.stack(
        [cos_z.reshape(devices, per_device, depth), sin_part.reshape(devices, per_device, depth)],
        axis=1,
    ).reshape(2 * columns, depth)
    z_high, z_low = split_parts(table_z)
    rows = members * local_x * local_y

    e_high, e_low = split_parts(electric.reshape(rows, depth))
    spec_z = "dpjz,cyz->dcpjy"
    blocks = (devices, 2, per_device, depth)
    lines = (members * local_x, local_y, depth)
    z_high4, z_low4 = z_high.reshape(blocks), z_low.reshape(blocks)
    e_high, e_low = e_high.reshape(lines), e_low.reshape(lines)
    spectrum = (
        jnp.einsum(spec_z, z_high4, e_high, preferred_element_type=F32)
        + jnp.einsum(spec_z, z_high4, e_low, preferred_element_type=F32)
        + jnp.einsum(spec_z, z_low4, e_high, preferred_element_type=F32)
    )
    spectrum = spectrum.astype(BF16)
    gathered = lax.all_to_all(
        spectrum, ("row", "col"), split_axis=0, concat_axis=0, tiled=True
    )
    gathered = gathered.reshape(
        row_count, col_count, members, local_x, 2, per_device, local_y
    )
    gathered = jnp.transpose(gathered, (2, 4, 5, 0, 3, 1, 6)).reshape(
        members, 2, per_device, span_x, width_y
    )

    cos_y, sin_y = phase_table(width_y, width_y, width_y)
    both_y_parts = split_parts(jnp.concatenate([cos_y, sin_y], axis=1))
    spec_y = "yk,cpjxy->cpjxk"
    by_both = mat(both_y_parts, gathered, spec_y)
    by_cos, by_sin = by_both[..., :width_y], by_both[..., width_y:]
    y_real = by_cos[:, 0] + by_sin[:, 1]
    y_imag = by_cos[:, 1] - by_sin[:, 0]

    kernel = jnp.asarray(x_kernel(span_x))
    wave_y = wavenumber(lax.iota(jnp.int32, width_y), width_y)
    wave_z = wavenumber(me * per_device + lax.iota(jnp.int32, per_device), depth)

    def inverse_y(b_real, b_imag):
        stacked = jnp.stack([b_real, b_imag], axis=1).astype(BF16)
        by_both = mat(both_y_parts, stacked, spec_y)
        by_cos, by_sin = by_both[..., :width_y], by_both[..., width_y:]
        scale = 1.0 / width_y
        out_real = (by_cos[:, 0] - by_sin[:, 1]) * scale
        out_imag = (by_cos[:, 1] + by_sin[:, 0]) * scale
        return rounded(out_real), rounded(out_imag)

    b_real, b_imag = curl_update(rounded(y_real), rounded(y_imag), wave_y, wave_z, kernel)
    back_real, back_imag = inverse_y(rounded(b_real), rounded(b_imag))

    if hermitian:
        plane_real = by_cos[:, :, 0]
        plane_imag = -by_sin[:, :, 0]
        pb_real, pb_imag = curl_update(
            rounded(plane_real), rounded(plane_imag), wave_y, jnp.zeros((2,), F32), kernel
        )
        pback_real, _ = inverse_y(rounded(pb_real), rounded(pb_imag))
        is_first = me == 0
        packed = ((lax.iota(jnp.int32, per_device) == 0) & is_first)[None, :, None, None]
        back_real = jnp.where(packed, pback_real[:, 0:1], back_real)
        back_imag = jnp.where(packed, pback_real[:, 1:2], back_imag)

    outgoing = jnp.stack([back_real, back_imag], axis=1).astype(BF16)
    outgoing = outgoing.reshape(
        members, 2, per_device, row_count, local_x, col_count, local_y
    )
    outgoing = jnp.transpose(outgoing, (3, 5, 1, 2, 0, 4, 6)).reshape(
        devices, 2, per_device, members, local_x, local_y
    )
    returned = lax.all_to_all(
        outgoing, ("row", "col"), split_axis=0, concat_axis=0, tiled=True
    )
    returned = returned.reshape(2 * columns, rows)

    weight = np.full((devices, 2, per_device), 1.0 / depth, np.float32)
    if hermitian:
        weight[:] = 2.0 / depth
        weight[0, :, 0] = 1.0 / depth
    weight = jnp.asarray(weight.reshape(2 * columns, 1))
    back_high = (z_high.astype(F32) * weight).astype(BF16)
    back_low = (z_low.astype(F32) * weight).astype(BF16)
    spec_back = "kr,kz->rz"
    field = jnp.einsum(spec_back, returned, back_high, preferred_element_type=F32) + jnp.einsum(
        spec_back, returned, back_low, preferred_element_type=F32
    )
    field = field.reshape(members, local_x, local_y, depth)
    return (magnetic.astype(F32) + field).astype(BF16)


def solution(mesh):
    in_specs = (
        P(None, "row", "col", None),
        P(None, "row", "col", None),
        P("row", "col", None),
        P(),
    )
    out_specs = P(None, "row", "col", None)
    return jax.shard_map(
        on_device, mesh=mesh, in_specs=in_specs, out_specs=out_specs, check_vma=False
    )
```

```python
import math

import numpy as np
import jax
import jax.numpy as jnp
from jax import lax
from jax.sharding import PartitionSpec as P

TIME_STEP = 0.5
F32 = jnp.float32
BF16 = jnp.bfloat16


def wavenumber(wave_index, length):
    signed = jnp.where(2 * wave_index < length, wave_index, wave_index - length)
    return jnp.where(
        2 * wave_index == length, 0.0, signed.astype(F32) * (2.0 * math.pi / length)
    )


def rounded(values):
    return lax.reduce_precision(values, exponent_bits=8, mantissa_bits=7)


def split_parts(values):
    high = rounded(values)
    low = values - high
    return high.astype(BF16), low.astype(BF16)


def direct_phase(rows, cols, length, step):
    product = (lax.iota(jnp.int32, rows)[:, None] * step) * lax.iota(jnp.int32, cols)[None, :]
    angle = (product % length).astype(F32) * (2.0 * math.pi / length)
    return jnp.cos(angle), jnp.sin(angle)


def phase_table(rows, cols, length):
    block = 32
    if rows % block or rows <= block:
        return direct_phase(rows, cols, length, 1)
    outer_cos, outer_sin = direct_phase(rows // block, cols, length, block)
    inner_cos, inner_sin = direct_phase(block, cols, length, 1)
    outer_cos, outer_sin = outer_cos[:, None], outer_sin[:, None]
    inner_cos, inner_sin = inner_cos[None], inner_sin[None]
    cosine = outer_cos * inner_cos - outer_sin * inner_sin
    sine = outer_sin * inner_cos + outer_cos * inner_sin
    return cosine.reshape(rows, cols), sine.reshape(rows, cols)


def x_kernel(span_x):
    index = np.arange(span_x)
    signed = np.where(2 * index < span_x, index, index - span_x)
    qx = np.where(2 * index == span_x, 0.0, signed * (2.0 * math.pi / span_x))
    shift = np.arange(span_x)
    phases = np.exp(2j * math.pi * np.outer(shift, index) / span_x)
    taps = (phases * (-0.5j * qx)[None, :]).sum(axis=1) / span_x
    taps = taps.real
    matrix = taps[(shift[:, None] - shift[None, :]) % span_x]
    return matrix.astype(np.float32)


def mat(table_parts, operand, spec):
    total = None
    for part in table_parts:
        term = jnp.einsum(spec, part, operand, preferred_element_type=F32)
        total = term if total is None else total + term
    return total


def curl_update(y_real, y_imag, wave_y, wave_z, kernel):
    half = TIME_STEP

    def along_x(values):
        return jnp.einsum("ab,jbk->jak", kernel, values, precision=lax.Precision.HIGHEST)

    xr, yr, zr = y_real[0], y_real[1], y_real[2]
    xi, yi, zi = y_imag[0], y_imag[1], y_imag[2]
    qy = half * wave_y
    qz = half * wave_z[:, None, None]
    gyr, gyi = along_x(yr), along_x(yi)
    gzr, gzi = along_x(zr), along_x(zi)
    b_real = jnp.stack([qy * zi - qz * yi, qz * xi - gzr, gyr - qy * xi])
    b_imag = jnp.stack([qz * yr - qy * zr, -qz * xr - gzi, gyi + qy * xr])
    return b_real, b_imag


def on_device(displacement, magnetic, region, permittivity):
    row_count = lax.axis_size("row")
    col_count = lax.axis_size("col")
    devices = row_count * col_count
    members, local_x, local_y, depth = displacement.shape
    width_y = local_y * col_count
    span_x = local_x * row_count
    hermitian = (depth // 2) % devices == 0
    columns = depth // 2 if hermitian else depth
    per_device = columns // devices
    me = lax.axis_index("row") * col_count + lax.axis_index("col")

    reciprocal = 1.0 / permittivity
    regions = permittivity.shape[0]
    first = rounded(reciprocal)
    rest = reciprocal - first
    second = rounded(rest)
    parts = jnp.concatenate([first, second, rest - second]).astype(BF16)
    slots = lax.iota(jnp.int32, 3 * regions) % regions
    one_hot = (region[..., None] == slots).astype(BF16)
    cell_scale = jnp.einsum("...k,k->...", one_hot, parts, preferred_element_type=F32)
    electric = displacement.astype(F32) * cell_scale[None]

    cos_z, sin_z = phase_table(columns, depth, depth)
    if hermitian:
        parity = (1 - 2 * (lax.iota(jnp.int32, depth) % 2)).astype(F32)
        first_row = (lax.iota(jnp.int32, columns) == 0)[:, None]
        sin_part = jnp.where(first_row, parity[None, :], -sin_z)
    else:
        sin_part = -sin_z
    table_z = jnp.stack(
        [cos_z.reshape(devices, per_device, depth), sin_part.reshape(devices, per_device, depth)],
        axis=1,
    ).reshape(2 * columns, depth)
    z_high, z_low = split_parts(table_z)
    rows = members * local_x * local_y

    e_high, e_low = split_parts(electric.reshape(rows, depth))
    spec_z = "dpjz,cyz->dcpjy"
    blocks = (devices, 2, per_device, depth)
    lines = (members * local_x, local_y, depth)
    z_high4, z_low4 = z_high.reshape(blocks), z_low.reshape(blocks)
    e_high, e_low = e_high.reshape(lines), e_low.reshape(lines)
    z_both = jnp.stack([z_high4, z_low4])
    by_high = jnp.einsum("h" + spec_z.replace("->", "->h"), z_both, e_high, preferred_element_type=F32)
    spectrum = (
        by_high[0]
        + by_high[1]
        + jnp.einsum(spec_z, z_high4, e_low, preferred_element_type=F32)
    )
    spectrum = spectrum.astype(BF16)
    gathered = lax.all_to_all(
        spectrum, ("row", "col"), split_axis=0, concat_axis=0, tiled=True
    )
    gathered = gathered.reshape(
        row_count, col_count, members, local_x, 2, per_device, local_y
    )
    gathered = jnp.transpose(gathered, (2, 4, 5, 0, 3, 1, 6)).reshape(
        members, 2, per_device, span_x, width_y
    )

    cos_y, sin_y = phase_table(width_y, width_y, width_y)
    both_y_parts = split_parts(jnp.concatenate([cos_y, sin_y], axis=1))
    spec_y = "yk,cpjxy->cpjxk"
    by_both = mat(both_y_parts, gathered, spec_y)
    by_cos, by_sin = by_both[..., :width_y], by_both[..., width_y:]
    y_real = by_cos[:, 0] + by_sin[:, 1]
    y_imag = by_cos[:, 1] - by_sin[:, 0]

    kernel = jnp.asarray(x_kernel(span_x))
    wave_y = wavenumber(lax.iota(jnp.int32, width_y), width_y)
    wave_z = wavenumber(me * per_device + lax.iota(jnp.int32, per_device), depth)

    def inverse_y(b_real, b_imag):
        stacked = jnp.stack([b_real, b_imag], axis=1).astype(BF16)
        by_both = mat(both_y_parts, stacked, spec_y)
        by_cos, by_sin = by_both[..., :width_y], by_both[..., width_y:]
        scale = 1.0 / width_y
        out_real = (by_cos[:, 0] - by_sin[:, 1]) * scale
        out_imag = (by_cos[:, 1] + by_sin[:, 0]) * scale
        return rounded(out_real), rounded(out_imag)

    b_real, b_imag = curl_update(rounded(y_real), rounded(y_imag), wave_y, wave_z, kernel)
    back_real, back_imag = inverse_y(rounded(b_real), rounded(b_imag))

    if hermitian:
        plane_real = by_cos[:, :, 0]
        plane_imag = -by_sin[:, :, 0]
        pb_real, pb_imag = curl_update(
            rounded(plane_real), rounded(plane_imag), wave_y, jnp.zeros((2,), F32), kernel
        )
        pback_real, _ = inverse_y(rounded(pb_real), rounded(pb_imag))
        is_first = me == 0
        packed = ((lax.iota(jnp.int32, per_device) == 0) & is_first)[None, :, None, None]
        back_real = jnp.where(packed, pback_real[:, 0:1], back_real)
        back_imag = jnp.where(packed, pback_real[:, 1:2], back_imag)

    outgoing = jnp.stack([back_real, back_imag], axis=1).astype(BF16)
    outgoing = outgoing.reshape(
        members, 2, per_device, row_count, local_x, col_count, local_y
    )
    outgoing = jnp.transpose(outgoing, (3, 5, 1, 2, 0, 4, 6)).reshape(
        devices, 2, per_device, members, local_x, local_y
    )
    returned = lax.all_to_all(
        outgoing, ("row", "col"), split_axis=0, concat_axis=0, tiled=True
    )
    returned = returned.reshape(2 * columns, rows)

    weight = np.full((devices, 2, per_device), 1.0 / depth, np.float32)
    if hermitian:
        weight[:] = 2.0 / depth
        weight[0, :, 0] = 1.0 / depth
    weight = jnp.asarray(weight.reshape(2 * columns, 1))
    back_high = (z_high.astype(F32) * weight).astype(BF16)
    back_low = (z_low.astype(F32) * weight).astype(BF16)
    back_both = jnp.stack([back_high, back_low], axis=1)
    field = jnp.einsum("kr,khz->rhz", returned, back_both, preferred_element_type=F32)
    field = field[:, 0] + field[:, 1]
    field = field.reshape(members, local_x, local_y, depth)
    return (magnetic.astype(F32) + field).astype(BF16)


def solution(mesh):
    in_specs = (
        P(None, "row", "col", None),
        P(None, "row", "col", None),
        P("row", "col", None),
        P(),
    )
    out_specs = P(None, "row", "col", None)
    return jax.shard_map(
        on_device, mesh=mesh, in_specs=in_specs, out_specs=out_specs, check_vma=False
    )
```

```python
import math

import numpy as np
import jax
import jax.numpy as jnp
from jax import lax
from jax.sharding import PartitionSpec as P

TIME_STEP = 0.5
F32 = jnp.float32
BF16 = jnp.bfloat16


def wavenumber(wave_index, length):
    signed = jnp.where(2 * wave_index < length, wave_index, wave_index - length)
    return jnp.where(
        2 * wave_index == length, 0.0, signed.astype(F32) * (2.0 * math.pi / length)
    )


def rounded(values):
    return lax.reduce_precision(values, exponent_bits=8, mantissa_bits=7)


def split_parts(values):
    high = rounded(values)
    low = values - high
    return high.astype(BF16), low.astype(BF16)


def direct_phase(rows, cols, length, step):
    product = (lax.iota(jnp.int32, rows)[:, None] * step) * lax.iota(jnp.int32, cols)[None, :]
    angle = (product % length).astype(F32) * (2.0 * math.pi / length)
    return jnp.cos(angle), jnp.sin(angle)


def phase_table(rows, cols, length):
    block = 32
    if rows % block or rows <= block:
        return direct_phase(rows, cols, length, 1)
    outer_cos, outer_sin = direct_phase(rows // block, cols, length, block)
    inner_cos, inner_sin = direct_phase(block, cols, length, 1)
    outer_cos, outer_sin = outer_cos[:, None], outer_sin[:, None]
    inner_cos, inner_sin = inner_cos[None], inner_sin[None]
    cosine = outer_cos * inner_cos - outer_sin * inner_sin
    sine = outer_sin * inner_cos + outer_cos * inner_sin
    return cosine.reshape(rows, cols), sine.reshape(rows, cols)


def x_kernel(span_x):
    index = np.arange(span_x)
    signed = np.where(2 * index < span_x, index, index - span_x)
    qx = np.where(2 * index == span_x, 0.0, signed * (2.0 * math.pi / span_x))
    shift = np.arange(span_x)
    phases = np.exp(2j * math.pi * np.outer(shift, index) / span_x)
    taps = (phases * (-0.5j * qx)[None, :]).sum(axis=1) / span_x
    taps = taps.real
    matrix = taps[(shift[:, None] - shift[None, :]) % span_x]
    return matrix.astype(np.float32)


def mat(table_parts, operand, spec):
    total = None
    for part in table_parts:
        term = jnp.einsum(spec, part, operand, preferred_element_type=F32)
        total = term if total is None else total + term
    return total


def curl_update(y_real, y_imag, wave_y, wave_z, kernel):
    half = TIME_STEP

    def along_x(values):
        return jnp.einsum("ab,jbk->jak", kernel, values, precision=lax.Precision.HIGHEST)

    xr, yr, zr = y_real[0], y_real[1], y_real[2]
    xi, yi, zi = y_imag[0], y_imag[1], y_imag[2]
    qy = half * wave_y
    qz = half * wave_z[:, None, None]
    gyr, gyi = along_x(yr), along_x(yi)
    gzr, gzi = along_x(zr), along_x(zi)
    b_real = jnp.stack([qy * zi - qz * yi, qz * xi - gzr, gyr - qy * xi])
    b_imag = jnp.stack([qz * yr - qy * zr, -qz * xr - gzi, gyi + qy * xr])
    return b_real, b_imag


def on_device(displacement, magnetic, region, permittivity):
    row_count = lax.axis_size("row")
    col_count = lax.axis_size("col")
    devices = row_count * col_count
    members, local_x, local_y, depth = displacement.shape
    width_y = local_y * col_count
    span_x = local_x * row_count
    hermitian = (depth // 2) % devices == 0
    columns = depth // 2 if hermitian else depth
    per_device = columns // devices
    me = lax.axis_index("row") * col_count + lax.axis_index("col")

    reciprocal = 1.0 / permittivity
    regions = permittivity.shape[0]
    first = rounded(reciprocal)
    rest = reciprocal - first
    second = rounded(rest)
    parts = jnp.concatenate([first, second, rest - second]).astype(BF16)
    slots = lax.iota(jnp.int32, 3 * regions) % regions
    one_hot = (region[..., None] == slots).astype(BF16)
    cell_scale = jnp.einsum("...k,k->...", one_hot, parts, preferred_element_type=F32)
    electric = displacement.astype(F32) * cell_scale[None]

    cos_z, sin_z = phase_table(columns, depth, depth)
    if hermitian:
        parity = (1 - 2 * (lax.iota(jnp.int32, depth) % 2)).astype(F32)
        first_row = (lax.iota(jnp.int32, columns) == 0)[:, None]
        sin_part = jnp.where(first_row, parity[None, :], -sin_z)
    else:
        sin_part = -sin_z
    table_z = jnp.stack(
        [cos_z.reshape(devices, per_device, depth), sin_part.reshape(devices, per_device, depth)],
        axis=1,
    ).reshape(2 * columns, depth)
    z_high, z_low = split_parts(table_z)
    rows = members * local_x * local_y

    e_high, e_low = split_parts(electric.reshape(rows, depth))
    spec_z = "dpjz,cyz->dcpjy"
    blocks = (devices, 2, per_device, depth)
    lines = (members * local_x, local_y, depth)
    z_high4, z_low4 = z_high.reshape(blocks), z_low.reshape(blocks)
    e_high, e_low = e_high.reshape(lines), e_low.reshape(lines)
    spectrum = (
        jnp.einsum(spec_z, z_high4, e_high, preferred_element_type=F32)
        + jnp.einsum(spec_z, z_high4, e_low, preferred_element_type=F32)
        + jnp.einsum(spec_z, z_low4, e_high, preferred_element_type=F32)
    )
    spectrum = spectrum.astype(BF16)
    gathered = lax.all_to_all(
        spectrum, ("row", "col"), split_axis=0, concat_axis=0, tiled=True
    )
    gathered = gathered.reshape(
        row_count, col_count, members, local_x, 2, per_device, local_y
    )
    gathered = jnp.transpose(gathered, (2, 4, 5, 0, 3, 1, 6)).reshape(
        members, 2, per_device, span_x, width_y
    )

    cos_y, sin_y = phase_table(width_y, width_y, width_y)
    both_y_parts = split_parts(jnp.concatenate([cos_y, sin_y], axis=1))
    spec_y = "yk,cpjxy->cpjxk"
    by_both = mat(both_y_parts, gathered, spec_y)
    by_cos, by_sin = by_both[..., :width_y], by_both[..., width_y:]
    y_real = by_cos[:, 0] + by_sin[:, 1]
    y_imag = by_cos[:, 1] - by_sin[:, 0]

    kernel = jnp.asarray(x_kernel(span_x))
    wave_y = wavenumber(lax.iota(jnp.int32, width_y), width_y)
    wave_z = wavenumber(me * per_device + lax.iota(jnp.int32, per_device), depth)

    def inverse_y(b_real, b_imag):
        stacked = jnp.stack([b_real, b_imag], axis=1).astype(BF16)
        by_both = mat(both_y_parts, stacked, spec_y)
        by_cos, by_sin = by_both[..., :width_y], by_both[..., width_y:]
        scale = 1.0 / width_y
        out_real = (by_cos[:, 0] - by_sin[:, 1]) * scale
        out_imag = (by_cos[:, 1] + by_sin[:, 0]) * scale
        return rounded(out_real), rounded(out_imag)

    b_real, b_imag = curl_update(rounded(y_real), rounded(y_imag), wave_y, wave_z, kernel)
    back_real, back_imag = inverse_y(rounded(b_real), rounded(b_imag))

    if hermitian:
        plane_real = by_cos[:, :, 0]
        plane_imag = -by_sin[:, :, 0]
        pb_real, pb_imag = curl_update(
            rounded(plane_real), rounded(plane_imag), wave_y, jnp.zeros((2,), F32), kernel
        )
        pback_real, _ = inverse_y(rounded(pb_real), rounded(pb_imag))
        is_first = me == 0
        packed = ((lax.iota(jnp.int32, per_device) == 0) & is_first)[None, :, None, None]
        back_real = jnp.where(packed, pback_real[:, 0:1], back_real)
        back_imag = jnp.where(packed, pback_real[:, 1:2], back_imag)

    outgoing = jnp.stack([back_real, back_imag], axis=1).astype(BF16)
    outgoing = outgoing.reshape(
        members, 2, per_device, row_count, local_x, col_count, local_y
    )
    outgoing = jnp.transpose(outgoing, (3, 5, 1, 2, 0, 4, 6)).reshape(
        devices, 2, per_device, members, local_x, local_y
    )
    returned = lax.all_to_all(
        outgoing, ("row", "col"), split_axis=0, concat_axis=0, tiled=True
    )
    returned = returned.reshape(2 * columns, rows)

    weight = np.full((devices, 2, per_device), 1.0 / depth, np.float32)
    if hermitian:
        weight[:] = 2.0 / depth
        weight[0, :, 0] = 1.0 / depth
    weight = jnp.asarray(weight.reshape(2 * columns, 1))
    back_high = (z_high.astype(F32) * weight).astype(BF16)
    back_low = (z_low.astype(F32) * weight).astype(BF16)
    back_both = jnp.stack([back_high, back_low], axis=1)
    field = jnp.einsum("kr,khz->rhz", returned, back_both, preferred_element_type=F32)
    field = field[:, 0] + field[:, 1]
    field = field.reshape(members, local_x, local_y, depth)
    return (magnetic.astype(F32) + field).astype(BF16)


def solution(mesh):
    in_specs = (
        P(None, "row", "col", None),
        P(None, "row", "col", None),
        P("row", "col", None),
        P(),
    )
    out_specs = P(None, "row", "col", None)
    return jax.shard_map(
        on_device, mesh=mesh, in_specs=in_specs, out_specs=out_specs, check_vma=False
    )
```

```python
import math

import numpy as np
import jax
import jax.numpy as jnp
from jax import lax
from jax.sharding import PartitionSpec as P

TIME_STEP = 0.5
F32 = jnp.float32
BF16 = jnp.bfloat16


def wavenumber(wave_index, length):
    signed = jnp.where(2 * wave_index < length, wave_index, wave_index - length)
    return jnp.where(
        2 * wave_index == length, 0.0, signed.astype(F32) * (2.0 * math.pi / length)
    )


def rounded(values):
    return lax.reduce_precision(values, exponent_bits=8, mantissa_bits=7)


def split_parts(values):
    high = rounded(values)
    low = values - high
    return high.astype(BF16), low.astype(BF16)


def direct_phase(rows, cols, length, step):
    product = (lax.iota(jnp.int32, rows)[:, None] * step) * lax.iota(jnp.int32, cols)[None, :]
    angle = (product % length).astype(F32) * (2.0 * math.pi / length)
    return jnp.cos(angle), jnp.sin(angle)


def phase_table(rows, cols, length):
    block = 32
    if rows % block or rows <= block:
        return direct_phase(rows, cols, length, 1)
    outer_cos, outer_sin = direct_phase(rows // block, cols, length, block)
    inner_cos, inner_sin = direct_phase(block, cols, length, 1)
    outer_cos, outer_sin = outer_cos[:, None], outer_sin[:, None]
    inner_cos, inner_sin = inner_cos[None], inner_sin[None]
    cosine = outer_cos * inner_cos - outer_sin * inner_sin
    sine = outer_sin * inner_cos + outer_cos * inner_sin
    return cosine.reshape(rows, cols), sine.reshape(rows, cols)


def x_kernel(span_x):
    index = np.arange(span_x)
    signed = np.where(2 * index < span_x, index, index - span_x)
    qx = np.where(2 * index == span_x, 0.0, signed * (2.0 * math.pi / span_x))
    shift = np.arange(span_x)
    phases = np.exp(2j * math.pi * np.outer(shift, index) / span_x)
    taps = (phases * (-0.5j * qx)[None, :]).sum(axis=1) / span_x
    taps = taps.real
    matrix = taps[(shift[:, None] - shift[None, :]) % span_x]
    return matrix.astype(np.float32)


def mat(table_parts, operand, spec):
    total = None
    for part in table_parts:
        term = jnp.einsum(spec, part, operand, preferred_element_type=F32)
        total = term if total is None else total + term
    return total


def curl_update(y_real, y_imag, wave_y, wave_z, kernel):
    half = TIME_STEP

    xr, yr, zr = y_real[0], y_real[1], y_real[2]
    xi, yi, zi = y_imag[0], y_imag[1], y_imag[2]
    qy = half * wave_y
    qz = half * wave_z[:, None, None]
    mixed = jnp.einsum(
        "ab,qjbk->qjak",
        kernel,
        jnp.stack([yr, yi, zr, zi]),
        precision=lax.Precision.HIGHEST,
    )
    gyr, gyi, gzr, gzi = mixed[0], mixed[1], mixed[2], mixed[3]
    b_real = jnp.stack([qy * zi - qz * yi, qz * xi - gzr, gyr - qy * xi])
    b_imag = jnp.stack([qz * yr - qy * zr, -qz * xr - gzi, gyi + qy * xr])
    return b_real, b_imag


def on_device(displacement, magnetic, region, permittivity):
    row_count = lax.axis_size("row")
    col_count = lax.axis_size("col")
    devices = row_count * col_count
    members, local_x, local_y, depth = displacement.shape
    width_y = local_y * col_count
    span_x = local_x * row_count
    hermitian = (depth // 2) % devices == 0
    columns = depth // 2 if hermitian else depth
    per_device = columns // devices
    me = lax.axis_index("row") * col_count + lax.axis_index("col")

    reciprocal = 1.0 / permittivity
    regions = permittivity.shape[0]
    first = rounded(reciprocal)
    rest = reciprocal - first
    second = rounded(rest)
    parts = jnp.concatenate([first, second, rest - second]).astype(BF16)
    slots = lax.iota(jnp.int32, 3 * regions) % regions
    one_hot = (region[..., None] == slots).astype(BF16)
    cell_scale = jnp.einsum("...k,k->...", one_hot, parts, preferred_element_type=F32)
    electric = displacement.astype(F32) * cell_scale[None]

    cos_z, sin_z = phase_table(columns, depth, depth)
    if hermitian:
        parity = (1 - 2 * (lax.iota(jnp.int32, depth) % 2)).astype(F32)
        first_row = (lax.iota(jnp.int32, columns) == 0)[:, None]
        sin_part = jnp.where(first_row, parity[None, :], -sin_z)
    else:
        sin_part = -sin_z
    table_z = jnp.stack(
        [cos_z.reshape(devices, per_device, depth), sin_part.reshape(devices, per_device, depth)],
        axis=1,
    ).reshape(2 * columns, depth)
    z_high, z_low = split_parts(table_z)
    rows = members * local_x * local_y

    e_high, e_low = split_parts(electric.reshape(rows, depth))
    spec_z = "dpjz,cyz->dcpjy"
    blocks = (devices, 2, per_device, depth)
    lines = (members * local_x, local_y, depth)
    z_high4, z_low4 = z_high.reshape(blocks), z_low.reshape(blocks)
    e_high, e_low = e_high.reshape(lines), e_low.reshape(lines)
    spectrum = (
        jnp.einsum(spec_z, z_high4, e_high, preferred_element_type=F32)
        + jnp.einsum(spec_z, z_high4, e_low, preferred_element_type=F32)
        + jnp.einsum(spec_z, z_low4, e_high, preferred_element_type=F32)
    )
    spectrum = spectrum.astype(BF16)
    gathered = lax.all_to_all(
        spectrum, ("row", "col"), split_axis=0, concat_axis=0, tiled=True
    )
    gathered = gathered.reshape(
        row_count, col_count, members, local_x, 2, per_device, local_y
    )
    gathered = jnp.transpose(gathered, (2, 4, 5, 0, 3, 1, 6)).reshape(
        members, 2, per_device, span_x, width_y
    )

    cos_y, sin_y = phase_table(width_y, width_y, width_y)
    both_y_parts = split_parts(jnp.concatenate([cos_y, sin_y], axis=1))
    spec_y = "yk,cpjxy->cpjxk"
    by_both = mat(both_y_parts, gathered, spec_y)
    by_cos, by_sin = by_both[..., :width_y], by_both[..., width_y:]
    y_real = by_cos[:, 0] + by_sin[:, 1]
    y_imag = by_cos[:, 1] - by_sin[:, 0]

    kernel = jnp.asarray(x_kernel(span_x))
    wave_y = wavenumber(lax.iota(jnp.int32, width_y), width_y)
    wave_z = wavenumber(me * per_device + lax.iota(jnp.int32, per_device), depth)

    def inverse_y(b_real, b_imag):
        stacked = jnp.stack([b_real, b_imag], axis=1).astype(BF16)
        by_both = mat(both_y_parts, stacked, spec_y)
        by_cos, by_sin = by_both[..., :width_y], by_both[..., width_y:]
        scale = 1.0 / width_y
        out_real = (by_cos[:, 0] - by_sin[:, 1]) * scale
        out_imag = (by_cos[:, 1] + by_sin[:, 0]) * scale
        return rounded(out_real), rounded(out_imag)

    b_real, b_imag = curl_update(rounded(y_real), rounded(y_imag), wave_y, wave_z, kernel)
    back_real, back_imag = inverse_y(rounded(b_real), rounded(b_imag))

    if hermitian:
        plane_real = by_cos[:, :, 0]
        plane_imag = -by_sin[:, :, 0]
        pb_real, pb_imag = curl_update(
            rounded(plane_real), rounded(plane_imag), wave_y, jnp.zeros((2,), F32), kernel
        )
        pback_real, _ = inverse_y(rounded(pb_real), rounded(pb_imag))
        is_first = me == 0
        packed = ((lax.iota(jnp.int32, per_device) == 0) & is_first)[None, :, None, None]
        back_real = jnp.where(packed, pback_real[:, 0:1], back_real)
        back_imag = jnp.where(packed, pback_real[:, 1:2], back_imag)

    outgoing = jnp.stack([back_real, back_imag], axis=1).astype(BF16)
    outgoing = outgoing.reshape(
        members, 2, per_device, row_count, local_x, col_count, local_y
    )
    outgoing = jnp.transpose(outgoing, (3, 5, 1, 2, 0, 4, 6)).reshape(
        devices, 2, per_device, members, local_x, local_y
    )
    returned = lax.all_to_all(
        outgoing, ("row", "col"), split_axis=0, concat_axis=0, tiled=True
    )
    returned = returned.reshape(2 * columns, rows)

    weight = np.full((devices, 2, per_device), 1.0 / depth, np.float32)
    if hermitian:
        weight[:] = 2.0 / depth
        weight[0, :, 0] = 1.0 / depth
    weight = jnp.asarray(weight.reshape(2 * columns, 1))
    back_high = (z_high.astype(F32) * weight).astype(BF16)
    back_low = (z_low.astype(F32) * weight).astype(BF16)
    spec_back = "kr,kz->rz"
    field = jnp.einsum(spec_back, returned, back_high, preferred_element_type=F32) + jnp.einsum(
        spec_back, returned, back_low, preferred_element_type=F32
    )
    field = field.reshape(members, local_x, local_y, depth)
    return (magnetic.astype(F32) + field).astype(BF16)


def solution(mesh):
    in_specs = (
        P(None, "row", "col", None),
        P(None, "row", "col", None),
        P("row", "col", None),
        P(),
    )
    out_specs = P(None, "row", "col", None)
    return jax.shard_map(
        on_device, mesh=mesh, in_specs=in_specs, out_specs=out_specs, check_vma=False
    )
```

```python
import math

import numpy as np
import jax
import jax.numpy as jnp
from jax import lax
from jax.sharding import PartitionSpec as P

TIME_STEP = 0.5
F32 = jnp.float32
BF16 = jnp.bfloat16


def wavenumber(wave_index, length):
    signed = jnp.where(2 * wave_index < length, wave_index, wave_index - length)
    return jnp.where(
        2 * wave_index == length, 0.0, signed.astype(F32) * (2.0 * math.pi / length)
    )


def rounded(values):
    return lax.reduce_precision(values, exponent_bits=8, mantissa_bits=7)


def split_parts(values):
    high = rounded(values)
    low = values - high
    return high.astype(BF16), low.astype(BF16)


def direct_phase(rows, cols, length, step):
    product = (lax.iota(jnp.int32, rows)[:, None] * step) * lax.iota(jnp.int32, cols)[None, :]
    angle = (product % length).astype(F32) * (2.0 * math.pi / length)
    return jnp.cos(angle), jnp.sin(angle)


def phase_table(rows, cols, length):
    block = 32
    if rows % block or rows <= block:
        return direct_phase(rows, cols, length, 1)
    outer_cos, outer_sin = direct_phase(rows // block, cols, length, block)
    inner_cos, inner_sin = direct_phase(block, cols, length, 1)
    outer_cos, outer_sin = outer_cos[:, None], outer_sin[:, None]
    inner_cos, inner_sin = inner_cos[None], inner_sin[None]
    cosine = outer_cos * inner_cos - outer_sin * inner_sin
    sine = outer_sin * inner_cos + outer_cos * inner_sin
    return cosine.reshape(rows, cols), sine.reshape(rows, cols)


def x_kernel(span_x):
    index = np.arange(span_x)
    signed = np.where(2 * index < span_x, index, index - span_x)
    qx = np.where(2 * index == span_x, 0.0, signed * (2.0 * math.pi / span_x))
    shift = np.arange(span_x)
    phases = np.exp(2j * math.pi * np.outer(shift, index) / span_x)
    taps = (phases * (-0.5j * qx)[None, :]).sum(axis=1) / span_x
    taps = taps.real
    matrix = taps[(shift[:, None] - shift[None, :]) % span_x]
    return matrix.astype(np.float32)


def mat(table_parts, operand, spec):
    total = None
    for part in table_parts:
        term = jnp.einsum(spec, part, operand, preferred_element_type=F32)
        total = term if total is None else total + term
    return total


def curl_update(y_real, y_imag, wave_y, wave_z, kernel):
    half = TIME_STEP

    xr, yr, zr = y_real[0], y_real[1], y_real[2]
    xi, yi, zi = y_imag[0], y_imag[1], y_imag[2]
    qy = half * wave_y
    qz = half * wave_z[:, None, None]
    mixed = jnp.einsum(
        "ab,qjbk->qjak",
        kernel,
        jnp.stack([yr, yi, zr, zi]),
        precision=lax.Precision.HIGHEST,
    )
    gyr, gyi, gzr, gzi = mixed[0], mixed[1], mixed[2], mixed[3]
    b_real = jnp.stack([qy * zi - qz * yi, qz * xi - gzr, gyr - qy * xi])
    b_imag = jnp.stack([qz * yr - qy * zr, -qz * xr - gzi, gyi + qy * xr])
    return b_real, b_imag


def on_device(displacement, magnetic, region, permittivity):
    row_count = lax.axis_size("row")
    col_count = lax.axis_size("col")
    devices = row_count * col_count
    members, local_x, local_y, depth = displacement.shape
    width_y = local_y * col_count
    span_x = local_x * row_count
    hermitian = (depth // 2) % devices == 0
    columns = depth // 2 if hermitian else depth
    per_device = columns // devices
    me = lax.axis_index("row") * col_count + lax.axis_index("col")

    reciprocal = 1.0 / permittivity
    regions = permittivity.shape[0]
    first = rounded(reciprocal)
    rest = reciprocal - first
    second = rounded(rest)
    parts = jnp.concatenate([first, second, rest - second]).astype(BF16)
    slots = lax.iota(jnp.int32, 3 * regions) % regions
    one_hot = (region[..., None] == slots).astype(BF16)
    cell_scale = jnp.einsum("...k,k->...", one_hot, parts, preferred_element_type=F32)
    electric = displacement.astype(F32) * cell_scale[None]

    cos_z, sin_z = phase_table(columns, depth, depth)
    if hermitian:
        parity = (1 - 2 * (lax.iota(jnp.int32, depth) % 2)).astype(F32)
        first_row = (lax.iota(jnp.int32, columns) == 0)[:, None]
        sin_part = jnp.where(first_row, parity[None, :], -sin_z)
    else:
        sin_part = -sin_z
    table_z = jnp.stack(
        [cos_z.reshape(devices, per_device, depth), sin_part.reshape(devices, per_device, depth)],
        axis=1,
    ).reshape(2 * columns, depth)
    z_high, z_low = split_parts(table_z)
    rows = members * local_x * local_y

    e_high, e_low = split_parts(electric.reshape(rows, depth))
    spec_z = "dpjz,cyz->dcpjy"
    blocks = (devices, 2, per_device, depth)
    lines = (members * local_x, local_y, depth)
    z_high4, z_low4 = z_high.reshape(blocks), z_low.reshape(blocks)
    e_high, e_low = e_high.reshape(lines), e_low.reshape(lines)
    spectrum = (
        jnp.einsum(spec_z, z_high4, e_high, preferred_element_type=F32)
        + jnp.einsum(spec_z, z_high4, e_low, preferred_element_type=F32)
        + jnp.einsum(spec_z, z_low4, e_high, preferred_element_type=F32)
    )
    spectrum = spectrum.astype(BF16)
    gathered = lax.all_to_all(
        spectrum, ("row", "col"), split_axis=0, concat_axis=0, tiled=True
    )
    gathered = gathered.reshape(
        row_count, col_count, members, local_x, 2, per_device, local_y
    )
    gathered = jnp.transpose(gathered, (2, 4, 5, 0, 3, 1, 6)).reshape(
        members, 2, per_device, span_x, width_y
    )

    cos_y, sin_y = phase_table(width_y, width_y, width_y)
    both_y_parts = split_parts(jnp.concatenate([cos_y, sin_y], axis=1))
    spec_y = "yk,cpjxy->cpjxk"
    by_both = mat(both_y_parts, gathered, spec_y)
    by_cos, by_sin = by_both[..., :width_y], by_both[..., width_y:]
    y_real = by_cos[:, 0] + by_sin[:, 1]
    y_imag = by_cos[:, 1] - by_sin[:, 0]

    kernel = jnp.asarray(x_kernel(span_x))
    wave_y = wavenumber(lax.iota(jnp.int32, width_y), width_y)
    wave_z = wavenumber(me * per_device + lax.iota(jnp.int32, per_device), depth)

    def inverse_y(b_real, b_imag):
        stacked = jnp.stack([b_real, b_imag], axis=1).astype(BF16)
        by_both = mat(both_y_parts, stacked, spec_y)
        by_cos, by_sin = by_both[..., :width_y], by_both[..., width_y:]
        scale = 1.0 / width_y
        out_real = (by_cos[:, 0] - by_sin[:, 1]) * scale
        out_imag = (by_cos[:, 1] + by_sin[:, 0]) * scale
        return rounded(out_real), rounded(out_imag)

    y_real, y_imag = rounded(y_real), rounded(y_imag)
    if hermitian:
        y_real = jnp.concatenate([y_real, rounded(by_cos[:, :, 0])], axis=1)
        y_imag = jnp.concatenate([y_imag, rounded(-by_sin[:, :, 0])], axis=1)
        wave_z = jnp.concatenate([wave_z, jnp.zeros((2,), F32)])
    b_real, b_imag = curl_update(y_real, y_imag, wave_y, wave_z, kernel)
    back_real, back_imag = inverse_y(rounded(b_real), rounded(b_imag))

    if hermitian:
        pback_real = back_real[:, per_device:]
        back_real, back_imag = back_real[:, :per_device], back_imag[:, :per_device]
        is_first = me == 0
        packed = ((lax.iota(jnp.int32, per_device) == 0) & is_first)[None, :, None, None]
        back_real = jnp.where(packed, pback_real[:, 0:1], back_real)
        back_imag = jnp.where(packed, pback_real[:, 1:2], back_imag)

    outgoing = jnp.stack([back_real, back_imag], axis=1).astype(BF16)
    outgoing = outgoing.reshape(
        members, 2, per_device, row_count, local_x, col_count, local_y
    )
    outgoing = jnp.transpose(outgoing, (3, 5, 1, 2, 0, 4, 6)).reshape(
        devices, 2, per_device, members, local_x, local_y
    )
    returned = lax.all_to_all(
        outgoing, ("row", "col"), split_axis=0, concat_axis=0, tiled=True
    )
    returned = returned.reshape(2 * columns, rows)

    weight = np.full((devices, 2, per_device), 1.0 / depth, np.float32)
    if hermitian:
        weight[:] = 2.0 / depth
        weight[0, :, 0] = 1.0 / depth
    weight = jnp.asarray(weight.reshape(2 * columns, 1))
    back_high = (z_high.astype(F32) * weight).astype(BF16)
    back_low = (z_low.astype(F32) * weight).astype(BF16)
    spec_back = "kr,kz->rz"
    field = jnp.einsum(spec_back, returned, back_high, preferred_element_type=F32) + jnp.einsum(
        spec_back, returned, back_low, preferred_element_type=F32
    )
    field = field.reshape(members, local_x, local_y, depth)
    return (magnetic.astype(F32) + field).astype(BF16)


def solution(mesh):
    in_specs = (
        P(None, "row", "col", None),
        P(None, "row", "col", None),
        P("row", "col", None),
        P(),
    )
    out_specs = P(None, "row", "col", None)
    return jax.shard_map(
        on_device, mesh=mesh, in_specs=in_specs, out_specs=out_specs, check_vma=False
    )
```

```python
import math

import numpy as np
import jax
import jax.numpy as jnp
from jax import lax
from jax.sharding import PartitionSpec as P

TIME_STEP = 0.5
F32 = jnp.float32
BF16 = jnp.bfloat16


def wavenumber(wave_index, length):
    signed = jnp.where(2 * wave_index < length, wave_index, wave_index - length)
    return jnp.where(
        2 * wave_index == length, 0.0, signed.astype(F32) * (2.0 * math.pi / length)
    )


def rounded(values):
    return lax.reduce_precision(values, exponent_bits=8, mantissa_bits=7)


def split_parts(values):
    high = rounded(values)
    low = values - high
    return high.astype(BF16), low.astype(BF16)


def direct_phase(rows, cols, length, step):
    product = (lax.iota(jnp.int32, rows)[:, None] * step) * lax.iota(jnp.int32, cols)[None, :]
    angle = (product % length).astype(F32) * (2.0 * math.pi / length)
    return jnp.cos(angle), jnp.sin(angle)


def phase_table(rows, cols, length):
    block = 32
    if rows % block or rows <= block:
        return direct_phase(rows, cols, length, 1)
    outer_cos, outer_sin = direct_phase(rows // block, cols, length, block)
    inner_cos, inner_sin = direct_phase(block, cols, length, 1)
    outer_cos, outer_sin = outer_cos[:, None], outer_sin[:, None]
    inner_cos, inner_sin = inner_cos[None], inner_sin[None]
    cosine = outer_cos * inner_cos - outer_sin * inner_sin
    sine = outer_sin * inner_cos + outer_cos * inner_sin
    return cosine.reshape(rows, cols), sine.reshape(rows, cols)


def x_kernel(span_x):
    index = np.arange(span_x)
    signed = np.where(2 * index < span_x, index, index - span_x)
    qx = np.where(2 * index == span_x, 0.0, signed * (2.0 * math.pi / span_x))
    shift = np.arange(span_x)
    phases = np.exp(2j * math.pi * np.outer(shift, index) / span_x)
    taps = (phases * (-0.5j * qx)[None, :]).sum(axis=1) / span_x
    taps = taps.real
    matrix = taps[(shift[:, None] - shift[None, :]) % span_x]
    return matrix.astype(np.float32)


def mat(table_parts, operand, spec):
    total = None
    for part in table_parts:
        term = jnp.einsum(spec, part, operand, preferred_element_type=F32)
        total = term if total is None else total + term
    return total


def curl_update(y_real, y_imag, wave_y, wave_z, kernel):
    half = TIME_STEP

    xr, yr, zr = y_real[0], y_real[1], y_real[2]
    xi, yi, zi = y_imag[0], y_imag[1], y_imag[2]
    qy = half * wave_y
    qz = half * wave_z[:, None, None]
    mixed = mat(split_parts(kernel), jnp.stack([yr, yi, zr, zi]).astype(BF16), "ab,qjbk->qjak")
    gyr, gyi, gzr, gzi = mixed[0], mixed[1], mixed[2], mixed[3]
    b_real = jnp.stack([qy * zi - qz * yi, qz * xi - gzr, gyr - qy * xi])
    b_imag = jnp.stack([qz * yr - qy * zr, -qz * xr - gzi, gyi + qy * xr])
    return b_real, b_imag


def on_device(displacement, magnetic, region, permittivity):
    row_count = lax.axis_size("row")
    col_count = lax.axis_size("col")
    devices = row_count * col_count
    members, local_x, local_y, depth = displacement.shape
    width_y = local_y * col_count
    span_x = local_x * row_count
    hermitian = (depth // 2) % devices == 0
    columns = depth // 2 if hermitian else depth
    per_device = columns // devices
    me = lax.axis_index("row") * col_count + lax.axis_index("col")

    reciprocal = 1.0 / permittivity
    regions = permittivity.shape[0]
    first = rounded(reciprocal)
    rest = reciprocal - first
    second = rounded(rest)
    parts = jnp.concatenate([first, second, rest - second]).astype(BF16)
    slots = lax.iota(jnp.int32, 3 * regions) % regions
    one_hot = (region[..., None] == slots).astype(BF16)
    cell_scale = jnp.einsum("...k,k->...", one_hot, parts, preferred_element_type=F32)
    electric = displacement.astype(F32) * cell_scale[None]

    cos_z, sin_z = phase_table(columns, depth, depth)
    if hermitian:
        parity = (1 - 2 * (lax.iota(jnp.int32, depth) % 2)).astype(F32)
        first_row = (lax.iota(jnp.int32, columns) == 0)[:, None]
        sin_part = jnp.where(first_row, parity[None, :], -sin_z)
    else:
        sin_part = -sin_z
    table_z = jnp.stack(
        [cos_z.reshape(devices, per_device, depth), sin_part.reshape(devices, per_device, depth)],
        axis=1,
    ).reshape(2 * columns, depth)
    z_high, z_low = split_parts(table_z)
    rows = members * local_x * local_y

    e_high, e_low = split_parts(electric.reshape(rows, depth))
    spec_z = "dpjz,cyz->dcpjy"
    blocks = (devices, 2, per_device, depth)
    lines = (members * local_x, local_y, depth)
    z_high4, z_low4 = z_high.reshape(blocks), z_low.reshape(blocks)
    e_high, e_low = e_high.reshape(lines), e_low.reshape(lines)
    spectrum = (
        jnp.einsum(spec_z, z_high4, e_high, preferred_element_type=F32)
        + jnp.einsum(spec_z, z_high4, e_low, preferred_element_type=F32)
        + jnp.einsum(spec_z, z_low4, e_high, preferred_element_type=F32)
    )
    spectrum = spectrum.astype(BF16)
    gathered = lax.all_to_all(
        spectrum, ("row", "col"), split_axis=0, concat_axis=0, tiled=True
    )
    gathered = gathered.reshape(
        row_count, col_count, members, local_x, 2, per_device, local_y
    )
    gathered = jnp.transpose(gathered, (2, 4, 5, 0, 3, 1, 6)).reshape(
        members, 2, per_device, span_x, width_y
    )

    cos_y, sin_y = phase_table(width_y, width_y, width_y)
    both_y_parts = split_parts(jnp.concatenate([cos_y, sin_y], axis=1))
    spec_y = "yk,cpjxy->cpjxk"
    by_both = mat(both_y_parts, gathered, spec_y)
    by_cos, by_sin = by_both[..., :width_y], by_both[..., width_y:]
    y_real = by_cos[:, 0] + by_sin[:, 1]
    y_imag = by_cos[:, 1] - by_sin[:, 0]

    kernel = jnp.asarray(x_kernel(span_x))
    wave_y = wavenumber(lax.iota(jnp.int32, width_y), width_y)
    wave_z = wavenumber(me * per_device + lax.iota(jnp.int32, per_device), depth)

    def inverse_y(b_real, b_imag):
        stacked = jnp.stack([b_real, b_imag], axis=1).astype(BF16)
        by_both = mat(both_y_parts, stacked, spec_y)
        by_cos, by_sin = by_both[..., :width_y], by_both[..., width_y:]
        scale = 1.0 / width_y
        out_real = (by_cos[:, 0] - by_sin[:, 1]) * scale
        out_imag = (by_cos[:, 1] + by_sin[:, 0]) * scale
        return rounded(out_real), rounded(out_imag)

    y_real, y_imag = rounded(y_real), rounded(y_imag)
    if hermitian:
        y_real = jnp.concatenate([y_real, rounded(by_cos[:, :, 0])], axis=1)
        y_imag = jnp.concatenate([y_imag, rounded(-by_sin[:, :, 0])], axis=1)
        wave_z = jnp.concatenate([wave_z, jnp.zeros((2,), F32)])
    b_real, b_imag = curl_update(y_real, y_imag, wave_y, wave_z, kernel)
    back_real, back_imag = inverse_y(rounded(b_real), rounded(b_imag))

    if hermitian:
        pback_real = back_real[:, per_device:]
        back_real, back_imag = back_real[:, :per_device], back_imag[:, :per_device]
        is_first = me == 0
        packed = ((lax.iota(jnp.int32, per_device) == 0) & is_first)[None, :, None, None]
        back_real = jnp.where(packed, pback_real[:, 0:1], back_real)
        back_imag = jnp.where(packed, pback_real[:, 1:2], back_imag)

    outgoing = jnp.stack([back_real, back_imag], axis=1).astype(BF16)
    outgoing = outgoing.reshape(
        members, 2, per_device, row_count, local_x, col_count, local_y
    )
    outgoing = jnp.transpose(outgoing, (3, 5, 1, 2, 0, 4, 6)).reshape(
        devices, 2, per_device, members, local_x, local_y
    )
    returned = lax.all_to_all(
        outgoing, ("row", "col"), split_axis=0, concat_axis=0, tiled=True
    )
    returned = returned.reshape(2 * columns, rows)

    weight = np.full((devices, 2, per_device), 1.0 / depth, np.float32)
    if hermitian:
        weight[:] = 2.0 / depth
        weight[0, :, 0] = 1.0 / depth
    weight = jnp.asarray(weight.reshape(2 * columns, 1))
    back_high = (z_high.astype(F32) * weight).astype(BF16)
    back_low = (z_low.astype(F32) * weight).astype(BF16)
    spec_back = "kr,kz->rz"
    field = jnp.einsum(spec_back, returned, back_high, preferred_element_type=F32) + jnp.einsum(
        spec_back, returned, back_low, preferred_element_type=F32
    )
    field = field.reshape(members, local_x, local_y, depth)
    return (magnetic.astype(F32) + field).astype(BF16)


def solution(mesh):
    in_specs = (
        P(None, "row", "col", None),
        P(None, "row", "col", None),
        P("row", "col", None),
        P(),
    )
    out_specs = P(None, "row", "col", None)
    return jax.shard_map(
        on_device, mesh=mesh, in_specs=in_specs, out_specs=out_specs, check_vma=False
    )
```

```python
import math

import numpy as np
import jax
import jax.numpy as jnp
from jax import lax
from jax.sharding import PartitionSpec as P

TIME_STEP = 0.5
F32 = jnp.float32
BF16 = jnp.bfloat16


def wavenumber(wave_index, length):
    signed = jnp.where(2 * wave_index < length, wave_index, wave_index - length)
    return jnp.where(
        2 * wave_index == length, 0.0, signed.astype(F32) * (2.0 * math.pi / length)
    )


def rounded(values):
    return lax.reduce_precision(values, exponent_bits=8, mantissa_bits=7)


def split_parts(values):
    high = rounded(values)
    low = values - high
    return high.astype(BF16), low.astype(BF16)


def direct_phase(rows, cols, length, step):
    product = (lax.iota(jnp.int32, rows)[:, None] * step) * lax.iota(jnp.int32, cols)[None, :]
    angle = (product % length).astype(F32) * (2.0 * math.pi / length)
    return jnp.cos(angle), jnp.sin(angle)


def phase_table(rows, cols, length):
    block = 32
    if rows % block or rows <= block:
        return direct_phase(rows, cols, length, 1)
    outer_cos, outer_sin = direct_phase(rows // block, cols, length, block)
    inner_cos, inner_sin = direct_phase(block, cols, length, 1)
    outer_cos, outer_sin = outer_cos[:, None], outer_sin[:, None]
    inner_cos, inner_sin = inner_cos[None], inner_sin[None]
    cosine = outer_cos * inner_cos - outer_sin * inner_sin
    sine = outer_sin * inner_cos + outer_cos * inner_sin
    return cosine.reshape(rows, cols), sine.reshape(rows, cols)


def x_kernel(span_x):
    index = np.arange(span_x)
    signed = np.where(2 * index < span_x, index, index - span_x)
    qx = np.where(2 * index == span_x, 0.0, signed * (2.0 * math.pi / span_x))
    shift = np.arange(span_x)
    phases = np.exp(2j * math.pi * np.outer(shift, index) / span_x)
    taps = (phases * (-0.5j * qx)[None, :]).sum(axis=1) / span_x
    taps = taps.real
    matrix = taps[(shift[:, None] - shift[None, :]) % span_x]
    return matrix.astype(np.float32)


def mat(table_parts, operand, spec):
    total = None
    for part in table_parts:
        term = jnp.einsum(spec, part, operand, preferred_element_type=F32)
        total = term if total is None else total + term
    return total


def curl_update(y_real, y_imag, wave_y, wave_z, kernel):
    half = TIME_STEP

    xr, yr, zr = y_real[0], y_real[1], y_real[2]
    xi, yi, zi = y_imag[0], y_imag[1], y_imag[2]
    qy = half * wave_y
    qz = half * wave_z[:, None, None]
    mixed = mat(split_parts(kernel), jnp.stack([yr, yi, zr, zi]).astype(BF16), "ab,qjbk->qjak")
    gyr, gyi, gzr, gzi = mixed[0], mixed[1], mixed[2], mixed[3]
    b_real = jnp.stack([qy * zi - qz * yi, qz * xi - gzr, gyr - qy * xi])
    b_imag = jnp.stack([qz * yr - qy * zr, -qz * xr - gzi, gyi + qy * xr])
    return b_real, b_imag


def on_device(displacement, magnetic, region, permittivity):
    row_count = lax.axis_size("row")
    col_count = lax.axis_size("col")
    devices = row_count * col_count
    members, local_x, local_y, depth = displacement.shape
    width_y = local_y * col_count
    span_x = local_x * row_count
    hermitian = (depth // 2) % devices == 0
    columns = depth // 2 if hermitian else depth
    per_device = columns // devices
    me = lax.axis_index("row") * col_count + lax.axis_index("col")

    reciprocal = 1.0 / permittivity
    regions = permittivity.shape[0]
    first = rounded(reciprocal)
    rest = reciprocal - first
    second = rounded(rest)
    parts = jnp.concatenate([first, second, rest - second]).astype(BF16)
    slots = lax.iota(jnp.int32, 3 * regions) % regions
    one_hot = (region[..., None] == slots).astype(BF16)
    cell_scale = jnp.einsum("...k,k->...", one_hot, parts, preferred_element_type=F32)
    electric = displacement.astype(F32) * cell_scale[None]

    cos_z, sin_z = phase_table(columns, depth, depth)
    if hermitian:
        parity = (1 - 2 * (lax.iota(jnp.int32, depth) % 2)).astype(F32)
        first_row = (lax.iota(jnp.int32, columns) == 0)[:, None]
        sin_part = jnp.where(first_row, parity[None, :], -sin_z)
    else:
        sin_part = -sin_z
    table_z = jnp.stack(
        [cos_z.reshape(devices, per_device, depth), sin_part.reshape(devices, per_device, depth)],
        axis=1,
    ).reshape(2 * columns, depth)
    z_high, z_low = split_parts(table_z)
    rows = members * local_x * local_y

    e_high, e_low = split_parts(electric.reshape(rows, depth))
    spec_z = "dpjz,cyz->dcpjy"
    blocks = (devices, 2, per_device, depth)
    lines = (members * local_x, local_y, depth)
    z_high4, z_low4 = z_high.reshape(blocks), z_low.reshape(blocks)
    e_high, e_low = e_high.reshape(lines), e_low.reshape(lines)
    spectrum = (
        jnp.einsum(spec_z, z_high4, e_high, preferred_element_type=F32)
        + jnp.einsum(spec_z, z_high4, e_low, preferred_element_type=F32)
        + jnp.einsum(spec_z, z_low4, e_high, preferred_element_type=F32)
    )
    spectrum = spectrum.astype(BF16)
    gathered = lax.all_to_all(
        spectrum, ("row", "col"), split_axis=0, concat_axis=0, tiled=True
    )
    gathered = gathered.reshape(
        row_count, col_count, members, local_x, 2, per_device, local_y
    )
    gathered = jnp.transpose(gathered, (2, 4, 5, 0, 3, 1, 6)).reshape(
        members, 2, per_device, span_x, width_y
    )

    cos_y, sin_y = phase_table(width_y, width_y, width_y)
    both_y_parts = (jnp.concatenate(split_parts(jnp.concatenate([cos_y, sin_y], axis=1)), axis=1),)
    spec_y = "yk,cpjxy->cpjxk"
    by_all = mat(both_y_parts, gathered, spec_y)
    by_both = by_all[..., : 2 * width_y] + by_all[..., 2 * width_y :]
    by_cos, by_sin = by_both[..., :width_y], by_both[..., width_y:]
    y_real = by_cos[:, 0] + by_sin[:, 1]
    y_imag = by_cos[:, 1] - by_sin[:, 0]

    kernel = jnp.asarray(x_kernel(span_x))
    wave_y = wavenumber(lax.iota(jnp.int32, width_y), width_y)
    wave_z = wavenumber(me * per_device + lax.iota(jnp.int32, per_device), depth)

    def inverse_y(b_real, b_imag):
        stacked = jnp.stack([b_real, b_imag], axis=1).astype(BF16)
        by_all = mat(both_y_parts, stacked, spec_y)
        by_both = by_all[..., : 2 * width_y] + by_all[..., 2 * width_y :]
        by_cos, by_sin = by_both[..., :width_y], by_both[..., width_y:]
        scale = 1.0 / width_y
        out_real = (by_cos[:, 0] - by_sin[:, 1]) * scale
        out_imag = (by_cos[:, 1] + by_sin[:, 0]) * scale
        return rounded(out_real), rounded(out_imag)

    y_real, y_imag = rounded(y_real), rounded(y_imag)
    if hermitian:
        y_real = jnp.concatenate([y_real, rounded(by_cos[:, :, 0])], axis=1)
        y_imag = jnp.concatenate([y_imag, rounded(-by_sin[:, :, 0])], axis=1)
        wave_z = jnp.concatenate([wave_z, jnp.zeros((2,), F32)])
    b_real, b_imag = curl_update(y_real, y_imag, wave_y, wave_z, kernel)
    back_real, back_imag = inverse_y(rounded(b_real), rounded(b_imag))

    if hermitian:
        pback_real = back_real[:, per_device:]
        back_real, back_imag = back_real[:, :per_device], back_imag[:, :per_device]
        is_first = me == 0
        packed = ((lax.iota(jnp.int32, per_device) == 0) & is_first)[None, :, None, None]
        back_real = jnp.where(packed, pback_real[:, 0:1], back_real)
        back_imag = jnp.where(packed, pback_real[:, 1:2], back_imag)

    outgoing = jnp.stack([back_real, back_imag], axis=1).astype(BF16)
    outgoing = outgoing.reshape(
        members, 2, per_device, row_count, local_x, col_count, local_y
    )
    outgoing = jnp.transpose(outgoing, (3, 5, 1, 2, 0, 4, 6)).reshape(
        devices, 2, per_device, members, local_x, local_y
    )
    returned = lax.all_to_all(
        outgoing, ("row", "col"), split_axis=0, concat_axis=0, tiled=True
    )
    returned = returned.reshape(2 * columns, rows)

    weight = np.full((devices, 2, per_device), 1.0 / depth, np.float32)
    if hermitian:
        weight[:] = 2.0 / depth
        weight[0, :, 0] = 1.0 / depth
    weight = jnp.asarray(weight.reshape(2 * columns, 1))
    back_high = (z_high.astype(F32) * weight).astype(BF16)
    back_low = (z_low.astype(F32) * weight).astype(BF16)
    spec_back = "kr,kz->rz"
    field = jnp.einsum(spec_back, returned, back_high, preferred_element_type=F32) + jnp.einsum(
        spec_back, returned, back_low, preferred_element_type=F32
    )
    field = field.reshape(members, local_x, local_y, depth)
    return (magnetic.astype(F32) + field).astype(BF16)


def solution(mesh):
    in_specs = (
        P(None, "row", "col", None),
        P(None, "row", "col", None),
        P("row", "col", None),
        P(),
    )
    out_specs = P(None, "row", "col", None)
    return jax.shard_map(
        on_device, mesh=mesh, in_specs=in_specs, out_specs=out_specs, check_vma=False
    )
```

```python
import math

import numpy as np
import jax
import jax.numpy as jnp
from jax import lax
from jax.sharding import PartitionSpec as P

TIME_STEP = 0.5
F32 = jnp.float32
BF16 = jnp.bfloat16


def wavenumber(wave_index, length):
    signed = jnp.where(2 * wave_index < length, wave_index, wave_index - length)
    return jnp.where(
        2 * wave_index == length, 0.0, signed.astype(F32) * (2.0 * math.pi / length)
    )


def rounded(values):
    return lax.reduce_precision(values, exponent_bits=8, mantissa_bits=7)


def split_parts(values):
    high = rounded(values)
    low = values - high
    return high.astype(BF16), low.astype(BF16)


def direct_phase(rows, cols, length, step):
    product = (lax.iota(jnp.int32, rows)[:, None] * step) * lax.iota(jnp.int32, cols)[None, :]
    angle = (product % length).astype(F32) * (2.0 * math.pi / length)
    return jnp.cos(angle), jnp.sin(angle)


def phase_table(rows, cols, length):
    block = 32
    if rows % block or rows <= block:
        return direct_phase(rows, cols, length, 1)
    outer_cos, outer_sin = direct_phase(rows // block, cols, length, block)
    inner_cos, inner_sin = direct_phase(block, cols, length, 1)
    outer_cos, outer_sin = outer_cos[:, None], outer_sin[:, None]
    inner_cos, inner_sin = inner_cos[None], inner_sin[None]
    cosine = outer_cos * inner_cos - outer_sin * inner_sin
    sine = outer_sin * inner_cos + outer_cos * inner_sin
    return cosine.reshape(rows, cols), sine.reshape(rows, cols)


def x_kernel(span_x):
    index = np.arange(span_x)
    signed = np.where(2 * index < span_x, index, index - span_x)
    qx = np.where(2 * index == span_x, 0.0, signed * (2.0 * math.pi / span_x))
    shift = np.arange(span_x)
    phases = np.exp(2j * math.pi * np.outer(shift, index) / span_x)
    taps = (phases * (-0.5j * qx)[None, :]).sum(axis=1) / span_x
    taps = taps.real
    matrix = taps[(shift[:, None] - shift[None, :]) % span_x]
    return matrix.astype(np.float32)


def mat(table_parts, operand, spec):
    total = None
    for part in table_parts:
        term = jnp.einsum(spec, part, operand, preferred_element_type=F32)
        total = term if total is None else total + term
    return total


def curl_update(y_real, y_imag, wave_y, wave_z, kernel):
    half = TIME_STEP

    xr, yr, zr = y_real[0], y_real[1], y_real[2]
    xi, yi, zi = y_imag[0], y_imag[1], y_imag[2]
    qy = half * wave_y
    qz = half * wave_z[:, None, None]
    mixed = mat(split_parts(kernel), jnp.stack([yr, yi, zr, zi]).astype(BF16), "ab,qjbk->qjak")
    gyr, gyi, gzr, gzi = mixed[0], mixed[1], mixed[2], mixed[3]
    b_real = jnp.stack([qy * zi - qz * yi, qz * xi - gzr, gyr - qy * xi])
    b_imag = jnp.stack([qz * yr - qy * zr, -qz * xr - gzi, gyi + qy * xr])
    return b_real, b_imag


def on_device(displacement, magnetic, region, permittivity):
    row_count = lax.axis_size("row")
    col_count = lax.axis_size("col")
    devices = row_count * col_count
    members, local_x, local_y, depth = displacement.shape
    width_y = local_y * col_count
    span_x = local_x * row_count
    hermitian = (depth // 2) % devices == 0
    columns = depth // 2 if hermitian else depth
    per_device = columns // devices
    me = lax.axis_index("row") * col_count + lax.axis_index("col")

    reciprocal = 1.0 / permittivity
    regions = permittivity.shape[0]
    first = rounded(reciprocal)
    rest = reciprocal - first
    second = rounded(rest)
    parts = jnp.concatenate([first, second, rest - second]).astype(BF16)
    slots = lax.iota(jnp.int32, 3 * regions) % regions
    one_hot = (region[..., None] == slots).astype(BF16)
    cell_scale = jnp.einsum("...k,k->...", one_hot, parts, preferred_element_type=F32)
    electric = displacement.astype(F32) * cell_scale[None]

    cos_z, sin_z = phase_table(columns, depth, depth)
    if hermitian:
        parity = (1 - 2 * (lax.iota(jnp.int32, depth) % 2)).astype(F32)
        first_row = (lax.iota(jnp.int32, columns) == 0)[:, None]
        sin_part = jnp.where(first_row, parity[None, :], -sin_z)
    else:
        sin_part = -sin_z
    table_z = jnp.stack(
        [cos_z.reshape(devices, per_device, depth), sin_part.reshape(devices, per_device, depth)],
        axis=1,
    ).reshape(2 * columns, depth)
    z_high, z_low = split_parts(table_z)
    rows = members * local_x * local_y

    e_high, e_low = split_parts(electric.reshape(rows, depth))
    spec_z = "dpjz,cyz->dcpjy"
    blocks = (devices, 2, per_device, depth)
    lines = (members * local_x, local_y, depth)
    z_high4, z_low4 = z_high.reshape(blocks), z_low.reshape(blocks)
    e_high, e_low = e_high.reshape(lines), e_low.reshape(lines)
    by_high = jnp.einsum(
        spec_z, z_high4, jnp.concatenate([e_high, e_low]), preferred_element_type=F32
    )
    spectrum = (
        by_high[:, : lines[0]]
        + by_high[:, lines[0] :]
        + jnp.einsum(spec_z, z_low4, e_high, preferred_element_type=F32)
    )
    spectrum = spectrum.astype(BF16)
    gathered = lax.all_to_all(
        spectrum, ("row", "col"), split_axis=0, concat_axis=0, tiled=True
    )
    gathered = gathered.reshape(
        row_count, col_count, members, local_x, 2, per_device, local_y
    )
    gathered = jnp.transpose(gathered, (2, 4, 5, 0, 3, 1, 6)).reshape(
        members, 2, per_device, span_x, width_y
    )

    cos_y, sin_y = phase_table(width_y, width_y, width_y)
    both_y_parts = split_parts(jnp.concatenate([cos_y, sin_y], axis=1))
    spec_y = "yk,cpjxy->cpjxk"
    by_both = mat(both_y_parts, gathered, spec_y)
    by_cos, by_sin = by_both[..., :width_y], by_both[..., width_y:]
    y_real = by_cos[:, 0] + by_sin[:, 1]
    y_imag = by_cos[:, 1] - by_sin[:, 0]

    kernel = jnp.asarray(x_kernel(span_x))
    wave_y = wavenumber(lax.iota(jnp.int32, width_y), width_y)
    wave_z = wavenumber(me * per_device + lax.iota(jnp.int32, per_device), depth)

    def inverse_y(b_real, b_imag):
        stacked = jnp.stack([b_real, b_imag], axis=1).astype(BF16)
        by_both = mat(both_y_parts, stacked, spec_y)
        by_cos, by_sin = by_both[..., :width_y], by_both[..., width_y:]
        scale = 1.0 / width_y
        out_real = (by_cos[:, 0] - by_sin[:, 1]) * scale
        out_imag = (by_cos[:, 1] + by_sin[:, 0]) * scale
        return rounded(out_real), rounded(out_imag)

    y_real, y_imag = rounded(y_real), rounded(y_imag)
    if hermitian:
        y_real = jnp.concatenate([y_real, rounded(by_cos[:, :, 0])], axis=1)
        y_imag = jnp.concatenate([y_imag, rounded(-by_sin[:, :, 0])], axis=1)
        wave_z = jnp.concatenate([wave_z, jnp.zeros((2,), F32)])
    b_real, b_imag = curl_update(y_real, y_imag, wave_y, wave_z, kernel)
    back_real, back_imag = inverse_y(rounded(b_real), rounded(b_imag))

    if hermitian:
        pback_real = back_real[:, per_device:]
        back_real, back_imag = back_real[:, :per_device], back_imag[:, :per_device]
        is_first = me == 0
        packed = ((lax.iota(jnp.int32, per_device) == 0) & is_first)[None, :, None, None]
        back_real = jnp.where(packed, pback_real[:, 0:1], back_real)
        back_imag = jnp.where(packed, pback_real[:, 1:2], back_imag)

    outgoing = jnp.stack([back_real, back_imag], axis=1).astype(BF16)
    outgoing = outgoing.reshape(
        members, 2, per_device, row_count, local_x, col_count, local_y
    )
    outgoing = jnp.transpose(outgoing, (3, 5, 1, 2, 0, 4, 6)).reshape(
        devices, 2, per_device, members, local_x, local_y
    )
    returned = lax.all_to_all(
        outgoing, ("row", "col"), split_axis=0, concat_axis=0, tiled=True
    )
    returned = returned.reshape(2 * columns, rows)

    weight = np.full((devices, 2, per_device), 1.0 / depth, np.float32)
    if hermitian:
        weight[:] = 2.0 / depth
        weight[0, :, 0] = 1.0 / depth
    weight = jnp.asarray(weight.reshape(2 * columns, 1))
    back_high = (z_high.astype(F32) * weight).astype(BF16)
    back_low = (z_low.astype(F32) * weight).astype(BF16)
    spec_back = "kr,kz->rz"
    field = jnp.einsum(spec_back, returned, back_high, preferred_element_type=F32) + jnp.einsum(
        spec_back, returned, back_low, preferred_element_type=F32
    )
    field = field.reshape(members, local_x, local_y, depth)
    return (magnetic.astype(F32) + field).astype(BF16)


def solution(mesh):
    in_specs = (
        P(None, "row", "col", None),
        P(None, "row", "col", None),
        P("row", "col", None),
        P(),
    )
    out_specs = P(None, "row", "col", None)
    return jax.shard_map(
        on_device, mesh=mesh, in_specs=in_specs, out_specs=out_specs, check_vma=False
    )
```
